32 devices in a mesh: seq: 16 (over z, x, core), tp: 2 (over y).
Axes of the slice: x: 2, y: 2, z: 4, core: 2. Of those that a mesh axis runs over, the one named last changes fastest.
Arguments:
- tokens: bfloat16 [8192, 5376], P(('seq', 'tp')), may hold values from -6 to 6
- norm_gain: float32 [5376], replicated, may hold values from 0.5 to 1.5
- w_query: bfloat16 [5376, 2048], P(None, 'tp'), may hold values from -0.078125 to 0.078125
- key_value_weight: bfloat16 [5376, 2048], P(None, 'tp'), may hold values from -0.078125 to 0.078125
- query_gain: float32 [128], replicated, may hold values from 0.5 to 7
- key_gain: float32 [128], replicated, may hold values from 0.5 to 7
- lengths: int32 [8], replicated, may hold values from 1 to 4096, as said below
- segment_ids: int32 [8192], P('seq'), may hold values from 0 to 7, as said below
- req_counts: int32 [8], replicated, may hold values from 8 to 16, as said below
- req_slots: int32 [128], replicated, may hold values from 0 to 131071, as said below
Outputs:
- attended: bfloat16 [8192, 2048], P('seq', 'tp')
- cache: bfloat16 [131072, 2048], P('seq', 'tp')
The draws below stay inside these ranges and needn't reach their ends.
Inputs may be any that keep to these rules, and one draw needn't show every extreme that they name: lengths sum to 8192; the longest is exactly 4096. Prompts lie in order: prompt p covers lengths[p] consecutive tokens, so segment_ids never falls. `req_counts`: the requests of prompt p follow those of prompts before it; entries past all requests are unused. `req_slots`: the cache rows of different requests never intersect and lie within the cache; unused entries are 0.
All inputs are finite; a program needn't handle non-finite values.
Results may differ from the reference program's by a relative error of at most 0.005.
The reference program's roundings to bfloat16 on the way (of `normed` and `weights`) count: a program that leaves them out, or rounds other values in their place, can miss the bound.
Values may be sent and summed in bfloat16 or wider, within the bound.
No kernel may reach another device: no remote copies, remote signals or barrier semaphores. Data moves between devices by JAX's collectives and lax.ppermute only.
A program may use at most 192 MiB of HBM per device.

```python
import math
import jax
import jax.numpy as jnp
from jax import lax

MODEL_WIDTH = 5376
HQ = 16
KEY_VALUE_HEADS = 8
HEAD_SIZE = 128
NPROMPT = 8
REQ_MOST = 16
PACKED_TOKENS = 8192
MAXLEN = 4096
CACHE_ROWS = 131072
MAXREQ = 128


fewest_requests = 8


def plan_draw(key):
    base_key = jax.random.fold_in(key, 4242)
    key_len, key_place, key_count, key_order, key_offset = jax.random.split(base_key, 5)
    remaining = PACKED_TOKENS - MAXLEN
    others = NPROMPT - 1
    shares = jax.random.randint(key_len, (others,), 1, 101)
    pieces_len = 1 + (remaining - others) * shares // jnp.sum(shares)
    pieces_len = pieces_len.at[0].add(remaining - jnp.sum(pieces_len))
    ordered = jnp.concatenate([jnp.full((1,), MAXLEN, jnp.int32), pieces_len.astype(jnp.int32)])
    placing = jax.random.permutation(key_place, NPROMPT)
    lengths = ordered[placing].astype(jnp.int32)
    counts = jax.random.randint(key_count, (NPROMPT,), fewest_requests, REQ_MOST + 1).astype(jnp.int32)
    request_ids = jnp.arange(MAXREQ, dtype=jnp.int32)
    request_ends = jnp.cumsum(counts).astype(jnp.int32)
    owner_prompt = jnp.sum((request_ends[None, :] <= request_ids[:, None]).astype(jnp.int32), axis=1)
    request_length = jnp.where(owner_prompt < NPROMPT, lengths[jnp.clip(owner_prompt, 0, NPROMPT - 1)], 0).astype(jnp.int32)
    written = jnp.sum(request_length)
    shuffle = jax.random.permutation(key_order, MAXREQ)
    placed = request_length[shuffle]
    earlier_rows = (jnp.cumsum(placed) - placed).astype(jnp.int32)
    offset = jax.random.randint(key_offset, (), 0, CACHE_ROWS - written + 1)
    slots = jnp.zeros((MAXREQ,), jnp.int32).at[shuffle].set(earlier_rows + offset)
    slots = jnp.where(request_length > 0, slots, 0).astype(jnp.int32)
    prompt_ends = jnp.cumsum(lengths).astype(jnp.int32)
    token_index = jnp.arange(PACKED_TOKENS, dtype=jnp.int32)
    segments = jnp.sum((token_index[:, None] >= prompt_ends[None, :]).astype(jnp.int32), axis=1).astype(jnp.int32)
    return (lengths, segments, counts, slots)


def draw_lengths(key, part):
    return plan_draw(key)[0]


def draw_segment_ids(key, part):
    return plan_draw(key)[1]


def draw_req_counts(key, part):
    return plan_draw(key)[2]


def draw_req_slots(key, part):
    return plan_draw(key)[3]


def gain_draw(key, salt):
    noise_key = jax.random.fold_in(key, salt)
    return jnp.clip(1.0 + 0.35 * jax.random.normal(noise_key, (HEAD_SIZE,), jnp.float32), 0.5, 1.8)


def draw_query_gain(key, part):
    return gain_draw(key, 11)


def draw_key_gain(key, part):
    return gain_draw(key, 12)


def block_levels(rng, shape, shards, smallest, largest):
    factor_of = 1.0
    for dim, parts in shards:
        heights = jax.random.uniform(jax.random.fold_in(jax.random.fold_in(rng, 6), dim), (parts,), jnp.float32, smallest / len(shards), largest / len(shards))
        factor_of = factor_of * jnp.repeat(jnp.exp(heights), shape[dim] // parts).reshape((-1,) + (1,) * (len(shape) - 1 - dim))
    return factor_of


def centred(rng, extent, deviation, bound, cuts=(), kind=jnp.bfloat16):
    result = jax.random.normal(rng, extent, jnp.float32) * deviation
    if len(cuts) > 0:
        result = block_levels(rng, extent, cuts, -0.22, 0.18) * result
    return jnp.clip(result, min=-bound, max=bound).astype(kind)


def setup_inputs(seed: int = 0) -> dict:
    arg_keys = jax.random.split(jax.random.key(seed), 11)
    return {
        "tokens": centred(arg_keys[0], (PACKED_TOKENS, MODEL_WIDTH), 1.0, 6.0, ((0, 32),)),
        "norm_gain": jnp.clip(1.0 + 0.1 * jax.random.normal(arg_keys[1], (MODEL_WIDTH,), jnp.float32), 0.5, 1.5),
        "w_query": centred(arg_keys[2], (MODEL_WIDTH, HQ * HEAD_SIZE), MODEL_WIDTH ** -0.5, 0.078125, ((1, 2),)),
        "key_value_weight": centred(arg_keys[3], (MODEL_WIDTH, KEY_VALUE_HEADS * 2 * HEAD_SIZE), MODEL_WIDTH ** -0.5, 0.078125, ((1, 2),)),
        "query_gain": draw_query_gain(jax.random.fold_in(arg_keys[10], 71), 0),
        "key_gain": draw_key_gain(jax.random.fold_in(arg_keys[10], 71), 0),
        "lengths": draw_lengths(jax.random.fold_in(arg_keys[10], 71), 0),
        "segment_ids": draw_segment_ids(jax.random.fold_in(arg_keys[10], 71), 0),
        "req_counts": draw_req_counts(jax.random.fold_in(arg_keys[10], 71), 0),
        "req_slots": draw_req_slots(jax.random.fold_in(arg_keys[10], 71), 0),
    }


rope_base = 1000000.0
query_scalar = 168.0
epsilon = 1e-06

def rms_scale(values, gains):
    return values * lax.rsqrt(lax.optimization_barrier(jnp.mean(values * values, axis=-1, keepdims=True)) + epsilon) * gains

def rope_table(positions, head_width):
    half_width = head_width // 2
    frequency = jnp.exp(jnp.arange(half_width, dtype=jnp.float32) * (-2.0 * math.log(rope_base) / head_width))
    angles = positions.astype(jnp.float32)[:, None] * frequency[None, :]
    return (jnp.cos(angles), jnp.sin(angles))

def rotate_pairs(values, cosine, sine_table):
    half_width = values.shape[-1] // 2
    front_half = values[..., :half_width]
    back_half = values[..., half_width:]
    cos_part = cosine[:, None, :]
    sin_part = sine_table[:, None, :]
    return jnp.concatenate([front_half * cos_part - back_half * sin_part, back_half * cos_part + front_half * sin_part], axis=-1)

def project(tokens, norm_gain, w_query, key_value_weight, query_gain, key_gain, positions):
    token_count = tokens.shape[0]
    head_width = query_gain.shape[0]
    as_float = tokens.astype(jnp.float32)
    normed = rms_scale(as_float, norm_gain).astype(jnp.bfloat16)
    query_raw = jnp.dot(normed, w_query, preferred_element_type=jnp.float32)
    keyval_raw = jnp.dot(normed, key_value_weight, preferred_element_type=jnp.float32)
    cosine, sine_table = rope_table(positions, head_width)
    query_rows = rotate_pairs(rms_scale(query_raw.reshape(token_count, -1, head_width), query_gain), cosine, sine_table) * query_scalar ** (-0.5)
    split_kv = keyval_raw.reshape(token_count, -1, 2, head_width)
    keys = rotate_pairs(rms_scale(split_kv[:, :, 0], key_gain), cosine, sine_table)
    key_value_rows = jnp.stack([keys, split_kv[:, :, 1]], axis=2).reshape(token_count, -1).astype(jnp.bfloat16)
    return (query_rows.reshape(token_count, -1).astype(jnp.bfloat16), key_value_rows)

def prompt_starts(segment_ids, lengths):
    starts = (jnp.cumsum(lengths) - lengths).astype(jnp.int32)
    prompt_ids = jnp.arange(lengths.shape[0], dtype=jnp.int32)
    chosen = jnp.where(segment_ids[:, None] == prompt_ids[None, :], starts[None, :], jnp.int32(0))
    return lax.optimization_barrier(jnp.sum(chosen, axis=1)).astype(jnp.int32)

def sources(cache_index, lengths, req_counts, req_slots):
    starts = (jnp.cumsum(lengths) - lengths).astype(jnp.int32)
    prompt_ids = jnp.arange(lengths.shape[0], dtype=jnp.int32)
    request_ids = jnp.arange(req_slots.shape[0], dtype=jnp.int32)
    request_ends = jnp.cumsum(req_counts).astype(jnp.int32)
    owner_prompt = lax.optimization_barrier(jnp.sum((request_ends[None, :] <= request_ids[:, None]).astype(jnp.int32), axis=1)).astype(jnp.int32)
    matches = owner_prompt[:, None] == prompt_ids[None, :]
    request_length = lax.optimization_barrier(jnp.sum(jnp.where(matches, lengths[None, :], jnp.int32(0)), axis=1)).astype(jnp.int32)
    request_start = lax.optimization_barrier(jnp.sum(jnp.where(matches, starts[None, :], jnp.int32(0)), axis=1)).astype(jnp.int32)
    inside = (cache_index[:, None] >= req_slots[None, :]) & (cache_index[:, None] < req_slots[None, :] + request_length[None, :])
    offsets = request_start[None, :] + cache_index[:, None] - req_slots[None, :]
    source_row = lax.optimization_barrier(jnp.sum(jnp.where(inside, offsets, jnp.int32(0)), axis=1)).astype(jnp.int32)
    source_live = lax.optimization_barrier(jnp.max(inside.astype(jnp.int32), axis=1)) > 0
    return (source_row, source_live)

def reference(tokens, norm_gain, w_query, key_value_weight, query_gain, key_gain, lengths, segment_ids, req_counts, req_slots):
    token_index = jnp.arange(PACKED_TOKENS, dtype=jnp.int32)
    positions = token_index - prompt_starts(segment_ids, lengths)
    query_rows, key_value_rows = project(tokens, norm_gain, w_query, key_value_weight, query_gain, key_gain, positions)
    grouped_query_rows = query_rows.reshape(PACKED_TOKENS, KEY_VALUE_HEADS, 2, HEAD_SIZE)
    grouped_heads = key_value_rows.reshape(PACKED_TOKENS, KEY_VALUE_HEADS, 2, HEAD_SIZE)
    key_part = grouped_heads[:, :, 0].astype(jnp.float32)
    value_part = grouped_heads[:, :, 1].astype(jnp.float32)
    block_span = math.gcd(PACKED_TOKENS, 256)

    def one_block(block_number):
        offset = block_number * block_span
        block_query = lax.dynamic_slice_in_dim(grouped_query_rows, offset, block_span, 0).astype(jnp.float32)
        block_seg = lax.dynamic_slice_in_dim(segment_ids, offset, block_span, 0)
        block_index = offset + jnp.arange(block_span, dtype=jnp.int32)
        allowed = (segment_ids[None, :] == block_seg[:, None]) & (token_index[None, :] <= block_index[:, None])
        scores = jnp.einsum('qgrd,kgd->grqk', block_query, key_part)
        row_peak = lax.optimization_barrier(jnp.max(jnp.where(allowed, scores, -jnp.inf), axis=-1, keepdims=True))
        exp_scores = jnp.where(allowed, jnp.exp(scores - row_peak), 0.0)
        totals = lax.optimization_barrier(jnp.sum(exp_scores, axis=-1))
        weights = exp_scores.astype(jnp.bfloat16).astype(jnp.float32)
        weighted = jnp.einsum('grqk,kgd->qgrd', weights, value_part)
        return (weighted / jnp.transpose(totals, (2, 0, 1))[..., None]).reshape(block_span, -1).astype(jnp.bfloat16)
    attended = lax.map(one_block, jnp.arange(PACKED_TOKENS // block_span, dtype=jnp.int32)).reshape(PACKED_TOKENS, -1)
    cache_index = jnp.arange(CACHE_ROWS, dtype=jnp.int32)
    source_row, source_live = sources(cache_index, lengths, req_counts, req_slots)
    picked = jnp.take(key_value_rows, source_row, axis=0)
    cache = jnp.where(source_live[:, None], picked, jnp.zeros_like(picked))
    return (attended, cache)
```

```python
import math

import jax
import jax.numpy as jnp
from jax import lax
from jax.sharding import PartitionSpec as P

CACHE_DEV = 8192


rope_base = 1000000.0
query_scalar = 168.0
epsilon = 1e-06


def rms_scale(values, gains):
    return values * lax.rsqrt(jnp.mean(values * values, axis=-1, keepdims=True) + epsilon) * gains


def rope_table(positions, head_width):
    half_width = head_width // 2
    frequency = jnp.exp(
        jnp.arange(half_width, dtype=jnp.float32) * (-2.0 * math.log(rope_base) / head_width)
    )
    angles = positions.astype(jnp.float32)[:, None] * frequency[None, :]
    return (jnp.cos(angles), jnp.sin(angles))


def rotate_pairs(values, cosine, sine_table):
    half_width = values.shape[-1] // 2
    front_half = values[..., :half_width]
    back_half = values[..., half_width:]
    cos_part = cosine[:, None, :]
    sin_part = sine_table[:, None, :]
    return jnp.concatenate(
        [
            front_half * cos_part - back_half * sin_part,
            back_half * cos_part + front_half * sin_part,
        ],
        axis=-1,
    )


def project(tokens, norm_gain, w_query, key_value_weight, query_gain, key_gain, positions):
    token_count = tokens.shape[0]
    head_width = query_gain.shape[0]
    as_float = tokens.astype(jnp.float32)
    normed = rms_scale(as_float, norm_gain).astype(jnp.bfloat16)
    query_raw = jnp.dot(normed, w_query, preferred_element_type=jnp.float32)
    keyval_raw = jnp.dot(normed, key_value_weight, preferred_element_type=jnp.float32)
    cosine, sine_table = rope_table(positions, head_width)
    query_rows = rotate_pairs(
        rms_scale(query_raw.reshape(token_count, -1, head_width), query_gain), cosine, sine_table
    ) * query_scalar ** (-0.5)
    split_kv = keyval_raw.reshape(token_count, -1, 2, head_width)
    keys = rotate_pairs(rms_scale(split_kv[:, :, 0], key_gain), cosine, sine_table)
    key_value_rows = (
        jnp.stack([keys, split_kv[:, :, 1]], axis=2).reshape(token_count, -1).astype(jnp.bfloat16)
    )
    return (query_rows.reshape(token_count, -1).astype(jnp.bfloat16), key_value_rows)


def prompt_starts(segment_ids, lengths):
    starts = jnp.cumsum(lengths) - lengths
    prompt_ids = jnp.arange(lengths.shape[0], dtype=jnp.int32)
    chosen = jnp.where(segment_ids[:, None] == prompt_ids[None, :], starts[None, :], jnp.int32(0))
    return jnp.sum(chosen, axis=1)


def sources(cache_index, lengths, req_counts, req_slots):
    starts = jnp.cumsum(lengths) - lengths
    prompt_ids = jnp.arange(lengths.shape[0], dtype=jnp.int32)
    request_ids = jnp.arange(req_slots.shape[0], dtype=jnp.int32)
    request_ends = jnp.cumsum(req_counts)
    owner_prompt = jnp.sum(
        (request_ends[None, :] <= request_ids[:, None]).astype(jnp.int32), axis=1
    )
    matches = owner_prompt[:, None] == prompt_ids[None, :]
    request_length = jnp.sum(jnp.where(matches, lengths[None, :], jnp.int32(0)), axis=1)
    request_start = jnp.sum(jnp.where(matches, starts[None, :], jnp.int32(0)), axis=1)
    inside = (cache_index[:, None] >= req_slots[None, :]) & (
        cache_index[:, None] < req_slots[None, :] + request_length[None, :]
    )
    offsets = request_start[None, :] + cache_index[:, None] - req_slots[None, :]
    source_row = jnp.sum(jnp.where(inside, offsets, jnp.int32(0)), axis=1)
    source_live = jnp.max(inside.astype(jnp.int32), axis=1) > 0
    return (source_row, source_live)


def gather_tp(tokens):
    tp_size = lax.axis_size("tp")
    tp_rank = lax.axis_index("tp")
    rows = tokens.shape[0]
    gathered = jnp.zeros((tp_size * rows,) + tokens.shape[1:], tokens.dtype)
    gathered = lax.dynamic_update_slice_in_dim(gathered, tokens, tp_rank * rows, 0)
    for shift in range(1, tp_size):
        pairs = [(i, (i + shift) % tp_size) for i in range(tp_size)]
        got = lax.ppermute(tokens, "tp", pairs)
        source = (tp_rank - shift) % tp_size
        gathered = lax.dynamic_update_slice_in_dim(gathered, got, source * rows, 0)
    return gathered


def on_device(
    tokens,
    norm_gain,
    w_query,
    key_value_weight,
    query_gain,
    key_gain,
    lengths,
    segment_ids,
    req_counts,
    req_slots,
):
    gathered = gather_tp(tokens)
    row_count = gathered.shape[0]
    seq_rank = lax.axis_index("seq")
    first_row = seq_rank * row_count
    query_index = first_row + jnp.arange(row_count, dtype=jnp.int32)
    segment_start = prompt_starts(segment_ids, lengths)
    positions = query_index - segment_start
    query_rows, key_value_rows = project(
        gathered, norm_gain, w_query, key_value_weight, query_gain, key_gain, positions
    )
    head_width = query_gain.shape[0]
    kv_heads = key_value_rows.shape[1] // (2 * head_width)
    query_heads = query_rows.reshape(row_count, kv_heads, 2, head_width)
    cache_rows = CACHE_DEV
    cache_index = seq_rank * cache_rows + jnp.arange(cache_rows, dtype=jnp.int32)
    source_row, source_live = sources(cache_index, lengths, req_counts, req_slots)

    def attend_block(state_now, key_block, block_start):
        maxima, totals, running = state_now
        key_count = key_block.shape[0]
        grouped_heads = key_block.reshape(key_count, kv_heads, 2, head_width)
        key_part = grouped_heads[:, :, 0]
        value_part = grouped_heads[:, :, 1]
        key_index = block_start + jnp.arange(key_count, dtype=jnp.int32)
        allowed = (key_index[None, :] >= segment_start[:, None]) & (
            key_index[None, :] <= query_index[:, None]
        )
        scores = jnp.einsum(
            "qgrd,kgd->grqk", query_heads, key_part, preferred_element_type=jnp.float32
        )
        new_maxima = jnp.maximum(maxima, jnp.max(jnp.where(allowed, scores, -1e30), axis=-1))
        factor = jnp.exp(maxima - new_maxima)
        exp_scores = jnp.where(allowed, jnp.exp(scores - new_maxima[..., None]), 0.0)
        totals = totals * factor + jnp.sum(exp_scores, axis=-1)
        weighted = jnp.einsum(
            "grqk,kgd->qgrd",
            exp_scores.astype(jnp.bfloat16),
            value_part,
            preferred_element_type=jnp.float32,
        )
        running = running * jnp.transpose(factor, (2, 0, 1))[..., None] + weighted
        return (new_maxima, totals, running)

    initial = (
        jnp.full((kv_heads, 2, row_count), -1e30, jnp.float32),
        jnp.zeros((kv_heads, 2, row_count), jnp.float32),
        jnp.zeros((row_count, kv_heads, 2, head_width), jnp.float32),
    )
    block_span = row_count
    state = attend_block(initial, key_value_rows, first_row)
    key_block = lax.all_gather(key_value_rows, "seq", axis=0, tiled=True)
    first_block = jnp.min(segment_start) // block_span

    def inner(counter, current):
        offset = counter * block_span
        key_slice = lax.dynamic_slice_in_dim(key_block, offset, block_span, 0)
        return attend_block(current, key_slice, offset)

    final_state = lax.fori_loop(first_block, seq_rank, inner, state)
    picked = jnp.take(key_block, source_row, axis=0)
    cache = jnp.where(source_live[:, None], picked, jnp.zeros_like(picked))
    maxima, totals, running = final_state
    attended = (
        (running / jnp.transpose(totals, (2, 0, 1))[..., None])
        .reshape(row_count, -1)
        .astype(jnp.bfloat16)
    )
    return (attended, cache)


def solution(mesh):
    placed = (
        P(("seq", "tp"), None),
        P(),
        P(None, "tp"),
        P(None, "tp"),
        P(),
        P(),
        P(),
        P("seq"),
        P(),
        P(),
    )
    return jax.shard_map(
        on_device,
        mesh=mesh,
        in_specs=placed,
        out_specs=(P("seq", "tp"), P("seq", "tp")),
        check_vma=False,
    )
```

```python
import math

import jax
import jax.numpy as jnp
from jax import lax
from jax.sharding import PartitionSpec as P

CACHE_DEV = 8192


rope_base = 1000000.0
query_scalar = 168.0
epsilon = 1e-06


def rms_scale(values, gains):
    return values * lax.rsqrt(jnp.mean(values * values, axis=-1, keepdims=True) + epsilon) * gains


def rope_table(positions, head_width):
    half_width = head_width // 2
    frequency = jnp.exp(
        jnp.arange(half_width, dtype=jnp.float32) * (-2.0 * math.log(rope_base) / head_width)
    )
    angles = positions.astype(jnp.float32)[:, None] * frequency[None, :]
    return (jnp.cos(angles), jnp.sin(angles))


def rotate_pairs(values, cosine, sine_table):
    half_width = values.shape[-1] // 2
    front_half = values[..., :half_width]
    back_half = values[..., half_width:]
    cos_part = cosine[:, None, :]
    sin_part = sine_table[:, None, :]
    return jnp.concatenate(
        [
            front_half * cos_part - back_half * sin_part,
            back_half * cos_part + front_half * sin_part,
        ],
        axis=-1,
    )


def project(tokens, norm_gain, w_query, key_value_weight, query_gain, key_gain, positions):
    token_count = tokens.shape[0]
    head_width = query_gain.shape[0]
    as_float = tokens.astype(jnp.float32)
    normed = rms_scale(as_float, norm_gain).astype(jnp.bfloat16)
    query_raw = jnp.dot(normed, w_query, preferred_element_type=jnp.float32)
    keyval_raw = jnp.dot(normed, key_value_weight, preferred_element_type=jnp.float32)
    cosine, sine_table = rope_table(positions, head_width)
    query_rows = rotate_pairs(
        rms_scale(query_raw.reshape(token_count, -1, head_width), query_gain), cosine, sine_table
    ) * query_scalar ** (-0.5)
    split_kv = keyval_raw.reshape(token_count, -1, 2, head_width)
    keys = rotate_pairs(rms_scale(split_kv[:, :, 0], key_gain), cosine, sine_table)
    key_value_rows = (
        jnp.stack([keys, split_kv[:, :, 1]], axis=2).reshape(token_count, -1).astype(jnp.bfloat16)
    )
    return (query_rows.reshape(token_count, -1).astype(jnp.bfloat16), key_value_rows)


def prompt_starts(segment_ids, lengths):
    starts = jnp.cumsum(lengths) - lengths
    prompt_ids = jnp.arange(lengths.shape[0], dtype=jnp.int32)
    chosen = jnp.where(segment_ids[:, None] == prompt_ids[None, :], starts[None, :], jnp.int32(0))
    return jnp.sum(chosen, axis=1)


def sources(cache_index, lengths, req_counts, req_slots):
    starts = jnp.cumsum(lengths) - lengths
    prompt_ids = jnp.arange(lengths.shape[0], dtype=jnp.int32)
    request_ids = jnp.arange(req_slots.shape[0], dtype=jnp.int32)
    request_ends = jnp.cumsum(req_counts)
    owner_prompt = jnp.sum(
        (request_ends[None, :] <= request_ids[:, None]).astype(jnp.int32), axis=1
    )
    matches = owner_prompt[:, None] == prompt_ids[None, :]
    request_length = jnp.sum(jnp.where(matches, lengths[None, :], jnp.int32(0)), axis=1)
    request_start = jnp.sum(jnp.where(matches, starts[None, :], jnp.int32(0)), axis=1)
    inside = (cache_index[:, None] >= req_slots[None, :]) & (
        cache_index[:, None] < req_slots[None, :] + request_length[None, :]
    )
    offsets = request_start[None, :] + cache_index[:, None] - req_slots[None, :]
    source_row = jnp.sum(jnp.where(inside, offsets, jnp.int32(0)), axis=1)
    source_live = jnp.max(inside.astype(jnp.int32), axis=1) > 0
    return (source_row, source_live)


def others_over_tp(tokens):
    tp_size = lax.axis_size("tp")
    tp_rank = lax.axis_index("tp")
    rows = tokens.shape[0]
    others = jnp.zeros(((tp_size - 1) * rows,) + tokens.shape[1:], tokens.dtype)
    for shift in range(1, tp_size):
        pairs = [(i, (i + shift) % tp_size) for i in range(tp_size)]
        got = lax.ppermute(tokens, "tp", pairs)
        source = (tp_rank - shift) % tp_size
        place = jnp.where(source < tp_rank, source, source - 1)
        others = lax.dynamic_update_slice_in_dim(others, got, place * rows, 0)
    return others


def other_chunk_index(tp_rank, chunk_rows, other_rows):
    place = jnp.arange(other_rows, dtype=jnp.int32) // chunk_rows
    chunk = jnp.where(place < tp_rank, place, place + 1)
    return chunk * chunk_rows + jnp.arange(other_rows, dtype=jnp.int32) % chunk_rows


def on_device(
    tokens,
    norm_gain,
    w_query,
    key_value_weight,
    query_gain,
    key_gain,
    lengths,
    segment_ids,
    req_counts,
    req_slots,
):
    tp_size = lax.axis_size("tp")
    tp_rank = lax.axis_index("tp")
    seq_size = lax.axis_size("seq")
    seq_rank = lax.axis_index("seq")
    chunk_rows = tokens.shape[0]
    row_count = chunk_rows * tp_size
    other_rows = row_count - chunk_rows
    first_row = seq_rank * row_count
    segment_start = prompt_starts(segment_ids, lengths)
    head_width = query_gain.shape[0]

    own_local = tp_rank * chunk_rows + jnp.arange(chunk_rows, dtype=jnp.int32)
    own_start = jnp.take(segment_start, own_local)
    own_q, own_kv = project(
        tokens, norm_gain, w_query, key_value_weight, query_gain, key_gain,
        first_row + own_local - own_start,
    )
    own_all = lax.all_gather(own_kv, "seq", axis=0, tiled=True)

    other_tokens = others_over_tp(tokens)
    other_tokens, own_all = lax.optimization_barrier((other_tokens, own_all))
    other_local = other_chunk_index(tp_rank, chunk_rows, other_rows)
    other_start = jnp.take(segment_start, other_local)
    other_q, other_kv = project(
        other_tokens, norm_gain, w_query, key_value_weight, query_gain, key_gain,
        first_row + other_local - other_start,
    )
    other_all = lax.all_gather(other_kv, "seq", axis=0, tiled=True)

    def to_block_order(own_part, other_part):
        whole = jnp.zeros((row_count,) + own_part.shape[1:], own_part.dtype)
        whole = whole.at[other_local].set(other_part, unique_indices=True)
        return lax.dynamic_update_slice_in_dim(whole, own_part, tp_rank * chunk_rows, 0)

    query_rows = to_block_order(own_q, other_q)
    key_value_rows = to_block_order(own_kv, other_kv)
    kv_heads = key_value_rows.shape[1] // (2 * head_width)
    query_heads = query_rows.reshape(row_count, kv_heads, 2, head_width)
    query_index = first_row + jnp.arange(row_count, dtype=jnp.int32)
    cache_rows = CACHE_DEV
    cache_index = seq_rank * cache_rows + jnp.arange(cache_rows, dtype=jnp.int32)
    source_row, source_live = sources(cache_index, lengths, req_counts, req_slots)

    def attend_block(state_now, key_block, key_index):
        maxima, totals, running = state_now
        key_count = key_block.shape[0]
        grouped_heads = key_block.reshape(key_count, kv_heads, 2, head_width)
        key_part = grouped_heads[:, :, 0]
        value_part = grouped_heads[:, :, 1]
        allowed = (key_index[None, :] >= segment_start[:, None]) & (
            key_index[None, :] <= query_index[:, None]
        )
        scores = jnp.einsum(
            "qgrd,kgd->grqk", query_heads, key_part, preferred_element_type=jnp.float32
        )
        new_maxima = jnp.maximum(maxima, jnp.max(jnp.where(allowed, scores, -1e30), axis=-1))
        factor = jnp.exp(maxima - new_maxima)
        exp_scores = jnp.where(allowed, jnp.exp(scores - new_maxima[..., None]), 0.0)
        totals = totals * factor + jnp.sum(exp_scores, axis=-1)
        weighted = jnp.einsum(
            "grqk,kgd->qgrd",
            exp_scores.astype(jnp.bfloat16),
            value_part,
            preferred_element_type=jnp.float32,
        )
        running = running * jnp.transpose(factor, (2, 0, 1))[..., None] + weighted
        return (new_maxima, totals, running)

    initial = (
        jnp.full((kv_heads, 2, row_count), -1e30, jnp.float32),
        jnp.zeros((kv_heads, 2, row_count), jnp.float32),
        jnp.zeros((row_count, kv_heads, 2, head_width), jnp.float32),
    )
    first_block = jnp.min(segment_start) // row_count
    own_key = tp_rank * chunk_rows + jnp.arange(chunk_rows, dtype=jnp.int32)

    def own_step(block, current):
        keys = lax.dynamic_slice_in_dim(own_all, block * chunk_rows, chunk_rows, 0)
        return attend_block(current, keys, block * row_count + own_key)

    def other_step(block, current):
        keys = lax.dynamic_slice_in_dim(other_all, block * other_rows, other_rows, 0)
        return attend_block(current, keys, block * row_count + other_local)

    state = lax.fori_loop(first_block, seq_rank, own_step, initial)
    state = attend_block(state, key_value_rows, query_index)
    final_state = lax.fori_loop(first_block, seq_rank, other_step, state)

    source_block = source_row // row_count
    source_within = source_row % row_count
    source_chunk = source_within // chunk_rows
    source_place = jnp.where(source_chunk < tp_rank, source_chunk, source_chunk - 1)
    table_row = jnp.where(
        source_chunk == tp_rank,
        source_block * chunk_rows + source_within % chunk_rows,
        seq_size * chunk_rows
        + source_block * other_rows
        + source_place * chunk_rows
        + source_within % chunk_rows,
    )
    table = jnp.concatenate([own_all, other_all], axis=0)
    picked = jnp.take(table, table_row, axis=0)
    cache = jnp.where(source_live[:, None], picked, jnp.zeros_like(picked))
    maxima, totals, running = final_state
    attended = (
        (running / jnp.transpose(totals, (2, 0, 1))[..., None])
        .reshape(row_count, -1)
        .astype(jnp.bfloat16)
    )
    return (attended, cache)


def solution(mesh):
    placed = (
        P(("seq", "tp"), None),
        P(),
        P(None, "tp"),
        P(None, "tp"),
        P(),
        P(),
        P(),
        P("seq"),
        P(),
        P(),
    )
    return jax.shard_map(
        on_device,
        mesh=mesh,
        in_specs=placed,
        out_specs=(P("seq", "tp"), P("seq", "tp")),
        check_vma=False,
    )
```

```python
import math

import jax
import jax.numpy as jnp
from jax import lax
from jax.sharding import PartitionSpec as P
from jax.experimental import pallas as pl
from jax.experimental.pallas import tpu as pltpu

CACHE_DEV = 8192


rope_base = 1000000.0
query_scalar = 168.0
epsilon = 1e-06


def rms_scale(values, gains):
    return values * lax.rsqrt(jnp.mean(values * values, axis=-1, keepdims=True) + epsilon) * gains


def rope_table(positions, head_width):
    half_width = head_width // 2
    frequency = jnp.exp(
        jnp.arange(half_width, dtype=jnp.float32) * (-2.0 * math.log(rope_base) / head_width)
    )
    angles = positions.astype(jnp.float32)[:, None] * frequency[None, :]
    return (jnp.cos(angles), jnp.sin(angles))


def rotate_pairs(values, cosine, sine_table):
    half_width = values.shape[-1] // 2
    front_half = values[..., :half_width]
    back_half = values[..., half_width:]
    cos_part = cosine[:, None, :]
    sin_part = sine_table[:, None, :]
    return jnp.concatenate(
        [
            front_half * cos_part - back_half * sin_part,
            back_half * cos_part + front_half * sin_part,
        ],
        axis=-1,
    )


def project(tokens, norm_gain, w_query, key_value_weight, query_gain, key_gain, positions):
    token_count = tokens.shape[0]
    head_width = query_gain.shape[0]
    as_float = tokens.astype(jnp.float32)
    normed = rms_scale(as_float, norm_gain).astype(jnp.bfloat16)
    query_raw = jnp.dot(normed, w_query, preferred_element_type=jnp.float32)
    keyval_raw = jnp.dot(normed, key_value_weight, preferred_element_type=jnp.float32)
    cosine, sine_table = rope_table(positions, head_width)
    query_rows = rotate_pairs(
        rms_scale(query_raw.reshape(token_count, -1, head_width), query_gain), cosine, sine_table
    ) * query_scalar ** (-0.5)
    split_kv = keyval_raw.reshape(token_count, -1, 2, head_width)
    keys = rotate_pairs(rms_scale(split_kv[:, :, 0], key_gain), cosine, sine_table)
    key_value_rows = (
        jnp.stack([keys, split_kv[:, :, 1]], axis=2).reshape(token_count, -1).astype(jnp.bfloat16)
    )
    return (query_rows.reshape(token_count, -1).astype(jnp.bfloat16), key_value_rows)


def prompt_starts(segment_ids, lengths):
    starts = jnp.cumsum(lengths) - lengths
    prompt_ids = jnp.arange(lengths.shape[0], dtype=jnp.int32)
    chosen = jnp.where(segment_ids[:, None] == prompt_ids[None, :], starts[None, :], jnp.int32(0))
    return jnp.sum(chosen, axis=1)


def sources(cache_index, lengths, req_counts, req_slots):
    starts = jnp.cumsum(lengths) - lengths
    prompt_ids = jnp.arange(lengths.shape[0], dtype=jnp.int32)
    request_ids = jnp.arange(req_slots.shape[0], dtype=jnp.int32)
    request_ends = jnp.cumsum(req_counts)
    owner_prompt = jnp.sum(
        (request_ends[None, :] <= request_ids[:, None]).astype(jnp.int32), axis=1
    )
    matches = owner_prompt[:, None] == prompt_ids[None, :]
    request_length = jnp.sum(jnp.where(matches, lengths[None, :], jnp.int32(0)), axis=1)
    request_start = jnp.sum(jnp.where(matches, starts[None, :], jnp.int32(0)), axis=1)
    inside = (cache_index[:, None] >= req_slots[None, :]) & (
        cache_index[:, None] < req_slots[None, :] + request_length[None, :]
    )
    offsets = request_start[None, :] + cache_index[:, None] - req_slots[None, :]
    source_row = jnp.sum(jnp.where(inside, offsets, jnp.int32(0)), axis=1)
    source_live = jnp.max(inside.astype(jnp.int32), axis=1) > 0
    return (source_row, source_live)


def request_runs(dev_lo, dev_rows, lengths, req_counts, req_slots):
    starts = (jnp.cumsum(lengths) - lengths).astype(jnp.int32)
    prompt_ids = jnp.arange(lengths.shape[0], dtype=jnp.int32)
    request_ids = jnp.arange(req_slots.shape[0], dtype=jnp.int32)
    request_ends = jnp.cumsum(req_counts).astype(jnp.int32)
    owner_prompt = jnp.sum((request_ends[None, :] <= request_ids[:, None]).astype(jnp.int32), axis=1)
    matches = owner_prompt[:, None] == prompt_ids[None, :]
    request_length = jnp.sum(jnp.where(matches, lengths[None, :], 0), axis=1).astype(jnp.int32)
    request_start = jnp.sum(jnp.where(matches, starts[None, :], 0), axis=1).astype(jnp.int32)
    low = jnp.maximum(req_slots, dev_lo)
    high = jnp.minimum(req_slots + request_length, dev_lo + dev_rows)
    count = jnp.maximum(high - low, 0)
    live = count > 0
    source = jnp.where(live, request_start + low - req_slots, 0).astype(jnp.int32)
    dest = jnp.where(live, low - dev_lo, 0).astype(jnp.int32)
    return dest, source, jnp.where(live, count, 0).astype(jnp.int32)


def fill_cache(key_rows, dest, source, count, dev_rows):
    n_req = dest.shape[0]
    n_bits = max(1, int(dev_rows).bit_length())

    def each_copy(r, start, key_ref, out_ref, sem, dest_ref, source_ref, count_ref):
        n = count_ref[r]
        parity = r % 2

        @pl.when(n > 0)
        def _():
            s0 = source_ref[r]
            d0 = dest_ref[r]
            for b in range(n_bits):
                size = 1 << b
                offset = n & (size - 1)

                @pl.when((n & size) != 0)
                def _():
                    cp = pltpu.make_async_copy(
                        key_ref.at[pl.ds(s0 + offset, size)],
                        out_ref.at[pl.ds(d0 + offset, size)],
                        sem.at[parity, b],
                    )
                    if start:
                        cp.start()
                    else:
                        cp.wait()

    def kernel(dest_ref, source_ref, count_ref, key_ref, zero_ref, out_ref, sem):
        def body(r, carry):
            each_copy(r, True, key_ref, out_ref, sem, dest_ref, source_ref, count_ref)

            @pl.when(r > 0)
            def _():
                each_copy(r - 1, False, key_ref, out_ref, sem, dest_ref, source_ref, count_ref)

            return carry

        lax.fori_loop(0, n_req, body, 0)
        each_copy(n_req - 1, False, key_ref, out_ref, sem, dest_ref, source_ref, count_ref)

    zeros = jnp.zeros((dev_rows,) + key_rows.shape[1:], key_rows.dtype)
    grid_spec = pltpu.PrefetchScalarGridSpec(
        num_scalar_prefetch=3,
        grid=(1,),
        in_specs=[pl.BlockSpec(memory_space=pl.ANY), pl.BlockSpec(memory_space=pl.ANY)],
        out_specs=pl.BlockSpec(memory_space=pl.ANY),
        scratch_shapes=[pltpu.SemaphoreType.DMA((2, n_bits))],
    )
    return pl.pallas_call(
        kernel,
        grid_spec=grid_spec,
        out_shape=jax.ShapeDtypeStruct(zeros.shape, key_rows.dtype),
        input_output_aliases={4: 0},
    )(dest, source, count, key_rows, zeros)


def gather_tp(tokens):
    tp_size = lax.axis_size("tp")
    tp_rank = lax.axis_index("tp")
    rows = tokens.shape[0]
    gathered = jnp.zeros((tp_size * rows,) + tokens.shape[1:], tokens.dtype)
    gathered = lax.dynamic_update_slice_in_dim(gathered, tokens, tp_rank * rows, 0)
    for shift in range(1, tp_size):
        pairs = [(i, (i + shift) % tp_size) for i in range(tp_size)]
        got = lax.ppermute(tokens, "tp", pairs)
        source = (tp_rank - shift) % tp_size
        gathered = lax.dynamic_update_slice_in_dim(gathered, got, source * rows, 0)
    return gathered


def on_device(
    tokens,
    norm_gain,
    w_query,
    key_value_weight,
    query_gain,
    key_gain,
    lengths,
    segment_ids,
    req_counts,
    req_slots,
):
    gathered = gather_tp(tokens)
    row_count = gathered.shape[0]
    seq_rank = lax.axis_index("seq")
    first_row = seq_rank * row_count
    query_index = first_row + jnp.arange(row_count, dtype=jnp.int32)
    segment_start = prompt_starts(segment_ids, lengths)
    positions = query_index - segment_start
    query_rows, key_value_rows = project(
        gathered, norm_gain, w_query, key_value_weight, query_gain, key_gain, positions
    )
    head_width = query_gain.shape[0]
    kv_heads = key_value_rows.shape[1] // (2 * head_width)
    query_heads = query_rows.reshape(row_count, kv_heads, 2, head_width)
    cache_rows = CACHE_DEV
    dest, source, count = request_runs(
        seq_rank * cache_rows, cache_rows, lengths, req_counts, req_slots
    )

    def attend_block(state_now, key_block, block_start):
        maxima, totals, running = state_now
        key_count = key_block.shape[0]
        grouped_heads = key_block.reshape(key_count, kv_heads, 2, head_width)
        key_part = grouped_heads[:, :, 0]
        value_part = grouped_heads[:, :, 1]
        key_index = block_start + jnp.arange(key_count, dtype=jnp.int32)
        allowed = (key_index[None, :] >= segment_start[:, None]) & (
            key_index[None, :] <= query_index[:, None]
        )
        scores = jnp.einsum(
            "qgrd,kgd->grqk", query_heads, key_part, preferred_element_type=jnp.float32
        )
        new_maxima = jnp.maximum(maxima, jnp.max(jnp.where(allowed, scores, -1e30), axis=-1))
        factor = jnp.exp(maxima - new_maxima)
        exp_scores = jnp.where(allowed, jnp.exp(scores - new_maxima[..., None]), 0.0)
        totals = totals * factor + jnp.sum(exp_scores, axis=-1)
        weighted = jnp.einsum(
            "grqk,kgd->qgrd",
            exp_scores.astype(jnp.bfloat16),
            value_part,
            preferred_element_type=jnp.float32,
        )
        running = running * jnp.transpose(factor, (2, 0, 1))[..., None] + weighted
        return (new_maxima, totals, running)

    initial = (
        jnp.full((kv_heads, 2, row_count), -1e30, jnp.float32),
        jnp.zeros((kv_heads, 2, row_count), jnp.float32),
        jnp.zeros((row_count, kv_heads, 2, head_width), jnp.float32),
    )
    block_span = row_count
    state = attend_block(initial, key_value_rows, first_row)
    key_block = lax.all_gather(key_value_rows, "seq", axis=0, tiled=True)
    key_count = key_block.shape[0]
    first_block = jnp.min(segment_start) // block_span

    def inner(counter, current):
        offset = counter * block_span
        key_slice = lax.dynamic_slice_in_dim(key_block, offset, block_span, 0)
        return attend_block(current, key_slice, offset)

    final_state = lax.fori_loop(first_block, seq_rank, inner, state)
    width = key_block.shape[1]
    cache = fill_cache(
        key_block.reshape(key_count, width // 128, 128), dest, source, count, cache_rows
    ).reshape(cache_rows, width)
    maxima, totals, running = final_state
    attended = (
        (running / jnp.transpose(totals, (2, 0, 1))[..., None])
        .reshape(row_count, -1)
        .astype(jnp.bfloat16)
    )
    return (attended, cache)


def solution(mesh):
    placed = (
        P(("seq", "tp"), None),
        P(),
        P(None, "tp"),
        P(None, "tp"),
        P(),
        P(),
        P(),
        P("seq"),
        P(),
        P(),
    )
    return jax.shard_map(
        on_device,
        mesh=mesh,
        in_specs=placed,
        out_specs=(P("seq", "tp"), P("seq", "tp")),
        check_vma=False,
    )
```

```python
import math

import jax
import jax.numpy as jnp
from jax import lax
from jax.sharding import PartitionSpec as P

CACHE_DEV = 8192


rope_base = 1000000.0
query_scalar = 168.0
epsilon = 1e-06


def rms_scale(values, gains):
    return values * lax.rsqrt(jnp.mean(values * values, axis=-1, keepdims=True) + epsilon) * gains


def rope_table(positions, head_width):
    half_width = head_width // 2
    frequency = jnp.exp(
        jnp.arange(half_width, dtype=jnp.float32) * (-2.0 * math.log(rope_base) / head_width)
    )
    angles = positions.astype(jnp.float32)[:, None] * frequency[None, :]
    return (jnp.cos(angles), jnp.sin(angles))


def rotate_pairs(values, cosine, sine_table):
    half_width = values.shape[-1] // 2
    front_half = values[..., :half_width]
    back_half = values[..., half_width:]
    cos_part = cosine[:, None, :]
    sin_part = sine_table[:, None, :]
    return jnp.concatenate(
        [
            front_half * cos_part - back_half * sin_part,
            back_half * cos_part + front_half * sin_part,
        ],
        axis=-1,
    )


def project(tokens, norm_gain, w_query, key_value_weight, query_gain, key_gain, positions):
    token_count = tokens.shape[0]
    head_width = query_gain.shape[0]
    as_float = tokens.astype(jnp.float32)
    normed = rms_scale(as_float, norm_gain).astype(jnp.bfloat16)
    query_raw = jnp.dot(normed, w_query, preferred_element_type=jnp.float32)
    keyval_raw = jnp.dot(normed, key_value_weight, preferred_element_type=jnp.float32)
    cosine, sine_table = rope_table(positions, head_width)
    query_rows = rotate_pairs(
        rms_scale(query_raw.reshape(token_count, -1, head_width), query_gain), cosine, sine_table
    ) * query_scalar ** (-0.5)
    split_kv = keyval_raw.reshape(token_count, -1, 2, head_width)
    keys = rotate_pairs(rms_scale(split_kv[:, :, 0], key_gain), cosine, sine_table)
    key_value_rows = (
        jnp.stack([keys, split_kv[:, :, 1]], axis=2).reshape(token_count, -1).astype(jnp.bfloat16)
    )
    return (query_rows.reshape(token_count, -1).astype(jnp.bfloat16), key_value_rows)


def prompt_starts(segment_ids, lengths):
    starts = jnp.cumsum(lengths) - lengths
    prompt_ids = jnp.arange(lengths.shape[0], dtype=jnp.int32)
    chosen = jnp.where(segment_ids[:, None] == prompt_ids[None, :], starts[None, :], jnp.int32(0))
    return jnp.sum(chosen, axis=1)


def sources(cache_index, lengths, req_counts, req_slots):
    starts = jnp.cumsum(lengths) - lengths
    prompt_ids = jnp.arange(lengths.shape[0], dtype=jnp.int32)
    request_ids = jnp.arange(req_slots.shape[0], dtype=jnp.int32)
    request_ends = jnp.cumsum(req_counts)
    owner_prompt = jnp.sum(
        (request_ends[None, :] <= request_ids[:, None]).astype(jnp.int32), axis=1
    )
    matches = owner_prompt[:, None] == prompt_ids[None, :]
    request_length = jnp.sum(jnp.where(matches, lengths[None, :], jnp.int32(0)), axis=1)
    request_start = jnp.sum(jnp.where(matches, starts[None, :], jnp.int32(0)), axis=1)
    inside = (cache_index[:, None] >= req_slots[None, :]) & (
        cache_index[:, None] < req_slots[None, :] + request_length[None, :]
    )
    offsets = request_start[None, :] + cache_index[:, None] - req_slots[None, :]
    source_row = jnp.sum(jnp.where(inside, offsets, jnp.int32(0)), axis=1)
    source_live = jnp.max(inside.astype(jnp.int32), axis=1) > 0
    return (source_row, source_live)


def gather_tp(tokens):
    tp_size = lax.axis_size("tp")
    tp_rank = lax.axis_index("tp")
    rows = tokens.shape[0]
    gathered = jnp.zeros((tp_size * rows,) + tokens.shape[1:], tokens.dtype)
    gathered = lax.dynamic_update_slice_in_dim(gathered, tokens, tp_rank * rows, 0)
    for shift in range(1, tp_size):
        pairs = [(i, (i + shift) % tp_size) for i in range(tp_size)]
        got = lax.ppermute(tokens, "tp", pairs)
        source = (tp_rank - shift) % tp_size
        gathered = lax.dynamic_update_slice_in_dim(gathered, got, source * rows, 0)
    return gathered


def on_device(
    tokens,
    norm_gain,
    w_query,
    key_value_weight,
    query_gain,
    key_gain,
    lengths,
    segment_ids,
    req_counts,
    req_slots,
):
    gathered = gather_tp(tokens)
    row_count = gathered.shape[0]
    seq_rank = lax.axis_index("seq")
    first_row = seq_rank * row_count
    query_index = first_row + jnp.arange(row_count, dtype=jnp.int32)
    segment_start = prompt_starts(segment_ids, lengths)
    positions = query_index - segment_start
    query_rows, key_value_rows = project(
        gathered, norm_gain, w_query, key_value_weight, query_gain, key_gain, positions
    )
    head_width = query_gain.shape[0]
    kv_heads = key_value_rows.shape[1] // (2 * head_width)
    query_heads = query_rows.reshape(row_count, kv_heads, 2, head_width)
    cache_rows = CACHE_DEV
    cache_index = seq_rank * cache_rows + jnp.arange(cache_rows, dtype=jnp.int32)
    source_row, source_live = sources(cache_index, lengths, req_counts, req_slots)

    def attend_block(state_now, key_block, block_start, key_end):
        maxima, totals, running = state_now
        key_count = key_block.shape[0]
        grouped_heads = key_block.reshape(key_count, kv_heads, 2, head_width)
        key_part = grouped_heads[:, :, 0]
        value_part = grouped_heads[:, :, 1]
        key_index = block_start + jnp.arange(key_count, dtype=jnp.int32)
        allowed = (
            (key_index[None, :] >= segment_start[:, None])
            & (key_index[None, :] <= query_index[:, None])
            & (key_index[None, :] < key_end)
        )
        scores = jnp.einsum(
            "qgrd,kgd->grqk", query_heads, key_part, preferred_element_type=jnp.float32
        )
        new_maxima = jnp.maximum(maxima, jnp.max(jnp.where(allowed, scores, -1e30), axis=-1))
        factor = jnp.exp(maxima - new_maxima)
        exp_scores = jnp.where(allowed, jnp.exp(scores - new_maxima[..., None]), 0.0)
        totals = totals * factor + jnp.sum(exp_scores, axis=-1)
        weighted = jnp.einsum(
            "grqk,kgd->qgrd",
            exp_scores.astype(jnp.bfloat16),
            value_part,
            preferred_element_type=jnp.float32,
        )
        running = running * jnp.transpose(factor, (2, 0, 1))[..., None] + weighted
        return (new_maxima, totals, running)

    initial = (
        jnp.full((kv_heads, 2, row_count), -1e30, jnp.float32),
        jnp.zeros((kv_heads, 2, row_count), jnp.float32),
        jnp.zeros((row_count, kv_heads, 2, head_width), jnp.float32),
    )
    state = attend_block(initial, key_value_rows, first_row, first_row + row_count)
    key_block = lax.all_gather(key_value_rows, "seq", axis=0, tiled=True)
    key_count = key_block.shape[0]
    step_span = min(2 * row_count, key_count)
    earliest = jnp.min(segment_start)
    steps = (first_row - earliest + step_span - 1) // step_span

    def inner(counter, current):
        key_end = first_row - counter * step_span
        offset = jnp.maximum(key_end - step_span, 0)
        key_slice = lax.dynamic_slice_in_dim(key_block, offset, step_span, 0)
        return attend_block(current, key_slice, offset, key_end)

    final_state = lax.fori_loop(0, steps, inner, state)
    picked = jnp.take(key_block, source_row, axis=0)
    cache = jnp.where(source_live[:, None], picked, jnp.zeros_like(picked))
    maxima, totals, running = final_state
    attended = (
        (running / jnp.transpose(totals, (2, 0, 1))[..., None])
        .reshape(row_count, -1)
        .astype(jnp.bfloat16)
    )
    return (attended, cache)


def solution(mesh):
    placed = (
        P(("seq", "tp"), None),
        P(),
        P(None, "tp"),
        P(None, "tp"),
        P(),
        P(),
        P(),
        P("seq"),
        P(),
        P(),
    )
    return jax.shard_map(
        on_device,
        mesh=mesh,
        in_specs=placed,
        out_specs=(P("seq", "tp"), P("seq", "tp")),
        check_vma=False,
    )
```

```python
import math

import jax
import jax.numpy as jnp
from jax import lax
from jax.sharding import PartitionSpec as P
from jax.experimental import pallas as pl
from jax.experimental.pallas import tpu as pltpu

CACHE_DEV = 8192


rope_base = 1000000.0
query_scalar = 168.0
epsilon = 1e-06


def rms_scale(values, gains):
    return values * lax.rsqrt(jnp.mean(values * values, axis=-1, keepdims=True) + epsilon) * gains


def rope_table(positions, head_width):
    half_width = head_width // 2
    frequency = jnp.exp(
        jnp.arange(half_width, dtype=jnp.float32) * (-2.0 * math.log(rope_base) / head_width)
    )
    angles = positions.astype(jnp.float32)[:, None] * frequency[None, :]
    return (jnp.cos(angles), jnp.sin(angles))


def rotate_pairs(values, cosine, sine_table):
    half_width = values.shape[-1] // 2
    front_half = values[..., :half_width]
    back_half = values[..., half_width:]
    cos_part = cosine[:, None, :]
    sin_part = sine_table[:, None, :]
    return jnp.concatenate(
        [
            front_half * cos_part - back_half * sin_part,
            back_half * cos_part + front_half * sin_part,
        ],
        axis=-1,
    )


def project(tokens, norm_gain, w_query, key_value_weight, query_gain, key_gain, positions):
    token_count = tokens.shape[0]
    head_width = query_gain.shape[0]
    as_float = tokens.astype(jnp.float32)
    normed = rms_scale(as_float, norm_gain).astype(jnp.bfloat16)
    query_raw = jnp.dot(normed, w_query, preferred_element_type=jnp.float32)
    keyval_raw = jnp.dot(normed, key_value_weight, preferred_element_type=jnp.float32)
    cosine, sine_table = rope_table(positions, head_width)
    query_rows = rotate_pairs(
        rms_scale(query_raw.reshape(token_count, -1, head_width), query_gain), cosine, sine_table
    ) * query_scalar ** (-0.5)
    split_kv = keyval_raw.reshape(token_count, -1, 2, head_width)
    keys = rotate_pairs(rms_scale(split_kv[:, :, 0], key_gain), cosine, sine_table)
    key_value_rows = (
        jnp.stack([keys, split_kv[:, :, 1]], axis=2).reshape(token_count, -1).astype(jnp.bfloat16)
    )
    return (query_rows.reshape(token_count, -1).astype(jnp.bfloat16), key_value_rows)


def prompt_starts(segment_ids, lengths):
    starts = jnp.cumsum(lengths) - lengths
    prompt_ids = jnp.arange(lengths.shape[0], dtype=jnp.int32)
    chosen = jnp.where(segment_ids[:, None] == prompt_ids[None, :], starts[None, :], jnp.int32(0))
    return jnp.sum(chosen, axis=1)


def sources(cache_index, lengths, req_counts, req_slots):
    starts = jnp.cumsum(lengths) - lengths
    prompt_ids = jnp.arange(lengths.shape[0], dtype=jnp.int32)
    request_ids = jnp.arange(req_slots.shape[0], dtype=jnp.int32)
    request_ends = jnp.cumsum(req_counts)
    owner_prompt = jnp.sum(
        (request_ends[None, :] <= request_ids[:, None]).astype(jnp.int32), axis=1
    )
    matches = owner_prompt[:, None] == prompt_ids[None, :]
    request_length = jnp.sum(jnp.where(matches, lengths[None, :], jnp.int32(0)), axis=1)
    request_start = jnp.sum(jnp.where(matches, starts[None, :], jnp.int32(0)), axis=1)
    inside = (cache_index[:, None] >= req_slots[None, :]) & (
        cache_index[:, None] < req_slots[None, :] + request_length[None, :]
    )
    offsets = request_start[None, :] + cache_index[:, None] - req_slots[None, :]
    source_row = jnp.sum(jnp.where(inside, offsets, jnp.int32(0)), axis=1)
    source_live = jnp.max(inside.astype(jnp.int32), axis=1) > 0
    return (source_row, source_live)


def flash_attention(query_rows, key_block, segment_start, diagonal, first_block, head_width):
    row_count, q_width = query_rows.shape
    key_count, kv_width = key_block.shape
    n_heads = q_width // head_width
    group = n_heads // (kv_width // (2 * head_width))
    span = row_count
    n_blocks = key_count // span
    meta = jnp.stack([diagonal, first_block]).astype(jnp.int32)
    seg = segment_start.reshape(row_count, 1).astype(jnp.int32)

    def kv_map(step, meta_ref):
        return (jnp.maximum(meta_ref[0] - step, meta_ref[1]), 0)

    def kernel(meta_ref, q_ref, kv_ref, seg_ref, o_ref, m_ref, l_ref, acc_ref):
        step = pl.program_id(0)
        block = meta_ref[0] - step

        @pl.when(step == 0)
        def _():
            m_ref[...] = jnp.full(m_ref.shape, -1e30, jnp.float32)
            l_ref[...] = jnp.zeros(l_ref.shape, jnp.float32)
            acc_ref[...] = jnp.zeros(acc_ref.shape, jnp.float32)

        @pl.when(block >= meta_ref[1])
        def _():
            key_index = block * span + lax.broadcasted_iota(jnp.int32, (1, span), 1)
            query_index = meta_ref[0] * span + lax.broadcasted_iota(jnp.int32, (row_count, 1), 0)
            allowed = (key_index >= seg_ref[...]) & (key_index <= query_index)
            for h in range(n_heads):
                g = h // group
                q = q_ref[:, h * head_width:(h + 1) * head_width]
                k = kv_ref[:, 2 * g * head_width:(2 * g + 1) * head_width]
                v = kv_ref[:, (2 * g + 1) * head_width:(2 * g + 2) * head_width]
                s = lax.dot_general(
                    q, k, (((1,), (1,)), ((), ())), preferred_element_type=jnp.float32
                )
                m_prev = m_ref[h]
                m_new = jnp.maximum(
                    m_prev, jnp.max(jnp.where(allowed, s, -1e30), axis=1, keepdims=True)
                )
                factor = jnp.exp(m_prev - m_new)
                p = jnp.where(allowed, jnp.exp(s - m_new), 0.0)
                l_ref[h] = l_ref[h] * factor + jnp.sum(p, axis=1, keepdims=True)
                acc_ref[h] = acc_ref[h] * factor + jnp.dot(
                    p.astype(jnp.bfloat16), v, preferred_element_type=jnp.float32
                )
                m_ref[h] = m_new

        @pl.when(step == n_blocks - 1)
        def _():
            for h in range(n_heads):
                o_ref[:, h * head_width:(h + 1) * head_width] = (
                    acc_ref[h] / l_ref[h]
                ).astype(o_ref.dtype)

    grid_spec = pltpu.PrefetchScalarGridSpec(
        num_scalar_prefetch=1,
        grid=(n_blocks,),
        in_specs=[
            pl.BlockSpec((row_count, q_width), lambda step, meta_ref: (0, 0)),
            pl.BlockSpec((span, kv_width), kv_map),
            pl.BlockSpec((row_count, 1), lambda step, meta_ref: (0, 0)),
        ],
        out_specs=pl.BlockSpec((row_count, q_width), lambda step, meta_ref: (0, 0)),
        scratch_shapes=[
            pltpu.VMEM((n_heads, row_count, 1), jnp.float32),
            pltpu.VMEM((n_heads, row_count, 1), jnp.float32),
            pltpu.VMEM((n_heads, row_count, head_width), jnp.float32),
        ],
    )
    return pl.pallas_call(
        kernel,
        grid_spec=grid_spec,
        out_shape=jax.ShapeDtypeStruct((row_count, q_width), jnp.bfloat16),
        compiler_params=pltpu.CompilerParams(dimension_semantics=("arbitrary",)),
    )(meta, query_rows, key_block, seg)


def gather_tp(tokens):
    tp_size = lax.axis_size("tp")
    tp_rank = lax.axis_index("tp")
    rows = tokens.shape[0]
    gathered = jnp.zeros((tp_size * rows,) + tokens.shape[1:], tokens.dtype)
    gathered = lax.dynamic_update_slice_in_dim(gathered, tokens, tp_rank * rows, 0)
    for shift in range(1, tp_size):
        pairs = [(i, (i + shift) % tp_size) for i in range(tp_size)]
        got = lax.ppermute(tokens, "tp", pairs)
        source = (tp_rank - shift) % tp_size
        gathered = lax.dynamic_update_slice_in_dim(gathered, got, source * rows, 0)
    return gathered


def on_device(
    tokens,
    norm_gain,
    w_query,
    key_value_weight,
    query_gain,
    key_gain,
    lengths,
    segment_ids,
    req_counts,
    req_slots,
):
    gathered = gather_tp(tokens)
    row_count = gathered.shape[0]
    seq_rank = lax.axis_index("seq")
    first_row = seq_rank * row_count
    query_index = first_row + jnp.arange(row_count, dtype=jnp.int32)
    segment_start = prompt_starts(segment_ids, lengths)
    positions = query_index - segment_start
    query_rows, key_value_rows = project(
        gathered, norm_gain, w_query, key_value_weight, query_gain, key_gain, positions
    )
    head_width = query_gain.shape[0]
    kv_heads = key_value_rows.shape[1] // (2 * head_width)
    query_heads = query_rows.reshape(row_count, kv_heads, 2, head_width)
    cache_rows = CACHE_DEV
    cache_index = seq_rank * cache_rows + jnp.arange(cache_rows, dtype=jnp.int32)
    source_row, source_live = sources(cache_index, lengths, req_counts, req_slots)

    key_block = lax.all_gather(key_value_rows, "seq", axis=0, tiled=True)
    first_block = jnp.min(segment_start) // row_count
    attended = flash_attention(
        query_rows, key_block, segment_start, seq_rank, first_block, head_width
    )
    picked = jnp.take(key_block, source_row, axis=0)
    cache = jnp.where(source_live[:, None], picked, jnp.zeros_like(picked))
    return (attended, cache)


def solution(mesh):
    placed = (
        P(("seq", "tp"), None),
        P(),
        P(None, "tp"),
        P(None, "tp"),
        P(),
        P(),
        P(),
        P("seq"),
        P(),
        P(),
    )
    return jax.shard_map(
        on_device,
        mesh=mesh,
        in_specs=placed,
        out_specs=(P("seq", "tp"), P("seq", "tp")),
        check_vma=False,
    )
```

```python
import math

import jax
import jax.numpy as jnp
from jax import lax
from jax.sharding import PartitionSpec as P
from jax.experimental import pallas as pl
from jax.experimental.pallas import tpu as pltpu

CACHE_DEV = 8192


rope_base = 1000000.0
query_scalar = 168.0
epsilon = 1e-06


def rms_scale(values, gains):
    return values * lax.rsqrt(jnp.mean(values * values, axis=-1, keepdims=True) + epsilon) * gains


def rope_table(positions, head_width):
    half_width = head_width // 2
    frequency = jnp.exp(
        jnp.arange(half_width, dtype=jnp.float32) * (-2.0 * math.log(rope_base) / head_width)
    )
    angles = positions.astype(jnp.float32)[:, None] * frequency[None, :]
    return (jnp.cos(angles), jnp.sin(angles))


def rotate_pairs(values, cosine, sine_table):
    half_width = values.shape[-1] // 2
    front_half = values[..., :half_width]
    back_half = values[..., half_width:]
    cos_part = cosine[:, None, :]
    sin_part = sine_table[:, None, :]
    return jnp.concatenate(
        [
            front_half * cos_part - back_half * sin_part,
            back_half * cos_part + front_half * sin_part,
        ],
        axis=-1,
    )


def project(tokens, norm_gain, w_query, key_value_weight, query_gain, key_gain, positions):
    token_count = tokens.shape[0]
    head_width = query_gain.shape[0]
    as_float = tokens.astype(jnp.float32)
    normed = rms_scale(as_float, norm_gain).astype(jnp.bfloat16)
    query_raw = jnp.dot(normed, w_query, preferred_element_type=jnp.float32)
    keyval_raw = jnp.dot(normed, key_value_weight, preferred_element_type=jnp.float32)
    cosine, sine_table = rope_table(positions, head_width)
    query_rows = rotate_pairs(
        rms_scale(query_raw.reshape(token_count, -1, head_width), query_gain), cosine, sine_table
    ) * query_scalar ** (-0.5)
    split_kv = keyval_raw.reshape(token_count, -1, 2, head_width)
    keys = rotate_pairs(rms_scale(split_kv[:, :, 0], key_gain), cosine, sine_table)
    key_value_rows = (
        jnp.stack([keys, split_kv[:, :, 1]], axis=2).reshape(token_count, -1).astype(jnp.bfloat16)
    )
    return (query_rows.reshape(token_count, -1).astype(jnp.bfloat16), key_value_rows)


def prompt_starts(segment_ids, lengths):
    starts = jnp.cumsum(lengths) - lengths
    prompt_ids = jnp.arange(lengths.shape[0], dtype=jnp.int32)
    chosen = jnp.where(segment_ids[:, None] == prompt_ids[None, :], starts[None, :], jnp.int32(0))
    return jnp.sum(chosen, axis=1)


def sources(cache_index, lengths, req_counts, req_slots):
    starts = jnp.cumsum(lengths) - lengths
    prompt_ids = jnp.arange(lengths.shape[0], dtype=jnp.int32)
    request_ids = jnp.arange(req_slots.shape[0], dtype=jnp.int32)
    request_ends = jnp.cumsum(req_counts)
    owner_prompt = jnp.sum(
        (request_ends[None, :] <= request_ids[:, None]).astype(jnp.int32), axis=1
    )
    matches = owner_prompt[:, None] == prompt_ids[None, :]
    request_length = jnp.sum(jnp.where(matches, lengths[None, :], jnp.int32(0)), axis=1)
    request_start = jnp.sum(jnp.where(matches, starts[None, :], jnp.int32(0)), axis=1)
    inside = (cache_index[:, None] >= req_slots[None, :]) & (
        cache_index[:, None] < req_slots[None, :] + request_length[None, :]
    )
    offsets = request_start[None, :] + cache_index[:, None] - req_slots[None, :]
    source_row = jnp.sum(jnp.where(inside, offsets, jnp.int32(0)), axis=1)
    source_live = jnp.max(inside.astype(jnp.int32), axis=1) > 0
    return (source_row, source_live)


def flash_attention(query_rows, key_block, segment_start, diagonal, first_block, head_width):
    row_count, q_width = query_rows.shape
    key_count, kv_width = key_block.shape
    n_heads = q_width // head_width
    group = n_heads // (kv_width // (2 * head_width))
    span = row_count
    n_blocks = key_count // span
    meta = jnp.stack([diagonal, first_block, jnp.max(segment_start)]).astype(jnp.int32)
    seg = segment_start.reshape(row_count, 1).astype(jnp.int32)

    def kv_map(step, meta_ref):
        return (jnp.maximum(meta_ref[0] - step, meta_ref[1]), 0)

    def kernel(meta_ref, q_ref, kv_ref, seg_ref, o_ref, m_ref, l_ref, acc_ref):
        step = pl.program_id(0)
        block = meta_ref[0] - step

        @pl.when(step == 0)
        def _():
            m_ref[...] = jnp.full(m_ref.shape, -1e30, jnp.float32)
            l_ref[...] = jnp.zeros(l_ref.shape, jnp.float32)
            acc_ref[...] = jnp.zeros(acc_ref.shape, jnp.float32)

        def accumulate(masked):
            if masked:
                key_index = block * span + lax.broadcasted_iota(jnp.int32, (1, span), 1)
                query_index = meta_ref[0] * span + lax.broadcasted_iota(
                    jnp.int32, (row_count, 1), 0
                )
                allowed = (key_index >= seg_ref[...]) & (key_index <= query_index)
            for h in range(n_heads):
                g = h // group
                q = q_ref[:, h * head_width:(h + 1) * head_width]
                k = kv_ref[:, 2 * g * head_width:(2 * g + 1) * head_width]
                v = kv_ref[:, (2 * g + 1) * head_width:(2 * g + 2) * head_width]
                s = lax.dot_general(
                    q, k, (((1,), (1,)), ((), ())), preferred_element_type=jnp.float32
                )
                m_prev = m_ref[h]
                if masked:
                    s_top = jnp.max(jnp.where(allowed, s, -1e30), axis=1, keepdims=True)
                else:
                    s_top = jnp.max(s, axis=1, keepdims=True)
                m_new = jnp.maximum(m_prev, s_top)
                factor = jnp.exp(m_prev - m_new)
                p = jnp.exp(s - m_new)
                if masked:
                    p = jnp.where(allowed, p, 0.0)
                l_ref[h] = l_ref[h] * factor + jnp.sum(p, axis=1, keepdims=True)
                acc_ref[h] = acc_ref[h] * factor + jnp.dot(
                    p.astype(jnp.bfloat16), v, preferred_element_type=jnp.float32
                )
                m_ref[h] = m_new

        whole = (block < meta_ref[0]) & (block * span >= meta_ref[2])

        @pl.when((block >= meta_ref[1]) & whole)
        def _():
            accumulate(False)

        @pl.when((block >= meta_ref[1]) & jnp.logical_not(whole))
        def _():
            accumulate(True)

        @pl.when(step == n_blocks - 1)
        def _():
            for h in range(n_heads):
                o_ref[:, h * head_width:(h + 1) * head_width] = (
                    acc_ref[h] / l_ref[h]
                ).astype(o_ref.dtype)

    grid_spec = pltpu.PrefetchScalarGridSpec(
        num_scalar_prefetch=1,
        grid=(n_blocks,),
        in_specs=[
            pl.BlockSpec((row_count, q_width), lambda step, meta_ref: (0, 0)),
            pl.BlockSpec((span, kv_width), kv_map),
            pl.BlockSpec((row_count, 1), lambda step, meta_ref: (0, 0)),
        ],
        out_specs=pl.BlockSpec((row_count, q_width), lambda step, meta_ref: (0, 0)),
        scratch_shapes=[
            pltpu.VMEM((n_heads, row_count, 1), jnp.float32),
            pltpu.VMEM((n_heads, row_count, 1), jnp.float32),
            pltpu.VMEM((n_heads, row_count, head_width), jnp.float32),
        ],
    )
    return pl.pallas_call(
        kernel,
        grid_spec=grid_spec,
        out_shape=jax.ShapeDtypeStruct((row_count, q_width), jnp.bfloat16),
        compiler_params=pltpu.CompilerParams(dimension_semantics=("arbitrary",)),
    )(meta, query_rows, key_block, seg)


def gather_tp(tokens):
    tp_size = lax.axis_size("tp")
    tp_rank = lax.axis_index("tp")
    rows = tokens.shape[0]
    gathered = jnp.zeros((tp_size * rows,) + tokens.shape[1:], tokens.dtype)
    gathered = lax.dynamic_update_slice_in_dim(gathered, tokens, tp_rank * rows, 0)
    for shift in range(1, tp_size):
        pairs = [(i, (i + shift) % tp_size) for i in range(tp_size)]
        got = lax.ppermute(tokens, "tp", pairs)
        source = (tp_rank - shift) % tp_size
        gathered = lax.dynamic_update_slice_in_dim(gathered, got, source * rows, 0)
    return gathered


def on_device(
    tokens,
    norm_gain,
    w_query,
    key_value_weight,
    query_gain,
    key_gain,
    lengths,
    segment_ids,
    req_counts,
    req_slots,
):
    tp_size = lax.axis_size("tp")
    tp_rank = lax.axis_index("tp")
    chunk_rows = tokens.shape[0]
    row_count = chunk_rows * tp_size
    seq_rank = lax.axis_index("seq")
    first_row = seq_rank * row_count
    query_index = first_row + jnp.arange(row_count, dtype=jnp.int32)
    segment_start = prompt_starts(segment_ids, lengths)
    positions = query_index - segment_start
    own_positions = lax.dynamic_slice_in_dim(positions, tp_rank * chunk_rows, chunk_rows, 0)
    own_q, own_kv = project(
        tokens, norm_gain, w_query, key_value_weight, query_gain, key_gain, own_positions
    )
    query_rows = jnp.zeros((row_count, own_q.shape[1]), own_q.dtype)
    key_value_rows = jnp.zeros((row_count, own_kv.shape[1]), own_kv.dtype)
    query_rows = lax.dynamic_update_slice_in_dim(query_rows, own_q, tp_rank * chunk_rows, 0)
    key_value_rows = lax.dynamic_update_slice_in_dim(
        key_value_rows, own_kv, tp_rank * chunk_rows, 0
    )
    for shift in range(1, tp_size):
        pairs = [(i, (i + shift) % tp_size) for i in range(tp_size)]
        got = lax.ppermute(tokens, "tp", pairs)
        place = ((tp_rank - shift) % tp_size) * chunk_rows
        got_q, got_kv = project(
            got, norm_gain, w_query, key_value_weight, query_gain, key_gain,
            lax.dynamic_slice_in_dim(positions, place, chunk_rows, 0),
        )
        query_rows = lax.dynamic_update_slice_in_dim(query_rows, got_q, place, 0)
        key_value_rows = lax.dynamic_update_slice_in_dim(key_value_rows, got_kv, place, 0)
    head_width = query_gain.shape[0]
    kv_heads = key_value_rows.shape[1] // (2 * head_width)
    query_heads = query_rows.reshape(row_count, kv_heads, 2, head_width)
    cache_rows = CACHE_DEV
    cache_index = seq_rank * cache_rows + jnp.arange(cache_rows, dtype=jnp.int32)
    source_row, source_live = sources(cache_index, lengths, req_counts, req_slots)

    key_block = lax.all_gather(key_value_rows, "seq", axis=0, tiled=True)
    first_block = jnp.min(segment_start) // row_count
    attended = flash_attention(
        query_rows, key_block, segment_start, seq_rank, first_block, head_width
    )
    picked = jnp.take(key_block, source_row, axis=0)
    cache = jnp.where(source_live[:, None], picked, jnp.zeros_like(picked))
    return (attended, cache)


def solution(mesh):
    placed = (
        P(("seq", "tp"), None),
        P(),
        P(None, "tp"),
        P(None, "tp"),
        P(),
        P(),
        P(),
        P("seq"),
        P(),
        P(),
    )
    return jax.shard_map(
        on_device,
        mesh=mesh,
        in_specs=placed,
        out_specs=(P("seq", "tp"), P("seq", "tp")),
        check_vma=False,
    )
```

```python
import math

import jax
import jax.numpy as jnp
from jax import lax
from jax.sharding import PartitionSpec as P
from jax.experimental import pallas as pl
from jax.experimental.pallas import tpu as pltpu

CACHE_DEV = 8192


rope_base = 1000000.0
query_scalar = 168.0
epsilon = 1e-06


def rms_scale(values, gains):
    return values * lax.rsqrt(jnp.mean(values * values, axis=-1, keepdims=True) + epsilon) * gains


def rope_table(positions, head_width):
    half_width = head_width // 2
    frequency = jnp.exp(
        jnp.arange(half_width, dtype=jnp.float32) * (-2.0 * math.log(rope_base) / head_width)
    )
    angles = positions.astype(jnp.float32)[:, None] * frequency[None, :]
    return (jnp.cos(angles), jnp.sin(angles))


def rotate_pairs(values, cosine, sine_table):
    half_width = values.shape[-1] // 2
    front_half = values[..., :half_width]
    back_half = values[..., half_width:]
    cos_part = cosine[:, None, :]
    sin_part = sine_table[:, None, :]
    return jnp.concatenate(
        [
            front_half * cos_part - back_half * sin_part,
            back_half * cos_part + front_half * sin_part,
        ],
        axis=-1,
    )


def project(tokens, norm_gain, w_query, key_value_weight, query_gain, key_gain, positions):
    token_count = tokens.shape[0]
    head_width = query_gain.shape[0]
    as_float = tokens.astype(jnp.float32)
    normed = rms_scale(as_float, norm_gain).astype(jnp.bfloat16)
    query_raw = jnp.dot(normed, w_query, preferred_element_type=jnp.float32)
    keyval_raw = jnp.dot(normed, key_value_weight, preferred_element_type=jnp.float32)
    cosine, sine_table = rope_table(positions, head_width)
    query_rows = rotate_pairs(
        rms_scale(query_raw.reshape(token_count, -1, head_width), query_gain), cosine, sine_table
    ) * query_scalar ** (-0.5)
    split_kv = keyval_raw.reshape(token_count, -1, 2, head_width)
    keys = rotate_pairs(rms_scale(split_kv[:, :, 0], key_gain), cosine, sine_table)
    key_value_rows = (
        jnp.stack([keys, split_kv[:, :, 1]], axis=2).reshape(token_count, -1).astype(jnp.bfloat16)
    )
    return (query_rows.reshape(token_count, -1).astype(jnp.bfloat16), key_value_rows)


def prompt_starts(segment_ids, lengths):
    starts = jnp.cumsum(lengths) - lengths
    prompt_ids = jnp.arange(lengths.shape[0], dtype=jnp.int32)
    chosen = jnp.where(segment_ids[:, None] == prompt_ids[None, :], starts[None, :], jnp.int32(0))
    return jnp.sum(chosen, axis=1)


def sources(cache_index, lengths, req_counts, req_slots):
    starts = jnp.cumsum(lengths) - lengths
    prompt_ids = jnp.arange(lengths.shape[0], dtype=jnp.int32)
    request_ids = jnp.arange(req_slots.shape[0], dtype=jnp.int32)
    request_ends = jnp.cumsum(req_counts)
    owner_prompt = jnp.sum(
        (request_ends[None, :] <= request_ids[:, None]).astype(jnp.int32), axis=1
    )
    matches = owner_prompt[:, None] == prompt_ids[None, :]
    request_length = jnp.sum(jnp.where(matches, lengths[None, :], jnp.int32(0)), axis=1)
    request_start = jnp.sum(jnp.where(matches, starts[None, :], jnp.int32(0)), axis=1)
    inside = (cache_index[:, None] >= req_slots[None, :]) & (
        cache_index[:, None] < req_slots[None, :] + request_length[None, :]
    )
    offsets = request_start[None, :] + cache_index[:, None] - req_slots[None, :]
    source_row = jnp.sum(jnp.where(inside, offsets, jnp.int32(0)), axis=1)
    source_live = jnp.max(inside.astype(jnp.int32), axis=1) > 0
    return (source_row, source_live)


def flash_attention(query_rows, key_block, segment_start, meta, head_width, n_steps, state):
    row_count, q_width = query_rows.shape
    key_count, kv_width = key_block.shape
    n_heads = q_width // head_width
    group = n_heads // (kv_width // (2 * head_width))
    span = row_count
    seg = segment_start.reshape(row_count, 1).astype(jnp.int32)

    def kv_map(step, meta_ref):
        return (jnp.maximum(meta_ref[4] - step, meta_ref[1]) - meta_ref[3], 0)

    def kernel(meta_ref, q_ref, kv_ref, seg_ref, m_in, l_in, acc_in, o_ref, m_ref, l_ref, acc_ref):
        step = pl.program_id(0)
        block = meta_ref[4] - step

        @pl.when(step == 0)
        def _():
            m_ref[...] = m_in[...]
            l_ref[...] = l_in[...]
            acc_ref[...] = acc_in[...]

        def accumulate(masked):
            if masked:
                key_index = block * span + lax.broadcasted_iota(jnp.int32, (1, span), 1)
                query_index = meta_ref[0] * span + lax.broadcasted_iota(
                    jnp.int32, (row_count, 1), 0
                )
                allowed = (key_index >= seg_ref[...]) & (key_index <= query_index)
            for h in range(n_heads):
                g = h // group
                q = q_ref[:, h * head_width:(h + 1) * head_width]
                k = kv_ref[:, 2 * g * head_width:(2 * g + 1) * head_width]
                v = kv_ref[:, (2 * g + 1) * head_width:(2 * g + 2) * head_width]
                s = lax.dot_general(
                    q, k, (((1,), (1,)), ((), ())), preferred_element_type=jnp.float32
                )
                m_prev = m_ref[h]
                if masked:
                    s_top = jnp.max(jnp.where(allowed, s, -1e30), axis=1, keepdims=True)
                else:
                    s_top = jnp.max(s, axis=1, keepdims=True)
                m_new = jnp.maximum(m_prev, s_top)
                factor = jnp.exp(m_prev - m_new)
                p = jnp.exp(s - m_new)
                if masked:
                    p = jnp.where(allowed, p, 0.0)
                l_ref[h] = l_ref[h] * factor + jnp.sum(p, axis=1, keepdims=True)
                acc_ref[h] = acc_ref[h] * factor + jnp.dot(
                    p.astype(jnp.bfloat16), v, preferred_element_type=jnp.float32
                )
                m_ref[h] = m_new

        whole = (block < meta_ref[0]) & (block * span >= meta_ref[2])
        active = block >= meta_ref[1]

        if n_steps > 1:

            @pl.when(active & whole)
            def _():
                accumulate(False)

            @pl.when(active & jnp.logical_not(whole))
            def _():
                accumulate(True)

        else:

            @pl.when(active)
            def _():
                accumulate(True)

        @pl.when(step == n_steps - 1)
        def _():
            for h in range(n_heads):
                o_ref[:, h * head_width:(h + 1) * head_width] = (
                    acc_ref[h] / l_ref[h]
                ).astype(o_ref.dtype)

    stat_shape = (n_heads, row_count, 1)
    acc_shape = (n_heads, row_count, head_width)
    if state is None:
        state = (
            jnp.full(stat_shape, -1e30, jnp.float32),
            jnp.zeros(stat_shape, jnp.float32),
            jnp.zeros(acc_shape, jnp.float32),
        )
    fixed = lambda step, meta_ref: (0, 0)
    fixed3 = lambda step, meta_ref: (0, 0, 0)
    grid_spec = pltpu.PrefetchScalarGridSpec(
        num_scalar_prefetch=1,
        grid=(n_steps,),
        in_specs=[
            pl.BlockSpec((row_count, q_width), fixed),
            pl.BlockSpec((span, kv_width), kv_map),
            pl.BlockSpec((row_count, 1), fixed),
            pl.BlockSpec(stat_shape, fixed3),
            pl.BlockSpec(stat_shape, fixed3),
            pl.BlockSpec(acc_shape, fixed3),
        ],
        out_specs=[
            pl.BlockSpec((row_count, q_width), fixed),
            pl.BlockSpec(stat_shape, fixed3),
            pl.BlockSpec(stat_shape, fixed3),
            pl.BlockSpec(acc_shape, fixed3),
        ],
    )
    out, m_out, l_out, acc_out = pl.pallas_call(
        kernel,
        grid_spec=grid_spec,
        out_shape=[
            jax.ShapeDtypeStruct((row_count, q_width), jnp.bfloat16),
            jax.ShapeDtypeStruct(stat_shape, jnp.float32),
            jax.ShapeDtypeStruct(stat_shape, jnp.float32),
            jax.ShapeDtypeStruct(acc_shape, jnp.float32),
        ],
        compiler_params=pltpu.CompilerParams(dimension_semantics=("arbitrary",)),
    )(meta, query_rows, key_block, seg, *state)
    return out, (m_out, l_out, acc_out)


def gather_tp(tokens):
    tp_size = lax.axis_size("tp")
    tp_rank = lax.axis_index("tp")
    rows = tokens.shape[0]
    gathered = jnp.zeros((tp_size * rows,) + tokens.shape[1:], tokens.dtype)
    gathered = lax.dynamic_update_slice_in_dim(gathered, tokens, tp_rank * rows, 0)
    for shift in range(1, tp_size):
        pairs = [(i, (i + shift) % tp_size) for i in range(tp_size)]
        got = lax.ppermute(tokens, "tp", pairs)
        source = (tp_rank - shift) % tp_size
        gathered = lax.dynamic_update_slice_in_dim(gathered, got, source * rows, 0)
    return gathered


def on_device(
    tokens,
    norm_gain,
    w_query,
    key_value_weight,
    query_gain,
    key_gain,
    lengths,
    segment_ids,
    req_counts,
    req_slots,
):
    tp_size = lax.axis_size("tp")
    tp_rank = lax.axis_index("tp")
    chunk_rows = tokens.shape[0]
    row_count = chunk_rows * tp_size
    seq_rank = lax.axis_index("seq")
    first_row = seq_rank * row_count
    query_index = first_row + jnp.arange(row_count, dtype=jnp.int32)
    segment_start = prompt_starts(segment_ids, lengths)
    positions = query_index - segment_start
    own_positions = lax.dynamic_slice_in_dim(positions, tp_rank * chunk_rows, chunk_rows, 0)
    own_q, own_kv = project(
        tokens, norm_gain, w_query, key_value_weight, query_gain, key_gain, own_positions
    )
    query_rows = jnp.zeros((row_count, own_q.shape[1]), own_q.dtype)
    key_value_rows = jnp.zeros((row_count, own_kv.shape[1]), own_kv.dtype)
    query_rows = lax.dynamic_update_slice_in_dim(query_rows, own_q, tp_rank * chunk_rows, 0)
    key_value_rows = lax.dynamic_update_slice_in_dim(
        key_value_rows, own_kv, tp_rank * chunk_rows, 0
    )
    for shift in range(1, tp_size):
        pairs = [(i, (i + shift) % tp_size) for i in range(tp_size)]
        got = lax.ppermute(tokens, "tp", pairs)
        place = ((tp_rank - shift) % tp_size) * chunk_rows
        got_q, got_kv = project(
            got, norm_gain, w_query, key_value_weight, query_gain, key_gain,
            lax.dynamic_slice_in_dim(positions, place, chunk_rows, 0),
        )
        query_rows = lax.dynamic_update_slice_in_dim(query_rows, got_q, place, 0)
        key_value_rows = lax.dynamic_update_slice_in_dim(key_value_rows, got_kv, place, 0)
    head_width = query_gain.shape[0]
    kv_heads = key_value_rows.shape[1] // (2 * head_width)
    query_heads = query_rows.reshape(row_count, kv_heads, 2, head_width)
    cache_rows = CACHE_DEV
    cache_index = seq_rank * cache_rows + jnp.arange(cache_rows, dtype=jnp.int32)
    source_row, source_live = sources(cache_index, lengths, req_counts, req_slots)

    first_block = jnp.min(segment_start) // row_count
    last_start = jnp.max(segment_start)
    diagonal_meta = jnp.stack([seq_rank, seq_rank, last_start, seq_rank, seq_rank])
    diagonal_meta = diagonal_meta.astype(jnp.int32)
    _, state = flash_attention(
        query_rows, key_value_rows, segment_start, diagonal_meta, head_width, 1, None
    )
    key_block = lax.all_gather(key_value_rows, "seq", axis=0, tiled=True)
    key_count = key_block.shape[0]
    n_steps = max(1, min(key_count // row_count - 1, key_count // (2 * row_count)))
    main_meta = jnp.stack([seq_rank, first_block, last_start, 0, seq_rank - 1]).astype(jnp.int32)
    attended, _ = flash_attention(
        query_rows, key_block, segment_start, main_meta, head_width, n_steps, state
    )
    picked = jnp.take(key_block, source_row, axis=0)
    cache = jnp.where(source_live[:, None], picked, jnp.zeros_like(picked))
    return (attended, cache)


def solution(mesh):
    placed = (
        P(("seq", "tp"), None),
        P(),
        P(None, "tp"),
        P(None, "tp"),
        P(),
        P(),
        P(),
        P("seq"),
        P(),
        P(),
    )
    return jax.shard_map(
        on_device,
        mesh=mesh,
        in_specs=placed,
        out_specs=(P("seq", "tp"), P("seq", "tp")),
        check_vma=False,
    )
```

```python
import math

import jax
import jax.numpy as jnp
from jax import lax
from jax.sharding import PartitionSpec as P
from jax.experimental import pallas as pl
from jax.experimental.pallas import tpu as pltpu

CACHE_DEV = 8192


rope_base = 1000000.0
query_scalar = 168.0
epsilon = 1e-06


def rms_scale(values, gains):
    return values * lax.rsqrt(jnp.mean(values * values, axis=-1, keepdims=True) + epsilon) * gains


def rope_table(positions, head_width):
    half_width = head_width // 2
    frequency = jnp.exp(
        jnp.arange(half_width, dtype=jnp.float32) * (-2.0 * math.log(rope_base) / head_width)
    )
    angles = positions.astype(jnp.float32)[:, None] * frequency[None, :]
    return (jnp.cos(angles), jnp.sin(angles))


def rotate_pairs(values, cosine, sine_table):
    half_width = values.shape[-1] // 2
    front_half = values[..., :half_width]
    back_half = values[..., half_width:]
    cos_part = cosine[:, None, :]
    sin_part = sine_table[:, None, :]
    return jnp.concatenate(
        [
            front_half * cos_part - back_half * sin_part,
            back_half * cos_part + front_half * sin_part,
        ],
        axis=-1,
    )


def project(tokens, norm_gain, w_query, key_value_weight, query_gain, key_gain, positions):
    token_count = tokens.shape[0]
    head_width = query_gain.shape[0]
    as_float = tokens.astype(jnp.float32)
    normed = rms_scale(as_float, norm_gain).astype(jnp.bfloat16)
    query_raw = jnp.dot(normed, w_query, preferred_element_type=jnp.float32)
    keyval_raw = jnp.dot(normed, key_value_weight, preferred_element_type=jnp.float32)
    cosine, sine_table = rope_table(positions, head_width)
    query_rows = rotate_pairs(
        rms_scale(query_raw.reshape(token_count, -1, head_width), query_gain), cosine, sine_table
    ) * query_scalar ** (-0.5)
    split_kv = keyval_raw.reshape(token_count, -1, 2, head_width)
    keys = rotate_pairs(rms_scale(split_kv[:, :, 0], key_gain), cosine, sine_table)
    key_value_rows = (
        jnp.stack([keys, split_kv[:, :, 1]], axis=2).reshape(token_count, -1).astype(jnp.bfloat16)
    )
    return (query_rows.reshape(token_count, -1).astype(jnp.bfloat16), key_value_rows)


def prompt_starts(segment_ids, lengths):
    starts = jnp.cumsum(lengths) - lengths
    prompt_ids = jnp.arange(lengths.shape[0], dtype=jnp.int32)
    chosen = jnp.where(segment_ids[:, None] == prompt_ids[None, :], starts[None, :], jnp.int32(0))
    return jnp.sum(chosen, axis=1)


def sources(cache_index, lengths, req_counts, req_slots):
    starts = jnp.cumsum(lengths) - lengths
    prompt_ids = jnp.arange(lengths.shape[0], dtype=jnp.int32)
    request_ids = jnp.arange(req_slots.shape[0], dtype=jnp.int32)
    request_ends = jnp.cumsum(req_counts)
    owner_prompt = jnp.sum(
        (request_ends[None, :] <= request_ids[:, None]).astype(jnp.int32), axis=1
    )
    matches = owner_prompt[:, None] == prompt_ids[None, :]
    request_length = jnp.sum(jnp.where(matches, lengths[None, :], jnp.int32(0)), axis=1)
    request_start = jnp.sum(jnp.where(matches, starts[None, :], jnp.int32(0)), axis=1)
    inside = (cache_index[:, None] >= req_slots[None, :]) & (
        cache_index[:, None] < req_slots[None, :] + request_length[None, :]
    )
    offsets = request_start[None, :] + cache_index[:, None] - req_slots[None, :]
    source_row = jnp.sum(jnp.where(inside, offsets, jnp.int32(0)), axis=1)
    source_live = jnp.max(inside.astype(jnp.int32), axis=1) > 0
    return (source_row, source_live)


def flash_attention(query_rows, key_block, segment_start, meta, head_width, n_steps, state):
    row_count, q_width = query_rows.shape
    key_count, kv_width = key_block.shape
    n_heads = q_width // head_width
    group = n_heads // (kv_width // (2 * head_width))
    span = row_count
    seg = segment_start.reshape(row_count, 1).astype(jnp.int32)

    def kv_map(step, meta_ref):
        return (jnp.maximum(meta_ref[4] - step, meta_ref[1]) - meta_ref[3], 0)

    def kernel(meta_ref, q_ref, kv_ref, seg_ref, m_in, l_in, acc_in, o_ref, m_ref, l_ref, acc_ref):
        step = pl.program_id(0)
        block = meta_ref[4] - step

        @pl.when(step == 0)
        def _():
            m_ref[...] = m_in[...]
            l_ref[...] = l_in[...]
            acc_ref[...] = acc_in[...]

        def accumulate(masked):
            if masked:
                key_index = block * span + lax.broadcasted_iota(jnp.int32, (1, span), 1)
                query_index = meta_ref[0] * span + lax.broadcasted_iota(
                    jnp.int32, (row_count, 1), 0
                )
                allowed = (key_index >= seg_ref[...]) & (key_index <= query_index)
            for h in range(n_heads):
                g = h // group
                q = q_ref[:, h * head_width:(h + 1) * head_width]
                k = kv_ref[:, 2 * g * head_width:(2 * g + 1) * head_width]
                v = kv_ref[:, (2 * g + 1) * head_width:(2 * g + 2) * head_width]
                s = lax.dot_general(
                    q, k, (((1,), (1,)), ((), ())), preferred_element_type=jnp.float32
                )
                m_prev = m_ref[h]
                if masked:
                    s_top = jnp.max(jnp.where(allowed, s, -1e30), axis=1, keepdims=True)
                else:
                    s_top = jnp.max(s, axis=1, keepdims=True)
                m_new = jnp.maximum(m_prev, s_top)
                factor = jnp.exp(m_prev - m_new)
                p = jnp.exp(s - m_new)
                if masked:
                    p = jnp.where(allowed, p, 0.0)
                both = jnp.dot(
                    p.astype(jnp.bfloat16),
                    jnp.concatenate([v, jnp.ones_like(v)], axis=1),
                    preferred_element_type=jnp.float32,
                )
                l_ref[h] = l_ref[h] * factor + both[:, head_width:head_width + 1]
                acc_ref[h] = acc_ref[h] * factor + both[:, :head_width]
                m_ref[h] = m_new

        active = block >= meta_ref[1]

        @pl.when(active)
        def _():
            accumulate(True)

        @pl.when(step == n_steps - 1)
        def _():
            for h in range(n_heads):
                o_ref[:, h * head_width:(h + 1) * head_width] = (
                    acc_ref[h] / l_ref[h]
                ).astype(o_ref.dtype)

    stat_shape = (n_heads, row_count, 1)
    acc_shape = (n_heads, row_count, head_width)
    if state is None:
        state = (
            jnp.full(stat_shape, -1e30, jnp.float32),
            jnp.zeros(stat_shape, jnp.float32),
            jnp.zeros(acc_shape, jnp.float32),
        )
    fixed = lambda step, meta_ref: (0, 0)
    fixed3 = lambda step, meta_ref: (0, 0, 0)
    grid_spec = pltpu.PrefetchScalarGridSpec(
        num_scalar_prefetch=1,
        grid=(n_steps,),
        in_specs=[
            pl.BlockSpec((row_count, q_width), fixed),
            pl.BlockSpec((span, kv_width), kv_map),
            pl.BlockSpec((row_count, 1), fixed),
            pl.BlockSpec(stat_shape, fixed3),
            pl.BlockSpec(stat_shape, fixed3),
            pl.BlockSpec(acc_shape, fixed3),
        ],
        out_specs=[
            pl.BlockSpec((row_count, q_width), fixed),
            pl.BlockSpec(stat_shape, fixed3),
            pl.BlockSpec(stat_shape, fixed3),
            pl.BlockSpec(acc_shape, fixed3),
        ],
    )
    out, m_out, l_out, acc_out = pl.pallas_call(
        kernel,
        grid_spec=grid_spec,
        out_shape=[
            jax.ShapeDtypeStruct((row_count, q_width), jnp.bfloat16),
            jax.ShapeDtypeStruct(stat_shape, jnp.float32),
            jax.ShapeDtypeStruct(stat_shape, jnp.float32),
            jax.ShapeDtypeStruct(acc_shape, jnp.float32),
        ],
        compiler_params=pltpu.CompilerParams(dimension_semantics=("arbitrary",)),
    )(meta, query_rows, key_block, seg, *state)
    return out, (m_out, l_out, acc_out)


def gather_tp(tokens):
    tp_size = lax.axis_size("tp")
    tp_rank = lax.axis_index("tp")
    rows = tokens.shape[0]
    gathered = jnp.zeros((tp_size * rows,) + tokens.shape[1:], tokens.dtype)
    gathered = lax.dynamic_update_slice_in_dim(gathered, tokens, tp_rank * rows, 0)
    for shift in range(1, tp_size):
        pairs = [(i, (i + shift) % tp_size) for i in range(tp_size)]
        got = lax.ppermute(tokens, "tp", pairs)
        source = (tp_rank - shift) % tp_size
        gathered = lax.dynamic_update_slice_in_dim(gathered, got, source * rows, 0)
    return gathered


def on_device(
    tokens,
    norm_gain,
    w_query,
    key_value_weight,
    query_gain,
    key_gain,
    lengths,
    segment_ids,
    req_counts,
    req_slots,
):
    tp_size = lax.axis_size("tp")
    tp_rank = lax.axis_index("tp")
    chunk_rows = tokens.shape[0]
    row_count = chunk_rows * tp_size
    seq_rank = lax.axis_index("seq")
    first_row = seq_rank * row_count
    query_index = first_row + jnp.arange(row_count, dtype=jnp.int32)
    segment_start = prompt_starts(segment_ids, lengths)
    positions = query_index - segment_start
    own_positions = lax.dynamic_slice_in_dim(positions, tp_rank * chunk_rows, chunk_rows, 0)
    own_q, own_kv = project(
        tokens, norm_gain, w_query, key_value_weight, query_gain, key_gain, own_positions
    )
    query_rows = jnp.zeros((row_count, own_q.shape[1]), own_q.dtype)
    key_value_rows = jnp.zeros((row_count, own_kv.shape[1]), own_kv.dtype)
    query_rows = lax.dynamic_update_slice_in_dim(query_rows, own_q, tp_rank * chunk_rows, 0)
    key_value_rows = lax.dynamic_update_slice_in_dim(
        key_value_rows, own_kv, tp_rank * chunk_rows, 0
    )
    for shift in range(1, tp_size):
        pairs = [(i, (i + shift) % tp_size) for i in range(tp_size)]
        got = lax.ppermute(tokens, "tp", pairs)
        place = ((tp_rank - shift) % tp_size) * chunk_rows
        got_q, got_kv = project(
            got, norm_gain, w_query, key_value_weight, query_gain, key_gain,
            lax.dynamic_slice_in_dim(positions, place, chunk_rows, 0),
        )
        query_rows = lax.dynamic_update_slice_in_dim(query_rows, got_q, place, 0)
        key_value_rows = lax.dynamic_update_slice_in_dim(key_value_rows, got_kv, place, 0)
    head_width = query_gain.shape[0]
    kv_heads = key_value_rows.shape[1] // (2 * head_width)
    query_heads = query_rows.reshape(row_count, kv_heads, 2, head_width)
    cache_rows = CACHE_DEV
    cache_index = seq_rank * cache_rows + jnp.arange(cache_rows, dtype=jnp.int32)
    source_row, source_live = sources(cache_index, lengths, req_counts, req_slots)

    first_block = jnp.min(segment_start) // row_count
    last_start = jnp.max(segment_start)
    diagonal_meta = jnp.stack([seq_rank, seq_rank, last_start, seq_rank, seq_rank])
    diagonal_meta = diagonal_meta.astype(jnp.int32)
    _, state = flash_attention(
        query_rows, key_value_rows, segment_start, diagonal_meta, head_width, 1, None
    )
    key_block = lax.all_gather(key_value_rows, "seq", axis=0, tiled=True)
    key_count = key_block.shape[0]
    n_steps = max(1, min(key_count // row_count - 1, key_count // (2 * row_count)))
    main_meta = jnp.stack([seq_rank, first_block, last_start, 0, seq_rank - 1]).astype(jnp.int32)
    attended, _ = flash_attention(
        query_rows, key_block, segment_start, main_meta, head_width, n_steps, state
    )
    picked = jnp.take(key_block, source_row, axis=0)
    cache = jnp.where(source_live[:, None], picked, jnp.zeros_like(picked))
    return (attended, cache)


def solution(mesh):
    placed = (
        P(("seq", "tp"), None),
        P(),
        P(None, "tp"),
        P(None, "tp"),
        P(),
        P(),
        P(),
        P("seq"),
        P(),
        P(),
    )
    return jax.shard_map(
        on_device,
        mesh=mesh,
        in_specs=placed,
        out_specs=(P("seq", "tp"), P("seq", "tp")),
        check_vma=False,
    )
```

```python
import math

import jax
import jax.numpy as jnp
from jax import lax
from jax.sharding import PartitionSpec as P
from jax.experimental import pallas as pl
from jax.experimental.pallas import tpu as pltpu

CACHE_DEV = 8192


rope_base = 1000000.0
query_scalar = 168.0
epsilon = 1e-06


def rms_scale(values, gains):
    return values * lax.rsqrt(jnp.mean(values * values, axis=-1, keepdims=True) + epsilon) * gains


def rope_table(positions, head_width):
    half_width = head_width // 2
    frequency = jnp.exp(
        jnp.arange(half_width, dtype=jnp.float32) * (-2.0 * math.log(rope_base) / head_width)
    )
    angles = positions.astype(jnp.float32)[:, None] * frequency[None, :]
    return (jnp.cos(angles), jnp.sin(angles))


def rotate_pairs(values, cosine, sine_table):
    half_width = values.shape[-1] // 2
    front_half = values[..., :half_width]
    back_half = values[..., half_width:]
    cos_part = cosine[:, None, :]
    sin_part = sine_table[:, None, :]
    return jnp.concatenate(
        [
            front_half * cos_part - back_half * sin_part,
            back_half * cos_part + front_half * sin_part,
        ],
        axis=-1,
    )


def project(tokens, norm_gain, w_query, key_value_weight, query_gain, key_gain, positions):
    token_count = tokens.shape[0]
    head_width = query_gain.shape[0]
    as_float = tokens.astype(jnp.float32)
    normed = rms_scale(as_float, norm_gain).astype(jnp.bfloat16)
    query_raw = jnp.dot(normed, w_query, preferred_element_type=jnp.float32)
    keyval_raw = jnp.dot(normed, key_value_weight, preferred_element_type=jnp.float32)
    cosine, sine_table = rope_table(positions, head_width)
    query_rows = rotate_pairs(
        rms_scale(query_raw.reshape(token_count, -1, head_width), query_gain), cosine, sine_table
    ) * query_scalar ** (-0.5)
    split_kv = keyval_raw.reshape(token_count, -1, 2, head_width)
    keys = rotate_pairs(rms_scale(split_kv[:, :, 0], key_gain), cosine, sine_table)
    key_value_rows = (
        jnp.stack([keys, split_kv[:, :, 1]], axis=2).reshape(token_count, -1).astype(jnp.bfloat16)
    )
    return (query_rows.reshape(token_count, -1).astype(jnp.bfloat16), key_value_rows)


def prompt_starts(segment_ids, lengths):
    starts = jnp.cumsum(lengths) - lengths
    prompt_ids = jnp.arange(lengths.shape[0], dtype=jnp.int32)
    chosen = jnp.where(segment_ids[:, None] == prompt_ids[None, :], starts[None, :], jnp.int32(0))
    return jnp.sum(chosen, axis=1)


def sources(cache_index, lengths, req_counts, req_slots):
    starts = jnp.cumsum(lengths) - lengths
    prompt_ids = jnp.arange(lengths.shape[0], dtype=jnp.int32)
    request_ids = jnp.arange(req_slots.shape[0], dtype=jnp.int32)
    request_ends = jnp.cumsum(req_counts)
    owner_prompt = jnp.sum(
        (request_ends[None, :] <= request_ids[:, None]).astype(jnp.int32), axis=1
    )
    matches = owner_prompt[:, None] == prompt_ids[None, :]
    request_length = jnp.sum(jnp.where(matches, lengths[None, :], jnp.int32(0)), axis=1)
    request_start = jnp.sum(jnp.where(matches, starts[None, :], jnp.int32(0)), axis=1)
    inside = (cache_index[:, None] >= req_slots[None, :]) & (
        cache_index[:, None] < req_slots[None, :] + request_length[None, :]
    )
    offsets = request_start[None, :] + cache_index[:, None] - req_slots[None, :]
    source_row = jnp.sum(jnp.where(inside, offsets, jnp.int32(0)), axis=1)
    source_live = jnp.max(inside.astype(jnp.int32), axis=1) > 0
    return (source_row, source_live)


def flash_attention(query_rows, key_block, segment_start, meta, head_width, n_steps, state):
    row_count, q_width = query_rows.shape
    key_count, kv_width = key_block.shape
    n_heads = q_width // head_width
    group = n_heads // (kv_width // (2 * head_width))
    span = row_count
    seg = segment_start.reshape(row_count, 1).astype(jnp.int32)

    def kv_map(step, meta_ref):
        return (jnp.maximum(meta_ref[4] - step, meta_ref[1]) - meta_ref[3], 0)

    def kernel(meta_ref, q_ref, kv_ref, seg_ref, m_in, l_in, acc_in, o_ref, m_ref, l_ref, acc_ref):
        step = pl.program_id(0)
        block = meta_ref[4] - step

        @pl.when(step == 0)
        def _():
            m_ref[...] = m_in[...]
            l_ref[...] = l_in[...]
            acc_ref[...] = acc_in[...]

        def accumulate(masked):
            if masked:
                key_index = block * span + lax.broadcasted_iota(jnp.int32, (1, span), 1)
                query_index = meta_ref[0] * span + lax.broadcasted_iota(
                    jnp.int32, (row_count, 1), 0
                )
                allowed = (key_index >= seg_ref[...]) & (key_index <= query_index)
            for h in range(n_heads):
                g = h // group
                q = q_ref[:, h * head_width:(h + 1) * head_width]
                k = kv_ref[:, 2 * g * head_width:(2 * g + 1) * head_width]
                v = kv_ref[:, (2 * g + 1) * head_width:(2 * g + 2) * head_width]
                s = lax.dot_general(
                    q, k, (((1,), (1,)), ((), ())), preferred_element_type=jnp.float32
                )
                m_prev = m_ref[h]
                s_masked = jnp.where(allowed, s, -1e30) if masked else s
                lanes = s_masked[:, 0:128]
                for c in range(1, span // 128):
                    lanes = jnp.maximum(lanes, s_masked[:, c * 128:(c + 1) * 128])
                s_top = jnp.max(lanes, axis=1, keepdims=True)
                m_new = jnp.maximum(m_prev, s_top)
                factor = jnp.exp(m_prev - m_new)
                p = jnp.exp(s - m_new)
                if masked:
                    p = jnp.where(allowed, p, 0.0)
                both = jnp.dot(
                    p.astype(jnp.bfloat16),
                    jnp.concatenate([v, jnp.ones_like(v)], axis=1),
                    preferred_element_type=jnp.float32,
                )
                l_ref[h] = l_ref[h] * factor + both[:, head_width:head_width + 1]
                acc_ref[h] = acc_ref[h] * factor + both[:, :head_width]
                m_ref[h] = m_new

        active = block >= meta_ref[1]

        @pl.when(active)
        def _():
            accumulate(True)

        @pl.when(step == n_steps - 1)
        def _():
            for h in range(n_heads):
                o_ref[:, h * head_width:(h + 1) * head_width] = (
                    acc_ref[h] / l_ref[h]
                ).astype(o_ref.dtype)

    stat_shape = (n_heads, row_count, 1)
    acc_shape = (n_heads, row_count, head_width)
    if state is None:
        state = (
            jnp.full(stat_shape, -1e30, jnp.float32),
            jnp.zeros(stat_shape, jnp.float32),
            jnp.zeros(acc_shape, jnp.float32),
        )
    fixed = lambda step, meta_ref: (0, 0)
    fixed3 = lambda step, meta_ref: (0, 0, 0)
    grid_spec = pltpu.PrefetchScalarGridSpec(
        num_scalar_prefetch=1,
        grid=(n_steps,),
        in_specs=[
            pl.BlockSpec((row_count, q_width), fixed),
            pl.BlockSpec((span, kv_width), kv_map),
            pl.BlockSpec((row_count, 1), fixed),
            pl.BlockSpec(stat_shape, fixed3),
            pl.BlockSpec(stat_shape, fixed3),
            pl.BlockSpec(acc_shape, fixed3),
        ],
        out_specs=[
            pl.BlockSpec((row_count, q_width), fixed),
            pl.BlockSpec(stat_shape, fixed3),
            pl.BlockSpec(stat_shape, fixed3),
            pl.BlockSpec(acc_shape, fixed3),
        ],
    )
    out, m_out, l_out, acc_out = pl.pallas_call(
        kernel,
        grid_spec=grid_spec,
        out_shape=[
            jax.ShapeDtypeStruct((row_count, q_width), jnp.bfloat16),
            jax.ShapeDtypeStruct(stat_shape, jnp.float32),
            jax.ShapeDtypeStruct(stat_shape, jnp.float32),
            jax.ShapeDtypeStruct(acc_shape, jnp.float32),
        ],
        compiler_params=pltpu.CompilerParams(dimension_semantics=("arbitrary",)),
    )(meta, query_rows, key_block, seg, *state)
    return out, (m_out, l_out, acc_out)


def gather_tp(tokens):
    tp_size = lax.axis_size("tp")
    tp_rank = lax.axis_index("tp")
    rows = tokens.shape[0]
    gathered = jnp.zeros((tp_size * rows,) + tokens.shape[1:], tokens.dtype)
    gathered = lax.dynamic_update_slice_in_dim(gathered, tokens, tp_rank * rows, 0)
    for shift in range(1, tp_size):
        pairs = [(i, (i + shift) % tp_size) for i in range(tp_size)]
        got = lax.ppermute(tokens, "tp", pairs)
        source = (tp_rank - shift) % tp_size
        gathered = lax.dynamic_update_slice_in_dim(gathered, got, source * rows, 0)
    return gathered


def on_device(
    tokens,
    norm_gain,
    w_query,
    key_value_weight,
    query_gain,
    key_gain,
    lengths,
    segment_ids,
    req_counts,
    req_slots,
):
    tp_size = lax.axis_size("tp")
    tp_rank = lax.axis_index("tp")
    chunk_rows = tokens.shape[0]
    row_count = chunk_rows * tp_size
    seq_rank = lax.axis_index("seq")
    first_row = seq_rank * row_count
    query_index = first_row + jnp.arange(row_count, dtype=jnp.int32)
    segment_start = prompt_starts(segment_ids, lengths)
    positions = query_index - segment_start
    own_positions = lax.dynamic_slice_in_dim(positions, tp_rank * chunk_rows, chunk_rows, 0)
    own_q, own_kv = project(
        tokens, norm_gain, w_query, key_value_weight, query_gain, key_gain, own_positions
    )
    query_rows = jnp.zeros((row_count, own_q.shape[1]), own_q.dtype)
    key_value_rows = jnp.zeros((row_count, own_kv.shape[1]), own_kv.dtype)
    query_rows = lax.dynamic_update_slice_in_dim(query_rows, own_q, tp_rank * chunk_rows, 0)
    key_value_rows = lax.dynamic_update_slice_in_dim(
        key_value_rows, own_kv, tp_rank * chunk_rows, 0
    )
    for shift in range(1, tp_size):
        pairs = [(i, (i + shift) % tp_size) for i in range(tp_size)]
        got = lax.ppermute(tokens, "tp", pairs)
        place = ((tp_rank - shift) % tp_size) * chunk_rows
        got_q, got_kv = project(
            got, norm_gain, w_query, key_value_weight, query_gain, key_gain,
            lax.dynamic_slice_in_dim(positions, place, chunk_rows, 0),
        )
        query_rows = lax.dynamic_update_slice_in_dim(query_rows, got_q, place, 0)
        key_value_rows = lax.dynamic_update_slice_in_dim(key_value_rows, got_kv, place, 0)
    head_width = query_gain.shape[0]
    kv_heads = key_value_rows.shape[1] // (2 * head_width)
    query_heads = query_rows.reshape(row_count, kv_heads, 2, head_width)
    cache_rows = CACHE_DEV
    cache_index = seq_rank * cache_rows + jnp.arange(cache_rows, dtype=jnp.int32)
    source_row, source_live = sources(cache_index, lengths, req_counts, req_slots)

    first_block = jnp.min(segment_start) // row_count
    last_start = jnp.max(segment_start)
    diagonal_meta = jnp.stack([seq_rank, seq_rank, last_start, seq_rank, seq_rank])
    diagonal_meta = diagonal_meta.astype(jnp.int32)
    _, state = flash_attention(
        query_rows, key_value_rows, segment_start, diagonal_meta, head_width, 1, None
    )
    key_block = lax.all_gather(key_value_rows, "seq", axis=0, tiled=True)
    key_count = key_block.shape[0]
    n_steps = max(1, min(key_count // row_count - 1, key_count // (2 * row_count)))
    main_meta = jnp.stack([seq_rank, first_block, last_start, 0, seq_rank - 1]).astype(jnp.int32)
    attended, _ = flash_attention(
        query_rows, key_block, segment_start, main_meta, head_width, n_steps, state
    )
    picked = jnp.take(key_block, source_row, axis=0)
    cache = jnp.where(source_live[:, None], picked, jnp.zeros_like(picked))
    return (attended, cache)


def solution(mesh):
    placed = (
        P(("seq", "tp"), None),
        P(),
        P(None, "tp"),
        P(None, "tp"),
        P(),
        P(),
        P(),
        P("seq"),
        P(),
        P(),
    )
    return jax.shard_map(
        on_device,
        mesh=mesh,
        in_specs=placed,
        out_specs=(P("seq", "tp"), P("seq", "tp")),
        check_vma=False,
    )
```

```python
import math

import jax
import jax.numpy as jnp
from jax import lax
from jax.sharding import PartitionSpec as P
from jax.experimental import pallas as pl
from jax.experimental.pallas import tpu as pltpu

CACHE_DEV = 8192


rope_base = 1000000.0
query_scalar = 168.0
epsilon = 1e-06


def rms_scale(values, gains):
    return values * lax.rsqrt(jnp.mean(values * values, axis=-1, keepdims=True) + epsilon) * gains


def rope_table(positions, head_width):
    half_width = head_width // 2
    frequency = jnp.exp(
        jnp.arange(half_width, dtype=jnp.float32) * (-2.0 * math.log(rope_base) / head_width)
    )
    angles = positions.astype(jnp.float32)[:, None] * frequency[None, :]
    return (jnp.cos(angles), jnp.sin(angles))


def rotate_pairs(values, cosine, sine_table):
    half_width = values.shape[-1] // 2
    front_half = values[..., :half_width]
    back_half = values[..., half_width:]
    cos_part = cosine[:, None, :]
    sin_part = sine_table[:, None, :]
    return jnp.concatenate(
        [
            front_half * cos_part - back_half * sin_part,
            back_half * cos_part + front_half * sin_part,
        ],
        axis=-1,
    )


def project(tokens, norm_gain, w_query, key_value_weight, query_gain, key_gain, positions):
    token_count = tokens.shape[0]
    head_width = query_gain.shape[0]
    as_float = tokens.astype(jnp.float32)
    normed = rms_scale(as_float, norm_gain).astype(jnp.bfloat16)
    query_raw = jnp.dot(normed, w_query, preferred_element_type=jnp.float32)
    keyval_raw = jnp.dot(normed, key_value_weight, preferred_element_type=jnp.float32)
    cosine, sine_table = rope_table(positions, head_width)
    query_rows = rotate_pairs(
        rms_scale(query_raw.reshape(token_count, -1, head_width), query_gain), cosine, sine_table
    ) * query_scalar ** (-0.5)
    split_kv = keyval_raw.reshape(token_count, -1, 2, head_width)
    keys = rotate_pairs(rms_scale(split_kv[:, :, 0], key_gain), cosine, sine_table)
    key_value_rows = (
        jnp.stack([keys, split_kv[:, :, 1]], axis=2).reshape(token_count, -1).astype(jnp.bfloat16)
    )
    return (query_rows.reshape(token_count, -1).astype(jnp.bfloat16), key_value_rows)


def prompt_starts(segment_ids, lengths):
    starts = jnp.cumsum(lengths) - lengths
    prompt_ids = jnp.arange(lengths.shape[0], dtype=jnp.int32)
    chosen = jnp.where(segment_ids[:, None] == prompt_ids[None, :], starts[None, :], jnp.int32(0))
    return jnp.sum(chosen, axis=1)


def sources(cache_index, lengths, req_counts, req_slots):
    starts = jnp.cumsum(lengths) - lengths
    prompt_ids = jnp.arange(lengths.shape[0], dtype=jnp.int32)
    request_ids = jnp.arange(req_slots.shape[0], dtype=jnp.int32)
    request_ends = jnp.cumsum(req_counts)
    owner_prompt = jnp.sum(
        (request_ends[None, :] <= request_ids[:, None]).astype(jnp.int32), axis=1
    )
    matches = owner_prompt[:, None] == prompt_ids[None, :]
    request_length = jnp.sum(jnp.where(matches, lengths[None, :], jnp.int32(0)), axis=1)
    request_start = jnp.sum(jnp.where(matches, starts[None, :], jnp.int32(0)), axis=1)
    inside = (cache_index[:, None] >= req_slots[None, :]) & (
        cache_index[:, None] < req_slots[None, :] + request_length[None, :]
    )
    offsets = request_start[None, :] + cache_index[:, None] - req_slots[None, :]
    source_row = jnp.sum(jnp.where(inside, offsets, jnp.int32(0)), axis=1)
    source_live = jnp.max(inside.astype(jnp.int32), axis=1) > 0
    return (source_row, source_live)


def flash_attention(query_rows, key_block, segment_start, meta, head_width, n_steps, state):
    row_count, q_width = query_rows.shape
    key_count, kv_width = key_block.shape
    n_heads = q_width // head_width
    group = n_heads // (kv_width // (2 * head_width))
    span = row_count
    seg = segment_start.reshape(row_count, 1).astype(jnp.int32)

    def kv_map(step, meta_ref):
        return (jnp.maximum(meta_ref[4] - step, meta_ref[1]) - meta_ref[3], 0)

    def kernel(meta_ref, q_ref, kv_ref, seg_ref, m_in, l_in, acc_in, o_ref, m_ref, l_ref, acc_ref):
        step = pl.program_id(0)
        block = meta_ref[4] - step

        @pl.when(step == 0)
        def _():
            m_ref[...] = m_in[...]
            l_ref[...] = l_in[...]
            acc_ref[...] = acc_in[...]

        def accumulate(masked):
            if masked:
                key_index = block * span + lax.broadcasted_iota(jnp.int32, (1, span), 1)
                query_index = meta_ref[0] * span + lax.broadcasted_iota(
                    jnp.int32, (row_count, 1), 0
                )
                allowed = (key_index >= seg_ref[...]) & (key_index <= query_index)
            for h in range(n_heads):
                g = h // group
                q = q_ref[:, h * head_width:(h + 1) * head_width]
                k = kv_ref[:, 2 * g * head_width:(2 * g + 1) * head_width]
                v = kv_ref[:, (2 * g + 1) * head_width:(2 * g + 2) * head_width]
                s = lax.dot_general(
                    q, k, (((1,), (1,)), ((), ())), preferred_element_type=jnp.float32
                )
                m_prev = m_ref[h]
                if masked:
                    s_top = jnp.max(jnp.where(allowed, s, -1e30), axis=1, keepdims=True)
                else:
                    s_top = jnp.max(s, axis=1, keepdims=True)
                m_new = jnp.maximum(m_prev, s_top)
                factor = jnp.exp(m_prev - m_new)
                p = jnp.exp(s - m_new)
                if masked:
                    p = jnp.where(allowed, p, 0.0)
                both = jnp.dot(
                    p.astype(jnp.bfloat16),
                    jnp.concatenate([v, jnp.ones_like(v)], axis=1),
                    preferred_element_type=jnp.float32,
                )
                l_ref[h] = l_ref[h] * factor + both[:, head_width:head_width + 1]
                acc_ref[h] = acc_ref[h] * factor + both[:, :head_width]
                m_ref[h] = m_new

        active = block >= meta_ref[1]

        @pl.when(active)
        def _():
            accumulate(True)

        @pl.when(step == n_steps - 1)
        def _():
            for h in range(n_heads):
                o_ref[:, h * head_width:(h + 1) * head_width] = (
                    acc_ref[h] / l_ref[h]
                ).astype(o_ref.dtype)

    stat_shape = (n_heads, row_count, 1)
    acc_shape = (n_heads, row_count, head_width)
    if state is None:
        state = (
            jnp.full(stat_shape, -1e30, jnp.float32),
            jnp.zeros(stat_shape, jnp.float32),
            jnp.zeros(acc_shape, jnp.float32),
        )
    fixed = lambda step, meta_ref: (0, 0)
    fixed3 = lambda step, meta_ref: (0, 0, 0)
    grid_spec = pltpu.PrefetchScalarGridSpec(
        num_scalar_prefetch=1,
        grid=(n_steps,),
        in_specs=[
            pl.BlockSpec((row_count, q_width), fixed),
            pl.BlockSpec((span, kv_width), kv_map),
            pl.BlockSpec((row_count, 1), fixed),
            pl.BlockSpec(stat_shape, fixed3),
            pl.BlockSpec(stat_shape, fixed3),
            pl.BlockSpec(acc_shape, fixed3),
        ],
        out_specs=[
            pl.BlockSpec((row_count, q_width), fixed),
            pl.BlockSpec(stat_shape, fixed3),
            pl.BlockSpec(stat_shape, fixed3),
            pl.BlockSpec(acc_shape, fixed3),
        ],
    )
    out, m_out, l_out, acc_out = pl.pallas_call(
        kernel,
        grid_spec=grid_spec,
        out_shape=[
            jax.ShapeDtypeStruct((row_count, q_width), jnp.bfloat16),
            jax.ShapeDtypeStruct(stat_shape, jnp.float32),
            jax.ShapeDtypeStruct(stat_shape, jnp.float32),
            jax.ShapeDtypeStruct(acc_shape, jnp.float32),
        ],
        compiler_params=pltpu.CompilerParams(dimension_semantics=("arbitrary",)),
    )(meta, query_rows, key_block, seg, *state)
    return out, (m_out, l_out, acc_out)


def gather_tp(tokens):
    tp_size = lax.axis_size("tp")
    tp_rank = lax.axis_index("tp")
    rows = tokens.shape[0]
    gathered = jnp.zeros((tp_size * rows,) + tokens.shape[1:], tokens.dtype)
    gathered = lax.dynamic_update_slice_in_dim(gathered, tokens, tp_rank * rows, 0)
    for shift in range(1, tp_size):
        pairs = [(i, (i + shift) % tp_size) for i in range(tp_size)]
        got = lax.ppermute(tokens, "tp", pairs)
        source = (tp_rank - shift) % tp_size
        gathered = lax.dynamic_update_slice_in_dim(gathered, got, source * rows, 0)
    return gathered


def on_device(
    tokens,
    norm_gain,
    w_query,
    key_value_weight,
    query_gain,
    key_gain,
    lengths,
    segment_ids,
    req_counts,
    req_slots,
):
    tp_size = lax.axis_size("tp")
    tp_rank = lax.axis_index("tp")
    chunk_rows = tokens.shape[0]
    row_count = chunk_rows * tp_size
    seq_rank = lax.axis_index("seq")
    first_row = seq_rank * row_count
    query_index = first_row + jnp.arange(row_count, dtype=jnp.int32)
    segment_start = prompt_starts(segment_ids, lengths)
    positions = query_index - segment_start
    own_positions = lax.dynamic_slice_in_dim(positions, tp_rank * chunk_rows, chunk_rows, 0)
    own_q, own_kv = project(
        tokens, norm_gain, w_query, key_value_weight, query_gain, key_gain, own_positions
    )
    query_rows = jnp.zeros((row_count, own_q.shape[1]), own_q.dtype)
    key_value_rows = jnp.zeros((row_count, own_kv.shape[1]), own_kv.dtype)
    query_rows = lax.dynamic_update_slice_in_dim(query_rows, own_q, tp_rank * chunk_rows, 0)
    key_value_rows = lax.dynamic_update_slice_in_dim(
        key_value_rows, own_kv, tp_rank * chunk_rows, 0
    )
    for shift in range(1, tp_size):
        pairs = [(i, (i + shift) % tp_size) for i in range(tp_size)]
        got = lax.ppermute(tokens, "tp", pairs)
        place = ((tp_rank - shift) % tp_size) * chunk_rows
        got_q, got_kv = project(
            got, norm_gain, w_query, key_value_weight, query_gain, key_gain,
            lax.dynamic_slice_in_dim(positions, place, chunk_rows, 0),
        )
        query_rows = lax.dynamic_update_slice_in_dim(query_rows, got_q, place, 0)
        key_value_rows = lax.dynamic_update_slice_in_dim(key_value_rows, got_kv, place, 0)
    head_width = query_gain.shape[0]
    kv_heads = key_value_rows.shape[1] // (2 * head_width)
    query_heads = query_rows.reshape(row_count, kv_heads, 2, head_width)
    cache_rows = CACHE_DEV
    cache_index = seq_rank * cache_rows + jnp.arange(cache_rows, dtype=jnp.int32)
    source_row, source_live = sources(cache_index, lengths, req_counts, req_slots)

    first_block = jnp.min(segment_start) // row_count
    last_start = jnp.max(segment_start)
    diagonal_meta = jnp.stack([seq_rank, seq_rank, last_start, seq_rank, seq_rank])
    diagonal_meta = diagonal_meta.astype(jnp.int32)
    main_meta = jnp.stack([seq_rank, first_block, last_start, 0, seq_rank - 1]).astype(jnp.int32)
    total_keys = row_count * lax.axis_size("seq")
    n_steps = max(1, min(total_keys // row_count - 1, total_keys // (2 * row_count)))
    n_groups = 2 if kv_heads % 2 == 0 else 1
    kv_group = key_value_rows.shape[1] // n_groups
    q_group = query_rows.shape[1] // n_groups
    attended_parts = []
    cache_parts = []
    for grp in range(n_groups):
        kv_local = key_value_rows[:, grp * kv_group:(grp + 1) * kv_group]
        q_local = query_rows[:, grp * q_group:(grp + 1) * q_group]
        _, state = flash_attention(
            q_local, kv_local, segment_start, diagonal_meta, head_width, 1, None
        )
        key_block = lax.all_gather(kv_local, "seq", axis=0, tiled=True)
        if grp > 0:
            key_block, attended_parts, cache_parts = lax.optimization_barrier(
                (key_block, attended_parts, cache_parts)
            )
        part, _ = flash_attention(
            q_local, key_block, segment_start, main_meta, head_width, n_steps, state
        )
        attended_parts.append(part)
        cache_parts.append(jnp.take(key_block, source_row, axis=0))
    attended = jnp.concatenate(attended_parts, axis=1)
    picked = jnp.concatenate(cache_parts, axis=1)
    cache = jnp.where(source_live[:, None], picked, jnp.zeros_like(picked))
    return (attended, cache)


def solution(mesh):
    placed = (
        P(("seq", "tp"), None),
        P(),
        P(None, "tp"),
        P(None, "tp"),
        P(),
        P(),
        P(),
        P("seq"),
        P(),
        P(),
    )
    return jax.shard_map(
        on_device,
        mesh=mesh,
        in_specs=placed,
        out_specs=(P("seq", "tp"), P("seq", "tp")),
        check_vma=False,
    )
```

```python
import math

import jax
import jax.numpy as jnp
from jax import lax
from jax.sharding import PartitionSpec as P
from jax.experimental import pallas as pl
from jax.experimental.pallas import tpu as pltpu

CACHE_DEV = 8192


rope_base = 1000000.0
query_scalar = 168.0
epsilon = 1e-06


def rms_scale(values, gains):
    return values * lax.rsqrt(jnp.mean(values * values, axis=-1, keepdims=True) + epsilon) * gains


def rope_table(positions, head_width):
    half_width = head_width // 2
    frequency = jnp.exp(
        jnp.arange(half_width, dtype=jnp.float32) * (-2.0 * math.log(rope_base) / head_width)
    )
    angles = positions.astype(jnp.float32)[:, None] * frequency[None, :]
    return (jnp.cos(angles), jnp.sin(angles))


def rotate_pairs(values, cosine, sine_table):
    half_width = values.shape[-1] // 2
    front_half = values[..., :half_width]
    back_half = values[..., half_width:]
    cos_part = cosine[:, None, :]
    sin_part = sine_table[:, None, :]
    return jnp.concatenate(
        [
            front_half * cos_part - back_half * sin_part,
            back_half * cos_part + front_half * sin_part,
        ],
        axis=-1,
    )


def project(tokens, norm_gain, w_query, key_value_weight, query_gain, key_gain, positions):
    token_count = tokens.shape[0]
    head_width = query_gain.shape[0]
    as_float = tokens.astype(jnp.float32)
    normed = rms_scale(as_float, norm_gain).astype(jnp.bfloat16)
    query_raw = jnp.dot(normed, w_query, preferred_element_type=jnp.float32)
    keyval_raw = jnp.dot(normed, key_value_weight, preferred_element_type=jnp.float32)
    cosine, sine_table = rope_table(positions, head_width)
    query_rows = rotate_pairs(
        rms_scale(query_raw.reshape(token_count, -1, head_width), query_gain), cosine, sine_table
    ) * query_scalar ** (-0.5)
    split_kv = keyval_raw.reshape(token_count, -1, 2, head_width)
    keys = rotate_pairs(rms_scale(split_kv[:, :, 0], key_gain), cosine, sine_table)
    key_value_rows = (
        jnp.stack([keys, split_kv[:, :, 1]], axis=2).reshape(token_count, -1).astype(jnp.bfloat16)
    )
    return (query_rows.reshape(token_count, -1).astype(jnp.bfloat16), key_value_rows)


def prompt_starts(segment_ids, lengths):
    starts = jnp.cumsum(lengths) - lengths
    prompt_ids = jnp.arange(lengths.shape[0], dtype=jnp.int32)
    chosen = jnp.where(segment_ids[:, None] == prompt_ids[None, :], starts[None, :], jnp.int32(0))
    return jnp.sum(chosen, axis=1)


def sources(cache_index, lengths, req_counts, req_slots):
    starts = jnp.cumsum(lengths) - lengths
    prompt_ids = jnp.arange(lengths.shape[0], dtype=jnp.int32)
    request_ids = jnp.arange(req_slots.shape[0], dtype=jnp.int32)
    request_ends = jnp.cumsum(req_counts)
    owner_prompt = jnp.sum(
        (request_ends[None, :] <= request_ids[:, None]).astype(jnp.int32), axis=1
    )
    matches = owner_prompt[:, None] == prompt_ids[None, :]
    request_length = jnp.sum(jnp.where(matches, lengths[None, :], jnp.int32(0)), axis=1)
    request_start = jnp.sum(jnp.where(matches, starts[None, :], jnp.int32(0)), axis=1)
    inside = (cache_index[:, None] >= req_slots[None, :]) & (
        cache_index[:, None] < req_slots[None, :] + request_length[None, :]
    )
    offsets = request_start[None, :] + cache_index[:, None] - req_slots[None, :]
    source_row = jnp.sum(jnp.where(inside, offsets, jnp.int32(0)), axis=1)
    source_live = jnp.max(inside.astype(jnp.int32), axis=1) > 0
    return (source_row, source_live)


def flash_attention(query_rows, key_block, segment_start, meta, head_width, n_steps, state):
    row_count, q_width = query_rows.shape
    _, block_rows, kv_width = key_block.shape
    n_heads = q_width // head_width
    group = n_heads // (kv_width // (2 * head_width))
    span = row_count
    seg = segment_start.reshape(row_count, 1).astype(jnp.int32)

    def kv_map(step, meta_ref):
        return (jnp.maximum(meta_ref[4] - step, meta_ref[1]) - meta_ref[3], 0, 0)

    def kernel(meta_ref, q_ref, kv_ref, seg_ref, m_in, l_in, acc_in, o_ref, m_ref, l_ref, acc_ref):
        step = pl.program_id(0)
        block = meta_ref[4] - step

        @pl.when(step == 0)
        def _():
            m_ref[...] = m_in[...]
            l_ref[...] = l_in[...]
            acc_ref[...] = acc_in[...]

        def accumulate(masked):
            if masked:
                key_index = block * span + lax.broadcasted_iota(jnp.int32, (1, span), 1)
                query_index = meta_ref[0] * span + lax.broadcasted_iota(
                    jnp.int32, (row_count, 1), 0
                )
                allowed = (key_index >= seg_ref[...]) & (key_index <= query_index)
            for h in range(n_heads):
                g = h // group
                q = q_ref[:, h * head_width:(h + 1) * head_width]
                k = kv_ref[:, 2 * g * head_width:(2 * g + 1) * head_width]
                v = kv_ref[:, (2 * g + 1) * head_width:(2 * g + 2) * head_width]
                s = lax.dot_general(
                    q, k, (((1,), (1,)), ((), ())), preferred_element_type=jnp.float32
                )
                m_prev = m_ref[h]
                if masked:
                    s_top = jnp.max(jnp.where(allowed, s, -1e30), axis=1, keepdims=True)
                else:
                    s_top = jnp.max(s, axis=1, keepdims=True)
                m_new = jnp.maximum(m_prev, s_top)
                factor = jnp.exp(m_prev - m_new)
                p = jnp.exp(s - m_new)
                if masked:
                    p = jnp.where(allowed, p, 0.0)
                both = jnp.dot(
                    p.astype(jnp.bfloat16),
                    jnp.concatenate([v, jnp.ones_like(v)], axis=1),
                    preferred_element_type=jnp.float32,
                )
                l_ref[h] = l_ref[h] * factor + both[:, head_width:head_width + 1]
                acc_ref[h] = acc_ref[h] * factor + both[:, :head_width]
                m_ref[h] = m_new

        active = block >= meta_ref[1]

        @pl.when(active)
        def _():
            accumulate(True)

        @pl.when(step == n_steps - 1)
        def _():
            for h in range(n_heads):
                o_ref[:, h * head_width:(h + 1) * head_width] = (
                    acc_ref[h] / l_ref[h]
                ).astype(o_ref.dtype)

    stat_shape = (n_heads, row_count, 1)
    acc_shape = (n_heads, row_count, head_width)
    if state is None:
        state = (
            jnp.full(stat_shape, -1e30, jnp.float32),
            jnp.zeros(stat_shape, jnp.float32),
            jnp.zeros(acc_shape, jnp.float32),
        )
    fixed = lambda step, meta_ref: (0, 0)
    fixed3 = lambda step, meta_ref: (0, 0, 0)
    grid_spec = pltpu.PrefetchScalarGridSpec(
        num_scalar_prefetch=1,
        grid=(n_steps,),
        in_specs=[
            pl.BlockSpec((row_count, q_width), fixed),
            pl.BlockSpec((None, span, kv_width), kv_map),
            pl.BlockSpec((row_count, 1), fixed),
            pl.BlockSpec(stat_shape, fixed3),
            pl.BlockSpec(stat_shape, fixed3),
            pl.BlockSpec(acc_shape, fixed3),
        ],
        out_specs=[
            pl.BlockSpec((row_count, q_width), fixed),
            pl.BlockSpec(stat_shape, fixed3),
            pl.BlockSpec(stat_shape, fixed3),
            pl.BlockSpec(acc_shape, fixed3),
        ],
    )
    out, m_out, l_out, acc_out = pl.pallas_call(
        kernel,
        grid_spec=grid_spec,
        out_shape=[
            jax.ShapeDtypeStruct((row_count, q_width), jnp.bfloat16),
            jax.ShapeDtypeStruct(stat_shape, jnp.float32),
            jax.ShapeDtypeStruct(stat_shape, jnp.float32),
            jax.ShapeDtypeStruct(acc_shape, jnp.float32),
        ],
        compiler_params=pltpu.CompilerParams(dimension_semantics=("arbitrary",)),
    )(meta, query_rows, key_block, seg, *state)
    return out, (m_out, l_out, acc_out)


def gather_tp(tokens):
    tp_size = lax.axis_size("tp")
    tp_rank = lax.axis_index("tp")
    rows = tokens.shape[0]
    gathered = jnp.zeros((tp_size * rows,) + tokens.shape[1:], tokens.dtype)
    gathered = lax.dynamic_update_slice_in_dim(gathered, tokens, tp_rank * rows, 0)
    for shift in range(1, tp_size):
        pairs = [(i, (i + shift) % tp_size) for i in range(tp_size)]
        got = lax.ppermute(tokens, "tp", pairs)
        source = (tp_rank - shift) % tp_size
        gathered = lax.dynamic_update_slice_in_dim(gathered, got, source * rows, 0)
    return gathered


def on_device(
    tokens,
    norm_gain,
    w_query,
    key_value_weight,
    query_gain,
    key_gain,
    lengths,
    segment_ids,
    req_counts,
    req_slots,
):
    tp_size = lax.axis_size("tp")
    tp_rank = lax.axis_index("tp")
    chunk_rows = tokens.shape[0]
    row_count = chunk_rows * tp_size
    seq_rank = lax.axis_index("seq")
    first_row = seq_rank * row_count
    query_index = first_row + jnp.arange(row_count, dtype=jnp.int32)
    segment_start = prompt_starts(segment_ids, lengths)
    positions = query_index - segment_start
    own_positions = lax.dynamic_slice_in_dim(positions, tp_rank * chunk_rows, chunk_rows, 0)
    own_q, own_kv = project(
        tokens, norm_gain, w_query, key_value_weight, query_gain, key_gain, own_positions
    )
    query_rows = jnp.zeros((row_count, own_q.shape[1]), own_q.dtype)
    key_value_rows = jnp.zeros((row_count, own_kv.shape[1]), own_kv.dtype)
    query_rows = lax.dynamic_update_slice_in_dim(query_rows, own_q, tp_rank * chunk_rows, 0)
    key_value_rows = lax.dynamic_update_slice_in_dim(
        key_value_rows, own_kv, tp_rank * chunk_rows, 0
    )
    for shift in range(1, tp_size):
        pairs = [(i, (i + shift) % tp_size) for i in range(tp_size)]
        got = lax.ppermute(tokens, "tp", pairs)
        place = ((tp_rank - shift) % tp_size) * chunk_rows
        got_q, got_kv = project(
            got, norm_gain, w_query, key_value_weight, query_gain, key_gain,
            lax.dynamic_slice_in_dim(positions, place, chunk_rows, 0),
        )
        query_rows = lax.dynamic_update_slice_in_dim(query_rows, got_q, place, 0)
        key_value_rows = lax.dynamic_update_slice_in_dim(key_value_rows, got_kv, place, 0)
    head_width = query_gain.shape[0]
    kv_heads = key_value_rows.shape[1] // (2 * head_width)
    query_heads = query_rows.reshape(row_count, kv_heads, 2, head_width)
    cache_rows = CACHE_DEV
    cache_index = seq_rank * cache_rows + jnp.arange(cache_rows, dtype=jnp.int32)
    source_row, source_live = sources(cache_index, lengths, req_counts, req_slots)

    first_block = jnp.min(segment_start) // row_count
    last_start = jnp.max(segment_start)
    pad_rows = 16
    padded = jnp.concatenate(
        [key_value_rows, jnp.zeros((pad_rows, key_value_rows.shape[1]), key_value_rows.dtype)]
    )
    block_rows = row_count + pad_rows
    diagonal_meta = jnp.stack([seq_rank, seq_rank, last_start, seq_rank, seq_rank])
    diagonal_meta = diagonal_meta.astype(jnp.int32)
    _, state = flash_attention(
        query_rows, padded[None], segment_start, diagonal_meta, head_width, 1, None
    )
    table = lax.all_gather(padded, "seq", axis=0, tiled=True)
    n_blocks = table.shape[0] // block_rows
    key_block = table.reshape(n_blocks, block_rows, table.shape[1])
    n_steps = max(1, min(n_blocks - 1, n_blocks // 2))
    main_meta = jnp.stack([seq_rank, first_block, last_start, 0, seq_rank - 1]).astype(jnp.int32)
    attended, _ = flash_attention(
        query_rows, key_block, segment_start, main_meta, head_width, n_steps, state
    )
    table_row = jnp.where(
        source_live,
        (source_row // row_count) * block_rows + source_row % row_count,
        row_count,
    )
    cache = jnp.take(table, table_row, axis=0, mode="clip")
    return (attended, cache)


def solution(mesh):
    placed = (
        P(("seq", "tp"), None),
        P(),
        P(None, "tp"),
        P(None, "tp"),
        P(),
        P(),
        P(),
        P("seq"),
        P(),
        P(),
    )
    return jax.shard_map(
        on_device,
        mesh=mesh,
        in_specs=placed,
        out_specs=(P("seq", "tp"), P("seq", "tp")),
        check_vma=False,
    )
```

```python
import math

import jax
import jax.numpy as jnp
from jax import lax
from jax.sharding import PartitionSpec as P
from jax.experimental import pallas as pl
from jax.experimental.pallas import tpu as pltpu

CACHE_DEV = 8192


rope_base = 1000000.0
query_scalar = 168.0
epsilon = 1e-06


def rms_scale(values, gains):
    return values * lax.rsqrt(jnp.mean(values * values, axis=-1, keepdims=True) + epsilon) * gains


def rope_table(positions, head_width):
    half_width = head_width // 2
    frequency = jnp.exp(
        jnp.arange(half_width, dtype=jnp.float32) * (-2.0 * math.log(rope_base) / head_width)
    )
    angles = positions.astype(jnp.float32)[:, None] * frequency[None, :]
    return (jnp.cos(angles), jnp.sin(angles))


def rotate_pairs(values, cosine, sine_table):
    half_width = values.shape[-1] // 2
    front_half = values[..., :half_width]
    back_half = values[..., half_width:]
    cos_part = cosine[:, None, :]
    sin_part = sine_table[:, None, :]
    return jnp.concatenate(
        [
            front_half * cos_part - back_half * sin_part,
            back_half * cos_part + front_half * sin_part,
        ],
        axis=-1,
    )


def project(tokens, norm_gain, w_query, key_value_weight, query_gain, key_gain, positions):
    token_count = tokens.shape[0]
    head_width = query_gain.shape[0]
    as_float = tokens.astype(jnp.float32)
    normed = rms_scale(as_float, norm_gain).astype(jnp.bfloat16)
    query_raw = jnp.dot(normed, w_query, preferred_element_type=jnp.float32)
    keyval_raw = jnp.dot(normed, key_value_weight, preferred_element_type=jnp.float32)
    cosine, sine_table = rope_table(positions, head_width)
    query_rows = rotate_pairs(
        rms_scale(query_raw.reshape(token_count, -1, head_width), query_gain), cosine, sine_table
    ) * query_scalar ** (-0.5)
    split_kv = keyval_raw.reshape(token_count, -1, 2, head_width)
    keys = rotate_pairs(rms_scale(split_kv[:, :, 0], key_gain), cosine, sine_table)
    key_value_rows = (
        jnp.stack([keys, split_kv[:, :, 1]], axis=2).reshape(token_count, -1).astype(jnp.bfloat16)
    )
    return (query_rows.reshape(token_count, -1).astype(jnp.bfloat16), key_value_rows)


def prompt_starts(segment_ids, lengths):
    starts = jnp.cumsum(lengths) - lengths
    prompt_ids = jnp.arange(lengths.shape[0], dtype=jnp.int32)
    chosen = jnp.where(segment_ids[:, None] == prompt_ids[None, :], starts[None, :], jnp.int32(0))
    return jnp.sum(chosen, axis=1)


def sources(cache_index, lengths, req_counts, req_slots):
    starts = jnp.cumsum(lengths) - lengths
    prompt_ids = jnp.arange(lengths.shape[0], dtype=jnp.int32)
    request_ids = jnp.arange(req_slots.shape[0], dtype=jnp.int32)
    request_ends = jnp.cumsum(req_counts)
    owner_prompt = jnp.sum(
        (request_ends[None, :] <= request_ids[:, None]).astype(jnp.int32), axis=1
    )
    matches = owner_prompt[:, None] == prompt_ids[None, :]
    request_length = jnp.sum(jnp.where(matches, lengths[None, :], jnp.int32(0)), axis=1)
    request_start = jnp.sum(jnp.where(matches, starts[None, :], jnp.int32(0)), axis=1)
    inside = (cache_index[:, None] >= req_slots[None, :]) & (
        cache_index[:, None] < req_slots[None, :] + request_length[None, :]
    )
    offsets = request_start[None, :] + cache_index[:, None] - req_slots[None, :]
    source_row = jnp.sum(jnp.where(inside, offsets, jnp.int32(0)), axis=1)
    source_live = jnp.max(inside.astype(jnp.int32), axis=1) > 0
    return (source_row, source_live)


def flash_attention(query_rows, key_block, segment_start, meta, head_width, n_steps, state):
    row_count, q_width = query_rows.shape
    _, block_rows, kv_width = key_block.shape
    n_heads = q_width // head_width
    group = n_heads // (kv_width // (2 * head_width))
    span = row_count
    seg = segment_start.reshape(row_count, 1).astype(jnp.int32)

    def kv_map(step, meta_ref):
        return (jnp.maximum(meta_ref[4] - step, meta_ref[1]) - meta_ref[3], 0, 0)

    def kernel(meta_ref, q_ref, kv_ref, seg_ref, m_in, l_in, acc_in, o_ref, m_ref, l_ref, acc_ref):
        step = pl.program_id(0)
        block = meta_ref[4] - step

        @pl.when(step == 0)
        def _():
            m_ref[...] = m_in[...]
            l_ref[...] = l_in[...]
            acc_ref[...] = acc_in[...]

        def accumulate(masked):
            if masked:
                key_index = block * span + lax.broadcasted_iota(jnp.int32, (1, span), 1)
                query_index = meta_ref[0] * span + lax.broadcasted_iota(
                    jnp.int32, (row_count, 1), 0
                )
                allowed = (key_index >= seg_ref[...]) & (key_index <= query_index)
            def one_head(h, carry):
                g = h // group
                q = q_ref[:, pl.ds(pl.multiple_of(h * head_width, head_width), head_width)]
                k = kv_ref[:, pl.ds(pl.multiple_of(2 * g * head_width, head_width), head_width)]
                v = kv_ref[
                    :, pl.ds(pl.multiple_of((2 * g + 1) * head_width, head_width), head_width)
                ]
                s = lax.dot_general(
                    q, k, (((1,), (1,)), ((), ())), preferred_element_type=jnp.float32
                )
                m_prev = m_ref[h]
                if masked:
                    s_top = jnp.max(jnp.where(allowed, s, -1e30), axis=1, keepdims=True)
                else:
                    s_top = jnp.max(s, axis=1, keepdims=True)
                m_new = jnp.maximum(m_prev, s_top)
                factor = jnp.exp(m_prev - m_new)
                p = jnp.exp(s - m_new)
                if masked:
                    p = jnp.where(allowed, p, 0.0)
                both = jnp.dot(
                    p.astype(jnp.bfloat16),
                    jnp.concatenate([v, jnp.ones_like(v)], axis=1),
                    preferred_element_type=jnp.float32,
                )
                l_ref[h] = l_ref[h] * factor + both[:, head_width:head_width + 1]
                acc_ref[h] = acc_ref[h] * factor + both[:, :head_width]
                m_ref[h] = m_new
                return carry

            lax.fori_loop(0, n_heads, one_head, 0)

        active = block >= meta_ref[1]

        @pl.when(active)
        def _():
            accumulate(True)

        @pl.when(step == n_steps - 1)
        def _():
            for h in range(n_heads):
                o_ref[:, h * head_width:(h + 1) * head_width] = (
                    acc_ref[h] / l_ref[h]
                ).astype(o_ref.dtype)

    stat_shape = (n_heads, row_count, 1)
    acc_shape = (n_heads, row_count, head_width)
    if state is None:
        state = (
            jnp.full(stat_shape, -1e30, jnp.float32),
            jnp.zeros(stat_shape, jnp.float32),
            jnp.zeros(acc_shape, jnp.float32),
        )
    fixed = lambda step, meta_ref: (0, 0)
    fixed3 = lambda step, meta_ref: (0, 0, 0)
    grid_spec = pltpu.PrefetchScalarGridSpec(
        num_scalar_prefetch=1,
        grid=(n_steps,),
        in_specs=[
            pl.BlockSpec((row_count, q_width), fixed),
            pl.BlockSpec((None, span, kv_width), kv_map),
            pl.BlockSpec((row_count, 1), fixed),
            pl.BlockSpec(stat_shape, fixed3),
            pl.BlockSpec(stat_shape, fixed3),
            pl.BlockSpec(acc_shape, fixed3),
        ],
        out_specs=[
            pl.BlockSpec((row_count, q_width), fixed),
            pl.BlockSpec(stat_shape, fixed3),
            pl.BlockSpec(stat_shape, fixed3),
            pl.BlockSpec(acc_shape, fixed3),
        ],
    )
    out, m_out, l_out, acc_out = pl.pallas_call(
        kernel,
        grid_spec=grid_spec,
        out_shape=[
            jax.ShapeDtypeStruct((row_count, q_width), jnp.bfloat16),
            jax.ShapeDtypeStruct(stat_shape, jnp.float32),
            jax.ShapeDtypeStruct(stat_shape, jnp.float32),
            jax.ShapeDtypeStruct(acc_shape, jnp.float32),
        ],
        compiler_params=pltpu.CompilerParams(dimension_semantics=("arbitrary",)),
    )(meta, query_rows, key_block, seg, *state)
    return out, (m_out, l_out, acc_out)


def gather_tp(tokens):
    tp_size = lax.axis_size("tp")
    tp_rank = lax.axis_index("tp")
    rows = tokens.shape[0]
    gathered = jnp.zeros((tp_size * rows,) + tokens.shape[1:], tokens.dtype)
    gathered = lax.dynamic_update_slice_in_dim(gathered, tokens, tp_rank * rows, 0)
    for shift in range(1, tp_size):
        pairs = [(i, (i + shift) % tp_size) for i in range(tp_size)]
        got = lax.ppermute(tokens, "tp", pairs)
        source = (tp_rank - shift) % tp_size
        gathered = lax.dynamic_update_slice_in_dim(gathered, got, source * rows, 0)
    return gathered


def on_device(
    tokens,
    norm_gain,
    w_query,
    key_value_weight,
    query_gain,
    key_gain,
    lengths,
    segment_ids,
    req_counts,
    req_slots,
):
    tp_size = lax.axis_size("tp")
    tp_rank = lax.axis_index("tp")
    chunk_rows = tokens.shape[0]
    row_count = chunk_rows * tp_size
    seq_rank = lax.axis_index("seq")
    first_row = seq_rank * row_count
    query_index = first_row + jnp.arange(row_count, dtype=jnp.int32)
    segment_start = prompt_starts(segment_ids, lengths)
    positions = query_index - segment_start
    own_positions = lax.dynamic_slice_in_dim(positions, tp_rank * chunk_rows, chunk_rows, 0)
    own_q, own_kv = project(
        tokens, norm_gain, w_query, key_value_weight, query_gain, key_gain, own_positions
    )
    query_rows = jnp.zeros((row_count, own_q.shape[1]), own_q.dtype)
    key_value_rows = jnp.zeros((row_count, own_kv.shape[1]), own_kv.dtype)
    query_rows = lax.dynamic_update_slice_in_dim(query_rows, own_q, tp_rank * chunk_rows, 0)
    key_value_rows = lax.dynamic_update_slice_in_dim(
        key_value_rows, own_kv, tp_rank * chunk_rows, 0
    )
    for shift in range(1, tp_size):
        pairs = [(i, (i + shift) % tp_size) for i in range(tp_size)]
        got = lax.ppermute(tokens, "tp", pairs)
        place = ((tp_rank - shift) % tp_size) * chunk_rows
        got_q, got_kv = project(
            got, norm_gain, w_query, key_value_weight, query_gain, key_gain,
            lax.dynamic_slice_in_dim(positions, place, chunk_rows, 0),
        )
        query_rows = lax.dynamic_update_slice_in_dim(query_rows, got_q, place, 0)
        key_value_rows = lax.dynamic_update_slice_in_dim(key_value_rows, got_kv, place, 0)
    head_width = query_gain.shape[0]
    kv_heads = key_value_rows.shape[1] // (2 * head_width)
    query_heads = query_rows.reshape(row_count, kv_heads, 2, head_width)
    cache_rows = CACHE_DEV
    cache_index = seq_rank * cache_rows + jnp.arange(cache_rows, dtype=jnp.int32)
    source_row, source_live = sources(cache_index, lengths, req_counts, req_slots)

    first_block = jnp.min(segment_start) // row_count
    last_start = jnp.max(segment_start)
    pad_rows = 16
    padded = jnp.concatenate(
        [key_value_rows, jnp.zeros((pad_rows, key_value_rows.shape[1]), key_value_rows.dtype)]
    )
    block_rows = row_count + pad_rows
    diagonal_meta = jnp.stack([seq_rank, seq_rank, last_start, seq_rank, seq_rank])
    diagonal_meta = diagonal_meta.astype(jnp.int32)
    _, state = flash_attention(
        query_rows, padded[None], segment_start, diagonal_meta, head_width, 1, None
    )
    table = lax.all_gather(padded, "seq", axis=0, tiled=True)
    n_blocks = table.shape[0] // block_rows
    key_block = table.reshape(n_blocks, block_rows, table.shape[1])
    n_steps = max(1, min(n_blocks - 1, n_blocks // 2))
    main_meta = jnp.stack([seq_rank, first_block, last_start, 0, seq_rank - 1]).astype(jnp.int32)
    attended, _ = flash_attention(
        query_rows, key_block, segment_start, main_meta, head_width, n_steps, state
    )
    table_row = jnp.where(
        source_live,
        (source_row // row_count) * block_rows + source_row % row_count,
        row_count,
    )
    cache = jnp.take(table, table_row, axis=0, mode="clip")
    return (attended, cache)


def solution(mesh):
    placed = (
        P(("seq", "tp"), None),
        P(),
        P(None, "tp"),
        P(None, "tp"),
        P(),
        P(),
        P(),
        P("seq"),
        P(),
        P(),
    )
    return jax.shard_map(
        on_device,
        mesh=mesh,
        in_specs=placed,
        out_specs=(P("seq", "tp"), P("seq", "tp")),
        check_vma=False,
    )
```

```python
import math

import jax
import jax.numpy as jnp
from jax import lax
from jax.sharding import PartitionSpec as P
from jax.experimental import pallas as pl
from jax.experimental.pallas import tpu as pltpu

CACHE_DEV = 8192


rope_base = 1000000.0
query_scalar = 168.0
epsilon = 1e-06


def rms_scale(values, gains):
    return values * lax.rsqrt(jnp.mean(values * values, axis=-1, keepdims=True) + epsilon) * gains


def rope_table(positions, head_width):
    half_width = head_width // 2
    frequency = jnp.exp(
        jnp.arange(half_width, dtype=jnp.float32) * (-2.0 * math.log(rope_base) / head_width)
    )
    angles = positions.astype(jnp.float32)[:, None] * frequency[None, :]
    return (jnp.cos(angles), jnp.sin(angles))


def rotate_pairs(values, cosine, sine_table):
    half_width = values.shape[-1] // 2
    front_half = values[..., :half_width]
    back_half = values[..., half_width:]
    cos_part = cosine[:, None, :]
    sin_part = sine_table[:, None, :]
    return jnp.concatenate(
        [
            front_half * cos_part - back_half * sin_part,
            back_half * cos_part + front_half * sin_part,
        ],
        axis=-1,
    )


def project(tokens, norm_gain, w_query, key_value_weight, query_gain, key_gain, positions):
    token_count = tokens.shape[0]
    head_width = query_gain.shape[0]
    as_float = tokens.astype(jnp.float32)
    normed = rms_scale(as_float, norm_gain).astype(jnp.bfloat16)
    query_raw = jnp.dot(normed, w_query, preferred_element_type=jnp.float32)
    keyval_raw = jnp.dot(normed, key_value_weight, preferred_element_type=jnp.float32)
    cosine, sine_table = rope_table(positions, head_width)
    query_rows = rotate_pairs(
        rms_scale(query_raw.reshape(token_count, -1, head_width), query_gain), cosine, sine_table
    ) * query_scalar ** (-0.5)
    split_kv = keyval_raw.reshape(token_count, -1, 2, head_width)
    keys = rotate_pairs(rms_scale(split_kv[:, :, 0], key_gain), cosine, sine_table)
    key_value_rows = (
        jnp.stack([keys, split_kv[:, :, 1]], axis=2).reshape(token_count, -1).astype(jnp.bfloat16)
    )
    return (query_rows.reshape(token_count, -1).astype(jnp.bfloat16), key_value_rows)


def prompt_starts(segment_ids, lengths):
    starts = jnp.cumsum(lengths) - lengths
    prompt_ids = jnp.arange(lengths.shape[0], dtype=jnp.int32)
    chosen = jnp.where(segment_ids[:, None] == prompt_ids[None, :], starts[None, :], jnp.int32(0))
    return jnp.sum(chosen, axis=1)


def sources(cache_index, lengths, req_counts, req_slots):
    starts = jnp.cumsum(lengths) - lengths
    prompt_ids = jnp.arange(lengths.shape[0], dtype=jnp.int32)
    request_ids = jnp.arange(req_slots.shape[0], dtype=jnp.int32)
    request_ends = jnp.cumsum(req_counts)
    owner_prompt = jnp.sum(
        (request_ends[None, :] <= request_ids[:, None]).astype(jnp.int32), axis=1
    )
    matches = owner_prompt[:, None] == prompt_ids[None, :]
    request_length = jnp.sum(jnp.where(matches, lengths[None, :], jnp.int32(0)), axis=1)
    request_start = jnp.sum(jnp.where(matches, starts[None, :], jnp.int32(0)), axis=1)
    inside = (cache_index[:, None] >= req_slots[None, :]) & (
        cache_index[:, None] < req_slots[None, :] + request_length[None, :]
    )
    offsets = request_start[None, :] + cache_index[:, None] - req_slots[None, :]
    source_row = jnp.sum(jnp.where(inside, offsets, jnp.int32(0)), axis=1)
    source_live = jnp.max(inside.astype(jnp.int32), axis=1) > 0
    return (source_row, source_live)


def flash_attention(query_rows, key_block, segment_start, meta, head_width, n_steps, state):
    row_count, q_width = query_rows.shape
    _, block_rows, kv_width = key_block.shape
    n_heads = q_width // head_width
    group = n_heads // (kv_width // (2 * head_width))
    span = row_count
    seg = segment_start.reshape(row_count, 1).astype(jnp.int32)

    def kv_map(step, meta_ref):
        return (jnp.maximum(meta_ref[4] - step, meta_ref[1]) - meta_ref[3], 0, 0)

    def kernel(meta_ref, q_ref, kv_ref, seg_ref, m_in, l_in, acc_in, o_ref, m_ref, l_ref, acc_ref):
        step = pl.program_id(0)
        block = meta_ref[4] - step

        @pl.when(step == 0)
        def _():
            m_ref[...] = m_in[...]
            l_ref[...] = l_in[...]
            acc_ref[...] = acc_in[...]

        def accumulate(masked):
            if masked:
                key_index = block * span + lax.broadcasted_iota(jnp.int32, (1, span), 1)
                query_index = meta_ref[0] * span + lax.broadcasted_iota(
                    jnp.int32, (row_count, 1), 0
                )
                allowed = (key_index >= seg_ref[...]) & (key_index <= query_index)
            for h in range(n_heads):
                g = h // group
                q = q_ref[:, h * head_width:(h + 1) * head_width]
                k = kv_ref[:, 2 * g * head_width:(2 * g + 1) * head_width]
                v = kv_ref[:, (2 * g + 1) * head_width:(2 * g + 2) * head_width]
                s = lax.dot_general(
                    q, k, (((1,), (1,)), ((), ())), preferred_element_type=jnp.float32
                )
                m_prev = m_ref[h]
                if masked:
                    s_top = jnp.max(jnp.where(allowed, s, -1e30), axis=1, keepdims=True)
                else:
                    s_top = jnp.max(s, axis=1, keepdims=True)
                m_new = jnp.maximum(m_prev, s_top)
                factor = jnp.exp(m_prev - m_new)
                p = jnp.exp(s - m_new)
                if masked:
                    p = jnp.where(allowed, p, 0.0)
                both = jnp.dot(
                    p.astype(jnp.bfloat16),
                    jnp.concatenate([v, jnp.ones_like(v)], axis=1),
                    preferred_element_type=jnp.float32,
                )
                l_ref[h] = l_ref[h] * factor + both[:, head_width:head_width + 1]
                acc_ref[h] = acc_ref[h] * factor + both[:, :head_width]
                m_ref[h] = m_new

        active = block >= meta_ref[1]

        @pl.when(active)
        def _():
            accumulate(True)

        @pl.when(step == n_steps - 1)
        def _():
            for h in range(n_heads):
                o_ref[:, h * head_width:(h + 1) * head_width] = (
                    acc_ref[h] / l_ref[h]
                ).astype(o_ref.dtype)

    stat_shape = (n_heads, row_count, 1)
    acc_shape = (n_heads, row_count, head_width)
    if state is None:
        state = (
            jnp.full(stat_shape, -1e30, jnp.float32),
            jnp.zeros(stat_shape, jnp.float32),
            jnp.zeros(acc_shape, jnp.float32),
        )
    fixed = lambda step, meta_ref: (0, 0)
    fixed3 = lambda step, meta_ref: (0, 0, 0)
    grid_spec = pltpu.PrefetchScalarGridSpec(
        num_scalar_prefetch=1,
        grid=(n_steps,),
        in_specs=[
            pl.BlockSpec((row_count, q_width), fixed),
            pl.BlockSpec((None, span, kv_width), kv_map),
            pl.BlockSpec((row_count, 1), fixed),
            pl.BlockSpec(stat_shape, fixed3),
            pl.BlockSpec(stat_shape, fixed3),
            pl.BlockSpec(acc_shape, fixed3),
        ],
        out_specs=[
            pl.BlockSpec((row_count, q_width), fixed),
            pl.BlockSpec(stat_shape, fixed3),
            pl.BlockSpec(stat_shape, fixed3),
            pl.BlockSpec(acc_shape, fixed3),
        ],
    )
    out, m_out, l_out, acc_out = pl.pallas_call(
        kernel,
        grid_spec=grid_spec,
        out_shape=[
            jax.ShapeDtypeStruct((row_count, q_width), jnp.bfloat16),
            jax.ShapeDtypeStruct(stat_shape, jnp.float32),
            jax.ShapeDtypeStruct(stat_shape, jnp.float32),
            jax.ShapeDtypeStruct(acc_shape, jnp.float32),
        ],
        compiler_params=pltpu.CompilerParams(dimension_semantics=("arbitrary",)),
    )(meta, query_rows, key_block, seg, *state)
    return out, (m_out, l_out, acc_out)


def gather_tp(tokens):
    tp_size = lax.axis_size("tp")
    tp_rank = lax.axis_index("tp")
    rows = tokens.shape[0]
    gathered = jnp.zeros((tp_size * rows,) + tokens.shape[1:], tokens.dtype)
    gathered = lax.dynamic_update_slice_in_dim(gathered, tokens, tp_rank * rows, 0)
    for shift in range(1, tp_size):
        pairs = [(i, (i + shift) % tp_size) for i in range(tp_size)]
        got = lax.ppermute(tokens, "tp", pairs)
        source = (tp_rank - shift) % tp_size
        gathered = lax.dynamic_update_slice_in_dim(gathered, got, source * rows, 0)
    return gathered


def on_device(
    tokens,
    norm_gain,
    w_query,
    key_value_weight,
    query_gain,
    key_gain,
    lengths,
    segment_ids,
    req_counts,
    req_slots,
):
    tp_size = lax.axis_size("tp")
    tp_rank = lax.axis_index("tp")
    chunk_rows = tokens.shape[0]
    row_count = chunk_rows * tp_size
    seq_rank = lax.axis_index("seq")
    first_row = seq_rank * row_count
    query_index = first_row + jnp.arange(row_count, dtype=jnp.int32)
    segment_start = prompt_starts(segment_ids, lengths)
    positions = query_index - segment_start
    own_positions = lax.dynamic_slice_in_dim(positions, tp_rank * chunk_rows, chunk_rows, 0)
    own_q, own_kv = project(
        tokens, norm_gain, w_query, key_value_weight, query_gain, key_gain, own_positions
    )
    query_rows = jnp.zeros((row_count, own_q.shape[1]), own_q.dtype)
    key_value_rows = jnp.zeros((row_count, own_kv.shape[1]), own_kv.dtype)
    query_rows = lax.dynamic_update_slice_in_dim(query_rows, own_q, tp_rank * chunk_rows, 0)
    key_value_rows = lax.dynamic_update_slice_in_dim(
        key_value_rows, own_kv, tp_rank * chunk_rows, 0
    )
    halves = 2 if chunk_rows % 16 == 0 else 1
    half_rows = chunk_rows // halves
    for shift in range(1, tp_size):
        pairs = [(i, (i + shift) % tp_size) for i in range(tp_size)]
        for half in range(halves):
            piece = tokens[half * half_rows:(half + 1) * half_rows]
            got = lax.ppermute(piece, "tp", pairs)
            place = ((tp_rank - shift) % tp_size) * chunk_rows + half * half_rows
            got_q, got_kv = project(
                got, norm_gain, w_query, key_value_weight, query_gain, key_gain,
                lax.dynamic_slice_in_dim(positions, place, half_rows, 0),
            )
            query_rows = lax.dynamic_update_slice_in_dim(query_rows, got_q, place, 0)
            key_value_rows = lax.dynamic_update_slice_in_dim(key_value_rows, got_kv, place, 0)
    head_width = query_gain.shape[0]
    kv_heads = key_value_rows.shape[1] // (2 * head_width)
    query_heads = query_rows.reshape(row_count, kv_heads, 2, head_width)
    cache_rows = CACHE_DEV
    cache_index = seq_rank * cache_rows + jnp.arange(cache_rows, dtype=jnp.int32)
    source_row, source_live = sources(cache_index, lengths, req_counts, req_slots)

    first_block = jnp.min(segment_start) // row_count
    last_start = jnp.max(segment_start)
    pad_rows = 16
    padded = jnp.concatenate(
        [key_value_rows, jnp.zeros((pad_rows, key_value_rows.shape[1]), key_value_rows.dtype)]
    )
    block_rows = row_count + pad_rows
    diagonal_meta = jnp.stack([seq_rank, seq_rank, last_start, seq_rank, seq_rank])
    diagonal_meta = diagonal_meta.astype(jnp.int32)
    _, state = flash_attention(
        query_rows, padded[None], segment_start, diagonal_meta, head_width, 1, None
    )
    table = lax.all_gather(padded, "seq", axis=0, tiled=True)
    n_blocks = table.shape[0] // block_rows
    key_block = table.reshape(n_blocks, block_rows, table.shape[1])
    n_steps = max(1, min(n_blocks - 1, n_blocks // 2))
    main_meta = jnp.stack([seq_rank, first_block, last_start, 0, seq_rank - 1]).astype(jnp.int32)
    attended, _ = flash_attention(
        query_rows, key_block, segment_start, main_meta, head_width, n_steps, state
    )
    table_row = jnp.where(
        source_live,
        (source_row // row_count) * block_rows + source_row % row_count,
        row_count,
    )
    cache = jnp.take(table, table_row, axis=0, mode="clip")
    return (attended, cache)


def solution(mesh):
    placed = (
        P(("seq", "tp"), None),
        P(),
        P(None, "tp"),
        P(None, "tp"),
        P(),
        P(),
        P(),
        P("seq"),
        P(),
        P(),
    )
    return jax.shard_map(
        on_device,
        mesh=mesh,
        in_specs=placed,
        out_specs=(P("seq", "tp"), P("seq", "tp")),
        check_vma=False,
    )
```

```python
import math

import jax
import jax.numpy as jnp
from jax import lax
from jax.sharding import PartitionSpec as P
from jax.experimental import pallas as pl
from jax.experimental.pallas import tpu as pltpu

CACHE_DEV = 8192


rope_base = 1000000.0
query_scalar = 168.0
epsilon = 1e-06


def rms_scale(values, gains):
    return values * lax.rsqrt(jnp.mean(values * values, axis=-1, keepdims=True) + epsilon) * gains


def rope_table(positions, head_width):
    half_width = head_width // 2
    frequency = jnp.exp(
        jnp.arange(half_width, dtype=jnp.float32) * (-2.0 * math.log(rope_base) / head_width)
    )
    angles = positions.astype(jnp.float32)[:, None] * frequency[None, :]
    return (jnp.cos(angles), jnp.sin(angles))


def rotate_pairs(values, cosine, sine_table):
    half_width = values.shape[-1] // 2
    front_half = values[..., :half_width]
    back_half = values[..., half_width:]
    cos_part = cosine[:, None, :]
    sin_part = sine_table[:, None, :]
    return jnp.concatenate(
        [
            front_half * cos_part - back_half * sin_part,
            back_half * cos_part + front_half * sin_part,
        ],
        axis=-1,
    )


def project(tokens, norm_gain, w_query, key_value_weight, query_gain, key_gain, positions):
    token_count = tokens.shape[0]
    head_width = query_gain.shape[0]
    as_float = tokens.astype(jnp.float32)
    normed = rms_scale(as_float, norm_gain).astype(jnp.bfloat16)
    query_raw = jnp.dot(normed, w_query, preferred_element_type=jnp.float32)
    keyval_raw = jnp.dot(normed, key_value_weight, preferred_element_type=jnp.float32)
    cosine, sine_table = rope_table(positions, head_width)
    query_rows = rotate_pairs(
        rms_scale(query_raw.reshape(token_count, -1, head_width), query_gain), cosine, sine_table
    ) * query_scalar ** (-0.5)
    split_kv = keyval_raw.reshape(token_count, -1, 2, head_width)
    keys = rotate_pairs(rms_scale(split_kv[:, :, 0], key_gain), cosine, sine_table)
    key_value_rows = (
        jnp.stack([keys, split_kv[:, :, 1]], axis=2).reshape(token_count, -1).astype(jnp.bfloat16)
    )
    return (query_rows.reshape(token_count, -1).astype(jnp.bfloat16), key_value_rows)


def prompt_starts(segment_ids, lengths):
    starts = jnp.cumsum(lengths) - lengths
    prompt_ids = jnp.arange(lengths.shape[0], dtype=jnp.int32)
    chosen = jnp.where(segment_ids[:, None] == prompt_ids[None, :], starts[None, :], jnp.int32(0))
    return jnp.sum(chosen, axis=1)


def sources(cache_index, lengths, req_counts, req_slots):
    starts = jnp.cumsum(lengths) - lengths
    prompt_ids = jnp.arange(lengths.shape[0], dtype=jnp.int32)
    request_ids = jnp.arange(req_slots.shape[0], dtype=jnp.int32)
    request_ends = jnp.cumsum(req_counts)
    owner_prompt = jnp.sum(
        (request_ends[None, :] <= request_ids[:, None]).astype(jnp.int32), axis=1
    )
    matches = owner_prompt[:, None] == prompt_ids[None, :]
    request_length = jnp.sum(jnp.where(matches, lengths[None, :], jnp.int32(0)), axis=1)
    request_start = jnp.sum(jnp.where(matches, starts[None, :], jnp.int32(0)), axis=1)
    inside = (cache_index[:, None] >= req_slots[None, :]) & (
        cache_index[:, None] < req_slots[None, :] + request_length[None, :]
    )
    offsets = request_start[None, :] + cache_index[:, None] - req_slots[None, :]
    source_row = jnp.sum(jnp.where(inside, offsets, jnp.int32(0)), axis=1)
    source_live = jnp.max(inside.astype(jnp.int32), axis=1) > 0
    return (source_row, source_live)


def flash_attention(query_rows, key_block, segment_start, meta, head_width, n_steps, state):
    row_count, q_width = query_rows.shape
    _, block_rows, kv_width = key_block.shape
    n_heads = q_width // head_width
    group = n_heads // (kv_width // (2 * head_width))
    span = row_count
    seg = segment_start.reshape(row_count, 1).astype(jnp.int32)

    def kv_map(step, meta_ref):
        return (jnp.maximum(meta_ref[4] - step, meta_ref[1]) - meta_ref[3], 0, 0)

    def kernel(meta_ref, q_ref, kv_ref, seg_ref, m_in, l_in, acc_in, o_ref, m_ref, l_ref, acc_ref):
        step = pl.program_id(0)
        block = meta_ref[4] - step

        @pl.when(step == 0)
        def _():
            m_ref[...] = m_in[...]
            l_ref[...] = l_in[...]
            acc_ref[...] = acc_in[...]

        def accumulate(masked):
            rows = group * row_count
            if masked:
                key_index = block * span + lax.broadcasted_iota(jnp.int32, (1, span), 1)
                query_index = meta_ref[0] * span + lax.broadcasted_iota(
                    jnp.int32, (rows, 1), 0
                ) % row_count
                seg_rows = jnp.concatenate([seg_ref[...]] * group, axis=0)
                allowed = (key_index >= seg_rows) & (key_index <= query_index)
            for g in range(n_heads // group):
                heads = range(g * group, (g + 1) * group)
                q = jnp.concatenate(
                    [q_ref[:, h * head_width:(h + 1) * head_width] for h in heads], axis=0
                )
                k = kv_ref[:, 2 * g * head_width:(2 * g + 1) * head_width]
                v = kv_ref[:, (2 * g + 1) * head_width:(2 * g + 2) * head_width]
                s = lax.dot_general(
                    q, k, (((1,), (1,)), ((), ())), preferred_element_type=jnp.float32
                )
                m_prev = jnp.concatenate([m_ref[h] for h in heads], axis=0)
                if masked:
                    s_top = jnp.max(jnp.where(allowed, s, -1e30), axis=1, keepdims=True)
                else:
                    s_top = jnp.max(s, axis=1, keepdims=True)
                m_new = jnp.maximum(m_prev, s_top)
                factor = jnp.exp(m_prev - m_new)
                p = jnp.exp(s - m_new)
                if masked:
                    p = jnp.where(allowed, p, 0.0)
                both = jnp.dot(
                    p.astype(jnp.bfloat16),
                    jnp.concatenate([v, jnp.ones_like(v)], axis=1),
                    preferred_element_type=jnp.float32,
                )
                for i, h in enumerate(heads):
                    part = slice(i * row_count, (i + 1) * row_count)
                    l_ref[h] = l_ref[h] * factor[part] + both[part, head_width:head_width + 1]
                    acc_ref[h] = acc_ref[h] * factor[part] + both[part, :head_width]
                    m_ref[h] = m_new[part]

        active = block >= meta_ref[1]

        @pl.when(active)
        def _():
            accumulate(True)

        @pl.when(step == n_steps - 1)
        def _():
            for h in range(n_heads):
                o_ref[:, h * head_width:(h + 1) * head_width] = (
                    acc_ref[h] / l_ref[h]
                ).astype(o_ref.dtype)

    stat_shape = (n_heads, row_count, 1)
    acc_shape = (n_heads, row_count, head_width)
    if state is None:
        state = (
            jnp.full(stat_shape, -1e30, jnp.float32),
            jnp.zeros(stat_shape, jnp.float32),
            jnp.zeros(acc_shape, jnp.float32),
        )
    fixed = lambda step, meta_ref: (0, 0)
    fixed3 = lambda step, meta_ref: (0, 0, 0)
    grid_spec = pltpu.PrefetchScalarGridSpec(
        num_scalar_prefetch=1,
        grid=(n_steps,),
        in_specs=[
            pl.BlockSpec((row_count, q_width), fixed),
            pl.BlockSpec((None, span, kv_width), kv_map),
            pl.BlockSpec((row_count, 1), fixed),
            pl.BlockSpec(stat_shape, fixed3),
            pl.BlockSpec(stat_shape, fixed3),
            pl.BlockSpec(acc_shape, fixed3),
        ],
        out_specs=[
            pl.BlockSpec((row_count, q_width), fixed),
            pl.BlockSpec(stat_shape, fixed3),
            pl.BlockSpec(stat_shape, fixed3),
            pl.BlockSpec(acc_shape, fixed3),
        ],
    )
    out, m_out, l_out, acc_out = pl.pallas_call(
        kernel,
        grid_spec=grid_spec,
        out_shape=[
            jax.ShapeDtypeStruct((row_count, q_width), jnp.bfloat16),
            jax.ShapeDtypeStruct(stat_shape, jnp.float32),
            jax.ShapeDtypeStruct(stat_shape, jnp.float32),
            jax.ShapeDtypeStruct(acc_shape, jnp.float32),
        ],
        compiler_params=pltpu.CompilerParams(dimension_semantics=("arbitrary",)),
    )(meta, query_rows, key_block, seg, *state)
    return out, (m_out, l_out, acc_out)


def gather_tp(tokens):
    tp_size = lax.axis_size("tp")
    tp_rank = lax.axis_index("tp")
    rows = tokens.shape[0]
    gathered = jnp.zeros((tp_size * rows,) + tokens.shape[1:], tokens.dtype)
    gathered = lax.dynamic_update_slice_in_dim(gathered, tokens, tp_rank * rows, 0)
    for shift in range(1, tp_size):
        pairs = [(i, (i + shift) % tp_size) for i in range(tp_size)]
        got = lax.ppermute(tokens, "tp", pairs)
        source = (tp_rank - shift) % tp_size
        gathered = lax.dynamic_update_slice_in_dim(gathered, got, source * rows, 0)
    return gathered


def on_device(
    tokens,
    norm_gain,
    w_query,
    key_value_weight,
    query_gain,
    key_gain,
    lengths,
    segment_ids,
    req_counts,
    req_slots,
):
    tp_size = lax.axis_size("tp")
    tp_rank = lax.axis_index("tp")
    chunk_rows = tokens.shape[0]
    row_count = chunk_rows * tp_size
    seq_rank = lax.axis_index("seq")
    first_row = seq_rank * row_count
    query_index = first_row + jnp.arange(row_count, dtype=jnp.int32)
    segment_start = prompt_starts(segment_ids, lengths)
    positions = query_index - segment_start
    own_positions = lax.dynamic_slice_in_dim(positions, tp_rank * chunk_rows, chunk_rows, 0)
    own_q, own_kv = project(
        tokens, norm_gain, w_query, key_value_weight, query_gain, key_gain, own_positions
    )
    query_rows = jnp.zeros((row_count, own_q.shape[1]), own_q.dtype)
    key_value_rows = jnp.zeros((row_count, own_kv.shape[1]), own_kv.dtype)
    query_rows = lax.dynamic_update_slice_in_dim(query_rows, own_q, tp_rank * chunk_rows, 0)
    key_value_rows = lax.dynamic_update_slice_in_dim(
        key_value_rows, own_kv, tp_rank * chunk_rows, 0
    )
    for shift in range(1, tp_size):
        pairs = [(i, (i + shift) % tp_size) for i in range(tp_size)]
        got = lax.ppermute(tokens, "tp", pairs)
        place = ((tp_rank - shift) % tp_size) * chunk_rows
        got_q, got_kv = project(
            got, norm_gain, w_query, key_value_weight, query_gain, key_gain,
            lax.dynamic_slice_in_dim(positions, place, chunk_rows, 0),
        )
        query_rows = lax.dynamic_update_slice_in_dim(query_rows, got_q, place, 0)
        key_value_rows = lax.dynamic_update_slice_in_dim(key_value_rows, got_kv, place, 0)
    head_width = query_gain.shape[0]
    kv_heads = key_value_rows.shape[1] // (2 * head_width)
    query_heads = query_rows.reshape(row_count, kv_heads, 2, head_width)
    cache_rows = CACHE_DEV
    cache_index = seq_rank * cache_rows + jnp.arange(cache_rows, dtype=jnp.int32)
    source_row, source_live = sources(cache_index, lengths, req_counts, req_slots)

    first_block = jnp.min(segment_start) // row_count
    last_start = jnp.max(segment_start)
    pad_rows = 16
    padded = jnp.concatenate(
        [key_value_rows, jnp.zeros((pad_rows, key_value_rows.shape[1]), key_value_rows.dtype)]
    )
    block_rows = row_count + pad_rows
    diagonal_meta = jnp.stack([seq_rank, seq_rank, last_start, seq_rank, seq_rank])
    diagonal_meta = diagonal_meta.astype(jnp.int32)
    _, state = flash_attention(
        query_rows, padded[None], segment_start, diagonal_meta, head_width, 1, None
    )
    table = lax.all_gather(padded, "seq", axis=0, tiled=True)
    n_blocks = table.shape[0] // block_rows
    key_block = table.reshape(n_blocks, block_rows, table.shape[1])
    n_steps = max(1, min(n_blocks - 1, n_blocks // 2))
    main_meta = jnp.stack([seq_rank, first_block, last_start, 0, seq_rank - 1]).astype(jnp.int32)
    attended, _ = flash_attention(
        query_rows, key_block, segment_start, main_meta, head_width, n_steps, state
    )
    table_row = jnp.where(
        source_live,
        (source_row // row_count) * block_rows + source_row % row_count,
        row_count,
    )
    cache = jnp.take(table, table_row, axis=0, mode="clip")
    return (attended, cache)


def solution(mesh):
    placed = (
        P(("seq", "tp"), None),
        P(),
        P(None, "tp"),
        P(None, "tp"),
        P(),
        P(),
        P(),
        P("seq"),
        P(),
        P(),
    )
    return jax.shard_map(
        on_device,
        mesh=mesh,
        in_specs=placed,
        out_specs=(P("seq", "tp"), P("seq", "tp")),
        check_vma=False,
    )
```

```python
import math

import jax
import jax.numpy as jnp
from jax import lax
from jax.sharding import PartitionSpec as P
from jax.experimental import pallas as pl
from jax.experimental.pallas import tpu as pltpu

CACHE_DEV = 8192


rope_base = 1000000.0
query_scalar = 168.0
epsilon = 1e-06


def rms_scale(values, gains):
    return values * lax.rsqrt(jnp.mean(values * values, axis=-1, keepdims=True) + epsilon) * gains


def rope_table(positions, head_width):
    half_width = head_width // 2
    frequency = jnp.exp(
        jnp.arange(half_width, dtype=jnp.float32) * (-2.0 * math.log(rope_base) / head_width)
    )
    angles = positions.astype(jnp.float32)[:, None] * frequency[None, :]
    return (jnp.cos(angles), jnp.sin(angles))


def rotate_pairs(values, cosine, sine_table):
    half_width = values.shape[-1] // 2
    front_half = values[..., :half_width]
    back_half = values[..., half_width:]
    cos_part = cosine[:, None, :]
    sin_part = sine_table[:, None, :]
    return jnp.concatenate(
        [
            front_half * cos_part - back_half * sin_part,
            back_half * cos_part + front_half * sin_part,
        ],
        axis=-1,
    )


def project(tokens, norm_gain, w_query, key_value_weight, query_gain, key_gain, positions):
    token_count = tokens.shape[0]
    head_width = query_gain.shape[0]
    as_float = tokens.astype(jnp.float32)
    normed = rms_scale(as_float, norm_gain).astype(jnp.bfloat16)
    query_raw = jnp.dot(normed, w_query, preferred_element_type=jnp.float32)
    keyval_raw = jnp.dot(normed, key_value_weight, preferred_element_type=jnp.float32)
    cosine, sine_table = rope_table(positions, head_width)
    query_rows = rotate_pairs(
        rms_scale(query_raw.reshape(token_count, -1, head_width), query_gain), cosine, sine_table
    ) * query_scalar ** (-0.5)
    split_kv = keyval_raw.reshape(token_count, -1, 2, head_width)
    keys = rotate_pairs(rms_scale(split_kv[:, :, 0], key_gain), cosine, sine_table)
    key_value_rows = (
        jnp.stack([keys, split_kv[:, :, 1]], axis=2).reshape(token_count, -1).astype(jnp.bfloat16)
    )
    return (query_rows.reshape(token_count, -1).astype(jnp.bfloat16), key_value_rows)


def prompt_starts(segment_ids, lengths):
    starts = jnp.cumsum(lengths) - lengths
    prompt_ids = jnp.arange(lengths.shape[0], dtype=jnp.int32)
    chosen = jnp.where(segment_ids[:, None] == prompt_ids[None, :], starts[None, :], jnp.int32(0))
    return jnp.sum(chosen, axis=1)


def sources(cache_index, lengths, req_counts, req_slots):
    starts = jnp.cumsum(lengths) - lengths
    prompt_ids = jnp.arange(lengths.shape[0], dtype=jnp.int32)
    request_ids = jnp.arange(req_slots.shape[0], dtype=jnp.int32)
    request_ends = jnp.cumsum(req_counts)
    owner_prompt = jnp.sum(
        (request_ends[None, :] <= request_ids[:, None]).astype(jnp.int32), axis=1
    )
    matches = owner_prompt[:, None] == prompt_ids[None, :]
    request_length = jnp.sum(jnp.where(matches, lengths[None, :], jnp.int32(0)), axis=1)
    request_start = jnp.sum(jnp.where(matches, starts[None, :], jnp.int32(0)), axis=1)
    inside = (cache_index[:, None] >= req_slots[None, :]) & (
        cache_index[:, None] < req_slots[None, :] + request_length[None, :]
    )
    offsets = request_start[None, :] + cache_index[:, None] - req_slots[None, :]
    source_row = jnp.sum(jnp.where(inside, offsets, jnp.int32(0)), axis=1)
    source_live = jnp.max(inside.astype(jnp.int32), axis=1) > 0
    return (source_row, source_live)


def flash_attention(query_rows, key_block, segment_start, meta, head_width, n_steps, state):
    row_count, q_width = query_rows.shape
    _, block_rows, kv_width = key_block.shape
    n_heads = q_width // head_width
    group = n_heads // (kv_width // (2 * head_width))
    span = row_count
    seg = segment_start.reshape(row_count, 1).astype(jnp.int32)

    def kv_map(step, meta_ref):
        return (jnp.maximum(meta_ref[4] - step, meta_ref[1]) - meta_ref[3], 0, 0)

    def kernel(meta_ref, q_ref, kv_ref, seg_ref, m_in, l_in, acc_in, o_ref, m_ref, l_ref, acc_ref):
        step = pl.program_id(0)
        block = meta_ref[4] - step

        @pl.when(step == 0)
        def _():
            m_ref[...] = m_in[...]
            l_ref[...] = l_in[...]
            acc_ref[...] = acc_in[...]

        def accumulate(masked):
            if masked:
                key_index = block * span + lax.broadcasted_iota(jnp.int32, (1, span), 1)
                query_index = meta_ref[0] * span + lax.broadcasted_iota(
                    jnp.int32, (row_count, 1), 0
                )
                allowed = (key_index >= seg_ref[...]) & (key_index <= query_index)
            for h in range(n_heads):
                g = h // group
                q = q_ref[:, h * head_width:(h + 1) * head_width]
                k = kv_ref[:, 2 * g * head_width:(2 * g + 1) * head_width]
                v = kv_ref[:, (2 * g + 1) * head_width:(2 * g + 2) * head_width]
                s = lax.dot_general(
                    q, k, (((1,), (1,)), ((), ())), preferred_element_type=jnp.float32
                )
                m_prev = m_ref[h]
                if masked:
                    s_top = jnp.max(jnp.where(allowed, s, -1e30), axis=1, keepdims=True)
                else:
                    s_top = jnp.max(s, axis=1, keepdims=True)
                m_new = jnp.maximum(m_prev, s_top)
                factor = jnp.exp(m_prev - m_new)
                p = jnp.exp(s - m_new)
                if masked:
                    p = jnp.where(allowed, p, 0.0)
                both = jnp.dot(
                    p.astype(jnp.bfloat16),
                    jnp.concatenate([v, jnp.ones_like(v)], axis=1),
                    preferred_element_type=jnp.float32,
                )
                l_ref[h] = l_ref[h] * factor + both[:, head_width:head_width + 1]
                acc_ref[h] = acc_ref[h] * factor + both[:, :head_width]
                m_ref[h] = m_new

        active = block >= meta_ref[1]

        @pl.when(active)
        def _():
            accumulate(True)

        @pl.when(step == n_steps - 1)
        def _():
            for h in range(n_heads):
                o_ref[:, h * head_width:(h + 1) * head_width] = (
                    acc_ref[h] / l_ref[h]
                ).astype(o_ref.dtype)

    stat_shape = (n_heads, row_count, 1)
    acc_shape = (n_heads, row_count, head_width)
    if state is None:
        state = (
            jnp.full(stat_shape, -1e30, jnp.float32),
            jnp.zeros(stat_shape, jnp.float32),
            jnp.zeros(acc_shape, jnp.float32),
        )
    fixed = lambda step, meta_ref: (0, 0)
    fixed3 = lambda step, meta_ref: (0, 0, 0)
    grid_spec = pltpu.PrefetchScalarGridSpec(
        num_scalar_prefetch=1,
        grid=(n_steps,),
        in_specs=[
            pl.BlockSpec((row_count, q_width), fixed),
            pl.BlockSpec((None, span, kv_width), kv_map),
            pl.BlockSpec((row_count, 1), fixed),
            pl.BlockSpec(stat_shape, fixed3),
            pl.BlockSpec(stat_shape, fixed3),
            pl.BlockSpec(acc_shape, fixed3),
        ],
        out_specs=[
            pl.BlockSpec((row_count, q_width), fixed),
            pl.BlockSpec(stat_shape, fixed3),
            pl.BlockSpec(stat_shape, fixed3),
            pl.BlockSpec(acc_shape, fixed3),
        ],
    )
    out, m_out, l_out, acc_out = pl.pallas_call(
        kernel,
        grid_spec=grid_spec,
        out_shape=[
            jax.ShapeDtypeStruct((row_count, q_width), jnp.bfloat16),
            jax.ShapeDtypeStruct(stat_shape, jnp.float32),
            jax.ShapeDtypeStruct(stat_shape, jnp.float32),
            jax.ShapeDtypeStruct(acc_shape, jnp.float32),
        ],
        compiler_params=pltpu.CompilerParams(dimension_semantics=("arbitrary",)),
    )(meta, query_rows, key_block, seg, *state)
    return out, (m_out, l_out, acc_out)


def gather_tp(tokens):
    tp_size = lax.axis_size("tp")
    tp_rank = lax.axis_index("tp")
    rows = tokens.shape[0]
    gathered = jnp.zeros((tp_size * rows,) + tokens.shape[1:], tokens.dtype)
    gathered = lax.dynamic_update_slice_in_dim(gathered, tokens, tp_rank * rows, 0)
    for shift in range(1, tp_size):
        pairs = [(i, (i + shift) % tp_size) for i in range(tp_size)]
        got = lax.ppermute(tokens, "tp", pairs)
        source = (tp_rank - shift) % tp_size
        gathered = lax.dynamic_update_slice_in_dim(gathered, got, source * rows, 0)
    return gathered


def on_device(
    tokens,
    norm_gain,
    w_query,
    key_value_weight,
    query_gain,
    key_gain,
    lengths,
    segment_ids,
    req_counts,
    req_slots,
):
    tp_size = lax.axis_size("tp")
    tp_rank = lax.axis_index("tp")
    chunk_rows = tokens.shape[0]
    row_count = chunk_rows * tp_size
    seq_rank = lax.axis_index("seq")
    first_row = seq_rank * row_count
    query_index = first_row + jnp.arange(row_count, dtype=jnp.int32)
    segment_start = prompt_starts(segment_ids, lengths)
    positions = query_index - segment_start
    own_positions = lax.dynamic_slice_in_dim(positions, tp_rank * chunk_rows, chunk_rows, 0)
    own_q, own_kv = project(
        tokens, norm_gain, w_query, key_value_weight, query_gain, key_gain, own_positions
    )
    query_rows = jnp.zeros((row_count, own_q.shape[1]), own_q.dtype)
    key_value_rows = jnp.zeros((row_count, own_kv.shape[1]), own_kv.dtype)
    query_rows = lax.dynamic_update_slice_in_dim(query_rows, own_q, tp_rank * chunk_rows, 0)
    key_value_rows = lax.dynamic_update_slice_in_dim(
        key_value_rows, own_kv, tp_rank * chunk_rows, 0
    )
    for shift in range(1, tp_size):
        pairs = [(i, (i + shift) % tp_size) for i in range(tp_size)]
        got = lax.ppermute(tokens, "tp", pairs)
        place = ((tp_rank - shift) % tp_size) * chunk_rows
        got_q, got_kv = project(
            got, norm_gain, w_query, key_value_weight, query_gain, key_gain,
            lax.dynamic_slice_in_dim(positions, place, chunk_rows, 0),
        )
        query_rows = lax.dynamic_update_slice_in_dim(query_rows, got_q, place, 0)
        key_value_rows = lax.dynamic_update_slice_in_dim(key_value_rows, got_kv, place, 0)
    head_width = query_gain.shape[0]
    kv_heads = key_value_rows.shape[1] // (2 * head_width)
    query_heads = query_rows.reshape(row_count, kv_heads, 2, head_width)
    cache_rows = CACHE_DEV
    cache_index = seq_rank * cache_rows + jnp.arange(cache_rows, dtype=jnp.int32)
    source_row, source_live = sources(cache_index, lengths, req_counts, req_slots)

    first_block = jnp.min(segment_start) // row_count
    last_start = jnp.max(segment_start)
    pad_rows = 8
    padded = jnp.concatenate(
        [key_value_rows, jnp.zeros((pad_rows, key_value_rows.shape[1]), key_value_rows.dtype)]
    )
    block_rows = row_count + pad_rows
    diagonal_meta = jnp.stack([seq_rank, seq_rank, last_start, seq_rank, seq_rank])
    diagonal_meta = diagonal_meta.astype(jnp.int32)
    _, state = flash_attention(
        query_rows, padded[None], segment_start, diagonal_meta, head_width, 1, None
    )
    table = lax.all_gather(padded, "seq", axis=0, tiled=True)
    n_blocks = table.shape[0] // block_rows
    key_block = table.reshape(n_blocks, block_rows, table.shape[1])
    n_steps = max(1, min(n_blocks - 1, n_blocks // 2))
    main_meta = jnp.stack([seq_rank, first_block, last_start, 0, seq_rank - 1]).astype(jnp.int32)
    attended, _ = flash_attention(
        query_rows, key_block, segment_start, main_meta, head_width, n_steps, state
    )
    table_row = jnp.where(
        source_live,
        (source_row // row_count) * block_rows + source_row % row_count,
        row_count,
    )
    cache = jnp.take(table, table_row, axis=0, mode="clip")
    return (attended, cache)


def solution(mesh):
    placed = (
        P(("seq", "tp"), None),
        P(),
        P(None, "tp"),
        P(None, "tp"),
        P(),
        P(),
        P(),
        P("seq"),
        P(),
        P(),
    )
    return jax.shard_map(
        on_device,
        mesh=mesh,
        in_specs=placed,
        out_specs=(P("seq", "tp"), P("seq", "tp")),
        check_vma=False,
    )
```

```python
import math

import jax
import jax.numpy as jnp
from jax import lax
from jax.sharding import PartitionSpec as P
from jax.experimental import pallas as pl
from jax.experimental.pallas import tpu as pltpu

CACHE_DEV = 8192


rope_base = 1000000.0
query_scalar = 168.0
epsilon = 1e-06


def rms_scale(values, gains):
    return values * lax.rsqrt(jnp.mean(values * values, axis=-1, keepdims=True) + epsilon) * gains


def rope_table(positions, head_width):
    half_width = head_width // 2
    frequency = jnp.exp(
        jnp.arange(half_width, dtype=jnp.float32) * (-2.0 * math.log(rope_base) / head_width)
    )
    angles = positions.astype(jnp.float32)[:, None] * frequency[None, :]
    return (jnp.cos(angles), jnp.sin(angles))


def rotate_pairs(values, cosine, sine_table):
    half_width = values.shape[-1] // 2
    front_half = values[..., :half_width]
    back_half = values[..., half_width:]
    cos_part = cosine[:, None, :]
    sin_part = sine_table[:, None, :]
    return jnp.concatenate(
        [
            front_half * cos_part - back_half * sin_part,
            back_half * cos_part + front_half * sin_part,
        ],
        axis=-1,
    )


def project(tokens, norm_gain, w_query, key_value_weight, query_gain, key_gain, positions):
    token_count = tokens.shape[0]
    head_width = query_gain.shape[0]
    as_float = tokens.astype(jnp.float32)
    normed = rms_scale(as_float, norm_gain).astype(jnp.bfloat16)
    query_raw = jnp.dot(normed, w_query, preferred_element_type=jnp.float32)
    keyval_raw = jnp.dot(normed, key_value_weight, preferred_element_type=jnp.float32)
    cosine, sine_table = rope_table(positions, head_width)
    query_rows = rotate_pairs(
        rms_scale(query_raw.reshape(token_count, -1, head_width), query_gain), cosine, sine_table
    ) * query_scalar ** (-0.5)
    split_kv = keyval_raw.reshape(token_count, -1, 2, head_width)
    keys = rotate_pairs(rms_scale(split_kv[:, :, 0], key_gain), cosine, sine_table)
    key_value_rows = (
        jnp.stack([keys, split_kv[:, :, 1]], axis=2).reshape(token_count, -1).astype(jnp.bfloat16)
    )
    return (query_rows.reshape(token_count, -1).astype(jnp.bfloat16), key_value_rows)


def prompt_starts(segment_ids, lengths):
    starts = jnp.cumsum(lengths) - lengths
    prompt_ids = jnp.arange(lengths.shape[0], dtype=jnp.int32)
    chosen = jnp.where(segment_ids[:, None] == prompt_ids[None, :], starts[None, :], jnp.int32(0))
    return jnp.sum(chosen, axis=1)


def sources(cache_index, lengths, req_counts, req_slots):
    starts = jnp.cumsum(lengths) - lengths
    prompt_ids = jnp.arange(lengths.shape[0], dtype=jnp.int32)
    request_ids = jnp.arange(req_slots.shape[0], dtype=jnp.int32)
    request_ends = jnp.cumsum(req_counts)
    owner_prompt = jnp.sum(
        (request_ends[None, :] <= request_ids[:, None]).astype(jnp.int32), axis=1
    )
    matches = owner_prompt[:, None] == prompt_ids[None, :]
    request_length = jnp.sum(jnp.where(matches, lengths[None, :], jnp.int32(0)), axis=1)
    request_start = jnp.sum(jnp.where(matches, starts[None, :], jnp.int32(0)), axis=1)
    inside = (cache_index[:, None] >= req_slots[None, :]) & (
        cache_index[:, None] < req_slots[None, :] + request_length[None, :]
    )
    offsets = request_start[None, :] + cache_index[:, None] - req_slots[None, :]
    source_row = jnp.sum(jnp.where(inside, offsets, jnp.int32(0)), axis=1)
    source_live = jnp.max(inside.astype(jnp.int32), axis=1) > 0
    return (source_row, source_live)


def flash_attention(query_rows, key_block, segment_start, meta, head_width, n_steps, state):
    row_count, q_width = query_rows.shape
    _, block_rows, kv_width = key_block.shape
    n_heads = q_width // head_width
    group = n_heads // (kv_width // (2 * head_width))
    span = row_count
    seg = segment_start.reshape(row_count, 1).astype(jnp.int32)

    def kv_map(step, meta_ref):
        return (jnp.maximum(meta_ref[4] - step, meta_ref[1]) - meta_ref[3], 0, 0)

    def kernel(meta_ref, q_ref, kv_ref, seg_ref, m_in, l_in, acc_in, o_ref, m_ref, l_ref, acc_ref):
        step = pl.program_id(0)
        block = meta_ref[4] - step

        @pl.when(step == 0)
        def _():
            m_ref[...] = m_in[...]
            l_ref[...] = l_in[...]
            acc_ref[...] = acc_in[...]

        def accumulate(masked):
            if masked:
                key_index = block * span + lax.broadcasted_iota(jnp.int32, (1, span), 1)
                query_index = meta_ref[0] * span + lax.broadcasted_iota(
                    jnp.int32, (row_count, 1), 0
                )
                allowed = (key_index >= seg_ref[...]) & (key_index <= query_index)
            for h in range(n_heads):
                g = h // group
                q = q_ref[:, h * head_width:(h + 1) * head_width]
                k = kv_ref[:, 2 * g * head_width:(2 * g + 1) * head_width]
                v = kv_ref[:, (2 * g + 1) * head_width:(2 * g + 2) * head_width]
                s = lax.dot_general(
                    q, k, (((1,), (1,)), ((), ())), preferred_element_type=jnp.float32
                )
                m_prev = m_ref[h]
                if masked:
                    s_top = jnp.max(jnp.where(allowed, s, -1e30), axis=1, keepdims=True)
                else:
                    s_top = jnp.max(s, axis=1, keepdims=True)
                m_new = jnp.maximum(m_prev, s_top)
                factor = jnp.exp(m_prev - m_new)
                p = jnp.exp(s - m_new)
                if masked:
                    p = jnp.where(allowed, p, 0.0)
                both = jnp.dot(
                    p.astype(jnp.bfloat16),
                    jnp.concatenate([v, jnp.ones_like(v)], axis=1),
                    preferred_element_type=jnp.float32,
                )
                l_ref[h] = l_ref[h] * factor + both[:, head_width:head_width + 1]
                acc_ref[h] = acc_ref[h] * factor + both[:, :head_width]
                m_ref[h] = m_new

        active = block >= meta_ref[1]

        @pl.when(active)
        def _():
            accumulate(True)

        @pl.when(step == n_steps - 1)
        def _():
            for h in range(n_heads):
                o_ref[:, h * head_width:(h + 1) * head_width] = (
                    acc_ref[h] / l_ref[h]
                ).astype(o_ref.dtype)

    stat_shape = (n_heads, row_count, 1)
    acc_shape = (n_heads, row_count, head_width)
    if state is None:
        state = (
            jnp.full(stat_shape, -1e30, jnp.float32),
            jnp.zeros(stat_shape, jnp.float32),
            jnp.zeros(acc_shape, jnp.float32),
        )
    fixed = lambda step, meta_ref: (0, 0)
    fixed3 = lambda step, meta_ref: (0, 0, 0)
    grid_spec = pltpu.PrefetchScalarGridSpec(
        num_scalar_prefetch=1,
        grid=(n_steps,),
        in_specs=[
            pl.BlockSpec((row_count, q_width), fixed),
            pl.BlockSpec((None, span, kv_width), kv_map),
            pl.BlockSpec((row_count, 1), fixed),
            pl.BlockSpec(stat_shape, fixed3),
            pl.BlockSpec(stat_shape, fixed3),
            pl.BlockSpec(acc_shape, fixed3),
        ],
        out_specs=[
            pl.BlockSpec((row_count, q_width), fixed),
            pl.BlockSpec(stat_shape, fixed3),
            pl.BlockSpec(stat_shape, fixed3),
            pl.BlockSpec(acc_shape, fixed3),
        ],
    )
    out, m_out, l_out, acc_out = pl.pallas_call(
        kernel,
        grid_spec=grid_spec,
        out_shape=[
            jax.ShapeDtypeStruct((row_count, q_width), jnp.bfloat16),
            jax.ShapeDtypeStruct(stat_shape, jnp.float32),
            jax.ShapeDtypeStruct(stat_shape, jnp.float32),
            jax.ShapeDtypeStruct(acc_shape, jnp.float32),
        ],
        compiler_params=pltpu.CompilerParams(dimension_semantics=("arbitrary",)),
    )(meta, query_rows, key_block, seg, *state)
    return out, (m_out, l_out, acc_out)


def gather_tp(tokens):
    tp_size = lax.axis_size("tp")
    tp_rank = lax.axis_index("tp")
    rows = tokens.shape[0]
    gathered = jnp.zeros((tp_size * rows,) + tokens.shape[1:], tokens.dtype)
    gathered = lax.dynamic_update_slice_in_dim(gathered, tokens, tp_rank * rows, 0)
    for shift in range(1, tp_size):
        pairs = [(i, (i + shift) % tp_size) for i in range(tp_size)]
        got = lax.ppermute(tokens, "tp", pairs)
        source = (tp_rank - shift) % tp_size
        gathered = lax.dynamic_update_slice_in_dim(gathered, got, source * rows, 0)
    return gathered


def on_device(
    tokens,
    norm_gain,
    w_query,
    key_value_weight,
    query_gain,
    key_gain,
    lengths,
    segment_ids,
    req_counts,
    req_slots,
):
    tp_size = lax.axis_size("tp")
    tp_rank = lax.axis_index("tp")
    chunk_rows = tokens.shape[0]
    row_count = chunk_rows * tp_size
    seq_rank = lax.axis_index("seq")
    first_row = seq_rank * row_count
    query_index = first_row + jnp.arange(row_count, dtype=jnp.int32)
    segment_start = prompt_starts(segment_ids, lengths)
    positions = query_index - segment_start
    own_positions = lax.dynamic_slice_in_dim(positions, tp_rank * chunk_rows, chunk_rows, 0)
    own_q, own_kv = project(
        tokens, norm_gain, w_query, key_value_weight, query_gain, key_gain, own_positions
    )
    query_rows = jnp.zeros((row_count, own_q.shape[1]), own_q.dtype)
    pad_rows = 8
    key_value_rows = jnp.zeros((row_count + pad_rows, own_kv.shape[1]), own_kv.dtype)
    query_rows = lax.dynamic_update_slice_in_dim(query_rows, own_q, tp_rank * chunk_rows, 0)
    key_value_rows = lax.dynamic_update_slice_in_dim(
        key_value_rows, own_kv, tp_rank * chunk_rows, 0
    )
    for shift in range(1, tp_size):
        pairs = [(i, (i + shift) % tp_size) for i in range(tp_size)]
        got = lax.ppermute(tokens, "tp", pairs)
        place = ((tp_rank - shift) % tp_size) * chunk_rows
        got_q, got_kv = project(
            got, norm_gain, w_query, key_value_weight, query_gain, key_gain,
            lax.dynamic_slice_in_dim(positions, place, chunk_rows, 0),
        )
        query_rows = lax.dynamic_update_slice_in_dim(query_rows, got_q, place, 0)
        key_value_rows = lax.dynamic_update_slice_in_dim(key_value_rows, got_kv, place, 0)
    head_width = query_gain.shape[0]
    kv_heads = key_value_rows.shape[1] // (2 * head_width)
    query_heads = query_rows.reshape(row_count, kv_heads, 2, head_width)
    cache_rows = CACHE_DEV
    cache_index = seq_rank * cache_rows + jnp.arange(cache_rows, dtype=jnp.int32)
    source_row, source_live = sources(cache_index, lengths, req_counts, req_slots)

    first_block = jnp.min(segment_start) // row_count
    last_start = jnp.max(segment_start)
    padded = key_value_rows
    block_rows = row_count + pad_rows
    diagonal_meta = jnp.stack([seq_rank, seq_rank, last_start, seq_rank, seq_rank])
    diagonal_meta = diagonal_meta.astype(jnp.int32)
    _, state = flash_attention(
        query_rows, padded[None], segment_start, diagonal_meta, head_width, 1, None
    )
    table = lax.all_gather(padded, "seq", axis=0, tiled=True)
    n_blocks = table.shape[0] // block_rows
    key_block = table.reshape(n_blocks, block_rows, table.shape[1])
    n_steps = max(1, min(n_blocks - 1, n_blocks // 2))
    main_meta = jnp.stack([seq_rank, first_block, last_start, 0, seq_rank - 1]).astype(jnp.int32)
    attended, _ = flash_attention(
        query_rows, key_block, segment_start, main_meta, head_width, n_steps, state
    )
    table_row = jnp.where(
        source_live,
        (source_row // row_count) * block_rows + source_row % row_count,
        row_count,
    )
    cache = jnp.take(table, table_row, axis=0, mode="clip")
    return (attended, cache)


def solution(mesh):
    placed = (
        P(("seq", "tp"), None),
        P(),
        P(None, "tp"),
        P(None, "tp"),
        P(),
        P(),
        P(),
        P("seq"),
        P(),
        P(),
    )
    return jax.shard_map(
        on_device,
        mesh=mesh,
        in_specs=placed,
        out_specs=(P("seq", "tp"), P("seq", "tp")),
        check_vma=False,
    )
```

```python
import math

import jax
import jax.numpy as jnp
from jax import lax
from jax.sharding import PartitionSpec as P
from jax.experimental import pallas as pl
from jax.experimental.pallas import tpu as pltpu

CACHE_DEV = 8192


rope_base = 1000000.0
query_scalar = 168.0
epsilon = 1e-06


def rms_scale(values, gains):
    return values * lax.rsqrt(jnp.mean(values * values, axis=-1, keepdims=True) + epsilon) * gains


def rope_table(positions, head_width):
    half_width = head_width // 2
    frequency = jnp.exp(
        jnp.arange(half_width, dtype=jnp.float32) * (-2.0 * math.log(rope_base) / head_width)
    )
    angles = positions.astype(jnp.float32)[:, None] * frequency[None, :]
    return (jnp.cos(angles), jnp.sin(angles))


def rotate_pairs(values, cosine, sine_table):
    half_width = values.shape[-1] // 2
    front_half = values[..., :half_width]
    back_half = values[..., half_width:]
    cos_part = cosine[:, None, :]
    sin_part = sine_table[:, None, :]
    return jnp.concatenate(
        [
            front_half * cos_part - back_half * sin_part,
            back_half * cos_part + front_half * sin_part,
        ],
        axis=-1,
    )


def project(tokens, norm_gain, w_query, key_value_weight, query_gain, key_gain, positions):
    token_count = tokens.shape[0]
    head_width = query_gain.shape[0]
    as_float = tokens.astype(jnp.float32)
    normed = rms_scale(as_float, norm_gain).astype(jnp.bfloat16)
    query_raw = jnp.dot(normed, w_query, preferred_element_type=jnp.float32)
    keyval_raw = jnp.dot(normed, key_value_weight, preferred_element_type=jnp.float32)
    cosine, sine_table = rope_table(positions, head_width)
    query_rows = rotate_pairs(
        rms_scale(query_raw.reshape(token_count, -1, head_width), query_gain), cosine, sine_table
    ) * query_scalar ** (-0.5)
    split_kv = keyval_raw.reshape(token_count, -1, 2, head_width)
    keys = rotate_pairs(rms_scale(split_kv[:, :, 0], key_gain), cosine, sine_table)
    key_value_rows = (
        jnp.stack([keys, split_kv[:, :, 1]], axis=2).reshape(token_count, -1).astype(jnp.bfloat16)
    )
    return (query_rows.reshape(token_count, -1).astype(jnp.bfloat16), key_value_rows)


def prompt_starts(segment_ids, lengths):
    starts = jnp.cumsum(lengths) - lengths
    prompt_ids = jnp.arange(lengths.shape[0], dtype=jnp.int32)
    chosen = jnp.where(segment_ids[:, None] == prompt_ids[None, :], starts[None, :], jnp.int32(0))
    return jnp.sum(chosen, axis=1)


def sources(cache_index, lengths, req_counts, req_slots):
    starts = jnp.cumsum(lengths) - lengths
    prompt_ids = jnp.arange(lengths.shape[0], dtype=jnp.int32)
    request_ids = jnp.arange(req_slots.shape[0], dtype=jnp.int32)
    request_ends = jnp.cumsum(req_counts)
    owner_prompt = jnp.sum(
        (request_ends[None, :] <= request_ids[:, None]).astype(jnp.int32), axis=1
    )
    matches = owner_prompt[:, None] == prompt_ids[None, :]
    request_length = jnp.sum(jnp.where(matches, lengths[None, :], jnp.int32(0)), axis=1)
    request_start = jnp.sum(jnp.where(matches, starts[None, :], jnp.int32(0)), axis=1)
    inside = (cache_index[:, None] >= req_slots[None, :]) & (
        cache_index[:, None] < req_slots[None, :] + request_length[None, :]
    )
    offsets = request_start[None, :] + cache_index[:, None] - req_slots[None, :]
    source_row = jnp.sum(jnp.where(inside, offsets, jnp.int32(0)), axis=1)
    source_live = jnp.max(inside.astype(jnp.int32), axis=1) > 0
    return (source_row, source_live)


def flash_attention(query_rows, key_block, segment_start, meta, head_width, n_steps, state):
    row_count, q_width = query_rows.shape
    _, block_rows, kv_width = key_block.shape
    n_heads = q_width // head_width
    group = n_heads // (kv_width // (2 * head_width))
    span = row_count
    seg = segment_start.reshape(row_count, 1).astype(jnp.int32)

    def kv_map(step, meta_ref):
        return (jnp.maximum(meta_ref[4] - step, meta_ref[1]) - meta_ref[3], 0, 0)

    def kernel(meta_ref, q_ref, kv_ref, seg_ref, m_in, l_in, acc_in, o_ref, m_ref, l_ref, acc_ref):
        step = pl.program_id(0)
        block = meta_ref[4] - step

        @pl.when(step == 0)
        def _():
            m_ref[...] = m_in[...]
            l_ref[...] = l_in[...]
            acc_ref[...] = acc_in[...]

        def accumulate(masked):
            if masked:
                key_index = block * span + lax.broadcasted_iota(jnp.int32, (1, span), 1)
                query_index = meta_ref[0] * span + lax.broadcasted_iota(
                    jnp.int32, (row_count, 1), 0
                )
                allowed = (key_index >= seg_ref[...]) & (key_index <= query_index)
            extended = {}
            for h in range(n_heads):
                g = h // group
                q = q_ref[:, h * head_width:(h + 1) * head_width]
                k = kv_ref[:, 2 * g * head_width:(2 * g + 1) * head_width]
                if g not in extended:
                    v = kv_ref[:, (2 * g + 1) * head_width:(2 * g + 2) * head_width]
                    extended[g] = jnp.concatenate([v, jnp.ones_like(v)], axis=1)
                s = lax.dot_general(
                    q, k, (((1,), (1,)), ((), ())), preferred_element_type=jnp.float32
                )
                m_prev = m_ref[h]
                if masked:
                    s_top = jnp.max(jnp.where(allowed, s, -1e30), axis=1, keepdims=True)
                else:
                    s_top = jnp.max(s, axis=1, keepdims=True)
                m_new = jnp.maximum(m_prev, s_top)
                factor = jnp.exp(m_prev - m_new)
                p = jnp.exp(s - m_new)
                if masked:
                    p = jnp.where(allowed, p, 0.0)
                both = jnp.dot(
                    p.astype(jnp.bfloat16),
                    extended[g],
                    preferred_element_type=jnp.float32,
                )
                l_ref[h] = l_ref[h] * factor + both[:, head_width:head_width + 1]
                acc_ref[h] = acc_ref[h] * factor + both[:, :head_width]
                m_ref[h] = m_new

        active = block >= meta_ref[1]

        @pl.when(active)
        def _():
            accumulate(True)

        @pl.when(step == n_steps - 1)
        def _():
            for h in range(n_heads):
                o_ref[:, h * head_width:(h + 1) * head_width] = (
                    acc_ref[h] / l_ref[h]
                ).astype(o_ref.dtype)

    stat_shape = (n_heads, row_count, 1)
    acc_shape = (n_heads, row_count, head_width)
    if state is None:
        state = (
            jnp.full(stat_shape, -1e30, jnp.float32),
            jnp.zeros(stat_shape, jnp.float32),
            jnp.zeros(acc_shape, jnp.float32),
        )
    fixed = lambda step, meta_ref: (0, 0)
    fixed3 = lambda step, meta_ref: (0, 0, 0)
    grid_spec = pltpu.PrefetchScalarGridSpec(
        num_scalar_prefetch=1,
        grid=(n_steps,),
        in_specs=[
            pl.BlockSpec((row_count, q_width), fixed),
            pl.BlockSpec((None, span, kv_width), kv_map),
            pl.BlockSpec((row_count, 1), fixed),
            pl.BlockSpec(stat_shape, fixed3),
            pl.BlockSpec(stat_shape, fixed3),
            pl.BlockSpec(acc_shape, fixed3),
        ],
        out_specs=[
            pl.BlockSpec((row_count, q_width), fixed),
            pl.BlockSpec(stat_shape, fixed3),
            pl.BlockSpec(stat_shape, fixed3),
            pl.BlockSpec(acc_shape, fixed3),
        ],
    )
    out, m_out, l_out, acc_out = pl.pallas_call(
        kernel,
        grid_spec=grid_spec,
        out_shape=[
            jax.ShapeDtypeStruct((row_count, q_width), jnp.bfloat16),
            jax.ShapeDtypeStruct(stat_shape, jnp.float32),
            jax.ShapeDtypeStruct(stat_shape, jnp.float32),
            jax.ShapeDtypeStruct(acc_shape, jnp.float32),
        ],
        compiler_params=pltpu.CompilerParams(dimension_semantics=("arbitrary",)),
    )(meta, query_rows, key_block, seg, *state)
    return out, (m_out, l_out, acc_out)


def gather_tp(tokens):
    tp_size = lax.axis_size("tp")
    tp_rank = lax.axis_index("tp")
    rows = tokens.shape[0]
    gathered = jnp.zeros((tp_size * rows,) + tokens.shape[1:], tokens.dtype)
    gathered = lax.dynamic_update_slice_in_dim(gathered, tokens, tp_rank * rows, 0)
    for shift in range(1, tp_size):
        pairs = [(i, (i + shift) % tp_size) for i in range(tp_size)]
        got = lax.ppermute(tokens, "tp", pairs)
        source = (tp_rank - shift) % tp_size
        gathered = lax.dynamic_update_slice_in_dim(gathered, got, source * rows, 0)
    return gathered


def on_device(
    tokens,
    norm_gain,
    w_query,
    key_value_weight,
    query_gain,
    key_gain,
    lengths,
    segment_ids,
    req_counts,
    req_slots,
):
    tp_size = lax.axis_size("tp")
    tp_rank = lax.axis_index("tp")
    chunk_rows = tokens.shape[0]
    row_count = chunk_rows * tp_size
    seq_rank = lax.axis_index("seq")
    first_row = seq_rank * row_count
    query_index = first_row + jnp.arange(row_count, dtype=jnp.int32)
    segment_start = prompt_starts(segment_ids, lengths)
    positions = query_index - segment_start
    own_positions = lax.dynamic_slice_in_dim(positions, tp_rank * chunk_rows, chunk_rows, 0)
    own_q, own_kv = project(
        tokens, norm_gain, w_query, key_value_weight, query_gain, key_gain, own_positions
    )
    query_rows = jnp.zeros((row_count, own_q.shape[1]), own_q.dtype)
    pad_rows = 8
    key_value_rows = jnp.zeros((row_count + pad_rows, own_kv.shape[1]), own_kv.dtype)
    query_rows = lax.dynamic_update_slice_in_dim(query_rows, own_q, tp_rank * chunk_rows, 0)
    key_value_rows = lax.dynamic_update_slice_in_dim(
        key_value_rows, own_kv, tp_rank * chunk_rows, 0
    )
    for shift in range(1, tp_size):
        pairs = [(i, (i + shift) % tp_size) for i in range(tp_size)]
        got = lax.ppermute(tokens, "tp", pairs)
        place = ((tp_rank - shift) % tp_size) * chunk_rows
        got_q, got_kv = project(
            got, norm_gain, w_query, key_value_weight, query_gain, key_gain,
            lax.dynamic_slice_in_dim(positions, place, chunk_rows, 0),
        )
        query_rows = lax.dynamic_update_slice_in_dim(query_rows, got_q, place, 0)
        key_value_rows = lax.dynamic_update_slice_in_dim(key_value_rows, got_kv, place, 0)
    head_width = query_gain.shape[0]
    kv_heads = key_value_rows.shape[1] // (2 * head_width)
    query_heads = query_rows.reshape(row_count, kv_heads, 2, head_width)
    cache_rows = CACHE_DEV
    cache_index = seq_rank * cache_rows + jnp.arange(cache_rows, dtype=jnp.int32)
    source_row, source_live = sources(cache_index, lengths, req_counts, req_slots)

    first_block = jnp.min(segment_start) // row_count
    last_start = jnp.max(segment_start)
    padded = key_value_rows
    block_rows = row_count + pad_rows
    diagonal_meta = jnp.stack([seq_rank, seq_rank, last_start, seq_rank, seq_rank])
    diagonal_meta = diagonal_meta.astype(jnp.int32)
    _, state = flash_attention(
        query_rows, padded[None], segment_start, diagonal_meta, head_width, 1, None
    )
    table = lax.all_gather(padded, "seq", axis=0, tiled=True)
    n_blocks = table.shape[0] // block_rows
    key_block = table.reshape(n_blocks, block_rows, table.shape[1])
    n_steps = max(1, min(n_blocks - 1, n_blocks // 2))
    main_meta = jnp.stack([seq_rank, first_block, last_start, 0, seq_rank - 1]).astype(jnp.int32)
    attended, _ = flash_attention(
        query_rows, key_block, segment_start, main_meta, head_width, n_steps, state
    )
    table_row = jnp.where(
        source_live,
        (source_row // row_count) * block_rows + source_row % row_count,
        row_count,
    )
    cache = jnp.take(table, table_row, axis=0, mode="clip")
    return (attended, cache)


def solution(mesh):
    placed = (
        P(("seq", "tp"), None),
        P(),
        P(None, "tp"),
        P(None, "tp"),
        P(),
        P(),
        P(),
        P("seq"),
        P(),
        P(),
    )
    return jax.shard_map(
        on_device,
        mesh=mesh,
        in_specs=placed,
        out_specs=(P("seq", "tp"), P("seq", "tp")),
        check_vma=False,
    )
```
